32 devices in a mesh: gx: 4 (over x, core), gy: 2 (over y), gz: 4 (over z).
Axes of the slice: x: 2, y: 2, z: 4, core: 2. Of those that a mesh axis runs over, the one named last changes fastest.
Arguments:
- latent: bfloat16 [4096, 512], P(('gx', 'gy', 'gz')), may hold values from -6 to 6
- positions: int32 [3, 4096], P(None, ('gx', 'gy', 'gz')), may hold values from 0 to 1279, as said below
- species: int32 [4096], P(('gx', 'gy', 'gz')), may hold values from 0 to 4
- send_list: int32 [32, 192], P(('gx', 'gy', 'gz')), may hold values from 0 to 287, as said below
- neighbour: int32 [32768], P(('gx', 'gy', 'gz')), may hold values from 0 to 319, as said below
- atom_count: int32 [32], P(('gx', 'gy', 'gz')), may hold values from 64 to 128, as said below
- centre_proj: bfloat16 [512, 512], replicated, may hold values from -0.25 to 0.25
- neigh_proj: bfloat16 [512, 512], replicated, may hold values from -0.25 to 0.25
- centre_table: float32 [5, 512], replicated, may hold values from -3 to 3
- neigh_table: float32 [5, 512], replicated, may hold values from -3 to 3
- basis_proj: bfloat16 [8, 512], replicated, may hold values from -2 to 2
- split_proj: bfloat16 [512, 384], replicated, may hold values from -0.25 to 0.25
- update_proj: bfloat16 [512, 512], replicated, may hold values from -0.25 to 0.25
- tensor_proj: bfloat16 [192, 512], replicated, may hold values from -0.4375 to 0.4375
- energy_proj: float32 [512], replicated, may hold values from -0.25 to 0.25
- species_shift: float32 [5], replicated, may hold values from -4 to 4
Outputs:
- energies: float32 [4096], P(('gx', 'gy', 'gz'))
- forces: float32 [3, 4096], P(None, ('gx', 'gy', 'gz'))
- latent_grad: float32 [4096, 512], P(('gx', 'gy', 'gz'))
The draws below stay inside these ranges and needn't reach their ends.
Inputs may be any that keep to these rules, and one draw needn't show every extreme that they name: `positions`: coordinates from the domain's lower corner in units of 1/64 angstrom: row one below 1024, row two below 512, row three below 1280. `send_list`: entries of a segment are distinct live rows of the sending domain's table: x segments name own atoms, y segments own atoms or x ghost rows (below 160), z segments own, x or y ghost rows; the rows nearest its low-x, high-x, low-y, high-y, low-z and high-z faces in that order of segments. `neighbour`: the 8 entries of an atom are distinct live table rows other than the atom itself, among its nearest ones. `atom_count`: the live atoms are a domain's first slots; some domain in every draw has all 128 live.
All inputs are finite; a program needn't handle non-finite values.
Results may differ from the reference program's by a relative error of at most 0.015.
Values may be sent and summed in bfloat16 or wider, within the bound.
No kernel may reach another device: no remote copies, remote signals or barrier semaphores. Data moves between devices by JAX's collectives and lax.ppermute only.
A program may use at most 128 MiB of HBM per device.

```python
import math
import jax
import jax.numpy as jnp
from jax import lax

A_DEV = 128
K = 8
HW = 512
CH = 64
NB = 8
NSPEC = 5
LX_FIX = 1024
LY_FIX = 512
LZ_FIX = 1280
SX = 16
SY = 64
SZ = 16
ATOMS = 4096
N_GX = 4
N_GY = 2
N_GZ = 4


def geometry(key):
    domains = N_GX * N_GY * N_GZ
    keys = jax.random.split(jax.random.fold_in(key, 11), 3)
    counts = jax.random.randint(keys[0], (domains,), A_DEV // 2, A_DEV + 1)
    full_at = jax.random.randint(keys[1], (), 0, domains)
    counts = jnp.where(jnp.arange(domains) == full_at, A_DEV, counts).astype(jnp.int32)
    limits = [LX_FIX, LY_FIX, LZ_FIX]
    limit_arr = jnp.array(limits, jnp.int32)
    coords = jax.random.randint(keys[2], (domains, 3, A_DEV), 0, limit_arr[None, :, None]).astype(jnp.int32)
    index = jnp.arange(A_DEV, dtype=jnp.int32)
    flags = (index[None, :] >= counts[:, None]).astype(jnp.int32) * (1 << 22)
    lengths = [SX, SX, SY, SY, SZ, SZ]
    ids = jnp.arange(domains, dtype=jnp.int32)
    grid_a = ids // (N_GY * N_GZ)
    grid_b = ids // N_GZ % N_GY
    grid_c = ids % N_GZ
    plan = [((-1, 0, 0), 1, 0, -LX_FIX), ((1, 0, 0), 0, 0, LX_FIX), ((0, -1, 0), 3, 1, -LY_FIX), ((0, 1, 0), 2, 1, LY_FIX), ((0, 0, -1), 5, 2, -LZ_FIX), ((0, 0, 1), 4, 2, LZ_FIX)]
    table = coords
    segments = [None] * 6
    for section in range(3):
        rows_now = table.shape[2]
        row_index = jnp.arange(rows_now, dtype=jnp.int32)
        for segment in (2 * section, 2 * section + 1):
            along = table[:, section]
            if segment % 2 == 1:
                along = limits[section] - 1 - along
            score = along * rows_now + row_index[None, :] + flags
            segments[segment] = jnp.argsort(score, axis=1)[:, :lengths[segment]].astype(jnp.int32)
        places = [table]
        for block in (2 * section, 2 * section + 1):
            step, segment, coord_axis, offset = plan[block]
            other = ((grid_a + step[0]) % N_GX * N_GY + (grid_b + step[1]) % N_GY) * N_GZ + (grid_c + step[2]) % N_GZ
            picked = segments[segment][other]
            moved = jnp.take_along_axis(table[other], picked[:, None, :], axis=2)
            places.append(moved.at[:, coord_axis].add(offset))
        table = jnp.concatenate(places, axis=2)
        extra = table.shape[2] - rows_now
        flags = jnp.concatenate([flags, jnp.zeros((domains, extra), jnp.int32)], axis=1)
    send = jnp.concatenate(segments, axis=1)
    total_rows = table.shape[2]
    rows = jnp.arange(total_rows, dtype=jnp.int32)

    def choose(operands):
        table_coords, count = operands
        coarse = jnp.floor_divide(table_coords, 16)
        own = coarse[:, :A_DEV]
        spread = coarse[:, None, :] - own[:, :, None]
        dist = jnp.sum(spread * spread, axis=0)
        barred = (rows[None, :] == index[:, None]) | (rows[None, :] < A_DEV) & (rows[None, :] >= count)
        score = dist * total_rows + rows[None, :] + barred.astype(jnp.int32) * (1 << 29)
        return jnp.argsort(score, axis=1)[:, :K].astype(jnp.int32)
    neigh = lax.map(choose, (table, counts))
    return (counts, coords, send, neigh)


def draw_positions(key, part):
    counts, coords, send, neigh = geometry(key)
    return coords.transpose(1, 0, 2).reshape(3, -1)


def draw_send_list(key, part):
    counts, coords, send, neigh = geometry(key)
    return send


def draw_neighbour(key, part):
    counts, coords, send, neigh = geometry(key)
    return neigh.reshape(-1)


def draw_atom_count(key, part):
    counts, coords, send, neigh = geometry(key)
    return counts


def with_ends(drawn, stream_key, low, largest):
    extent = drawn.shape
    place = [jax.random.randint(jax.random.fold_in(stream_key, axis), (), 0, extent[axis]) for axis in range(len(extent))]
    drawn = drawn.at[tuple(place)].set(low)
    longest = extent.index(max(extent))
    place[longest] = (place[longest] + 1) % extent[longest]
    return drawn.at[tuple(place)].set(largest)


def levels(stream_key, dims, shards, low, top_value):
    gain = 1.0
    for axis_at, shards_of in shards:
        heights = jax.random.uniform(jax.random.fold_in(jax.random.fold_in(stream_key, 6), axis_at), (shards_of,), jnp.float32, low / len(shards), top_value / len(shards))
        gain = gain * jnp.repeat(jnp.exp(heights), dims[axis_at] // shards_of).reshape((-1,) + (1,) * (len(dims) - 1 - axis_at))
    return gain


def gaussian(stream_key, extent, scale, limit, shards=(), held_as=jnp.bfloat16):
    values = jax.random.normal(stream_key, extent, jnp.float32) * scale
    if len(shards) > 0:
        values = levels(stream_key, extent, shards, -0.22, 0.18) * values
    return jnp.clip(values, min=-limit, max=limit).astype(held_as)


def setup_inputs(seed: int = 0) -> dict:
    streams_of = jax.random.split(jax.random.key(seed), 17)
    latent = gaussian(streams_of[0], (ATOMS, HW), 1.0, 6.0, ((0, 32),))
    positions = draw_positions(jax.random.fold_in(streams_of[16], 71), 0)
    species = with_ends(jax.random.randint(streams_of[2], (ATOMS,), 0, NSPEC), jax.random.fold_in(streams_of[2], 1), 0, NSPEC - 1).astype(jnp.int32)
    send_list = draw_send_list(jax.random.fold_in(streams_of[16], 71), 0)
    neighbour = draw_neighbour(jax.random.fold_in(streams_of[16], 71), 0)
    atom_count = draw_atom_count(jax.random.fold_in(streams_of[16], 71), 0)
    centre_proj = gaussian(streams_of[6], (HW, HW), HW ** -0.5, 0.25)
    neigh_proj = gaussian(streams_of[7], (HW, HW), HW ** -0.5, 0.25)
    centre_table = gaussian(streams_of[8], (NSPEC, HW), 0.5, 3.0, (), jnp.float32)
    neigh_table = gaussian(streams_of[9], (NSPEC, HW), 0.5, 3.0, (), jnp.float32)
    basis_proj = gaussian(streams_of[10], (NB, HW), NB ** -0.5, 2.0)
    split_proj = gaussian(streams_of[11], (HW, 6 * CH), HW ** -0.5, 0.25)
    update_proj = gaussian(streams_of[12], (HW, HW), HW ** -0.5, 0.25)
    tensor_proj = gaussian(streams_of[13], (3 * CH, HW), (3 * CH) ** -0.5, 0.4375)
    energy_proj = gaussian(streams_of[14], (HW,), HW ** -0.5, 0.25, (), jnp.float32)
    species_shift = gaussian(streams_of[15], (NSPEC,), 1.0, 4.0, (), jnp.float32)
    return {"latent": latent, "positions": positions, "species": species, "send_list": send_list, "neighbour": neighbour, "atom_count": atom_count, "centre_proj": centre_proj, "neigh_proj": neigh_proj, "centre_table": centre_table, "neigh_table": neigh_table, "basis_proj": basis_proj, "split_proj": split_proj, "update_proj": update_proj, "tensor_proj": tensor_proj, "energy_proj": energy_proj, "species_shift": species_shift}


CUTOFF = 6.0
SOFTEN = 0.25

def by_order(values):
    count = values.shape[1]
    pairs = values.shape[2]
    return jnp.concatenate([values[0:1], jnp.broadcast_to(values[1:2], (3, count, pairs)), jnp.broadcast_to(values[2:3], (5, count, pairs))], axis=0)

def pair_energy(delta, neigh_rows, centre_rows, valid_pair, basis_proj, split_proj, update_proj, tensor_proj, energy_proj):
    atoms = centre_rows.shape[0]
    pairs = delta.shape[1]
    radius = jnp.sqrt(lax.optimization_barrier(jnp.sum(delta * delta, axis=0)) + SOFTEN)
    unit = delta / radius
    ratio = radius / CUTOFF
    envelope = jnp.where(ratio < 1.0, (1.0 - ratio * ratio) ** 2, 0.0) * valid_pair
    orders = jnp.arange(1, NB + 1).astype(jnp.float32)
    basis = jnp.sin(orders[:, None] * (math.pi / CUTOFF) * radius[None, :]) * (envelope / radius)[None, :]
    radial = jnp.einsum('kp,kh->ph', basis, basis_proj.astype(jnp.float32), precision=lax.Precision.HIGHEST)
    hidden = jax.nn.silu(jnp.repeat(centre_rows, K, axis=0) + neigh_rows + radial) * envelope[:, None]
    hidden_low = hidden.astype(jnp.bfloat16)
    mixed = jnp.einsum('ph,hq->qp', hidden_low.astype(jnp.float32), split_proj.astype(jnp.float32), precision=lax.Precision.HIGHEST)
    amplitude = mixed[:3 * CH].reshape(3, CH, pairs)
    weights = mixed[3 * CH:].reshape(3, CH, pairs)
    unit_x = unit[0]
    unit_y = unit[1]
    unit_z = unit[2]
    root3 = math.sqrt(3.0)
    root15 = math.sqrt(15.0)
    root5 = math.sqrt(5.0)
    harmonics = jnp.stack([jnp.ones_like(unit_x), root3 * unit_x, root3 * unit_y, root3 * unit_z, root15 * unit_x * unit_y, root15 * unit_y * unit_z, 0.5 * root5 * (2.0 * unit_z * unit_z - unit_x * unit_x - unit_y * unit_y), root15 * unit_x * unit_z, 0.5 * root15 * (unit_x * unit_x - unit_y * unit_y)], axis=0)
    gathered = by_order(weights) * harmonics[:, None, :]
    environment = gathered.reshape(9, CH, atoms, K).sum(axis=3) / math.sqrt(K)
    expanded = jnp.repeat(environment, K, axis=2)
    products = by_order(amplitude) * harmonics[:, None, :] * expanded
    scalars = jnp.stack([products[0], products[1:4].sum(axis=0), products[4:9].sum(axis=0)], axis=0)
    scalars = scalars.reshape(3 * CH, pairs).astype(jnp.bfloat16)
    update = jax.nn.silu(jnp.dot(hidden_low, update_proj, preferred_element_type=jnp.float32) + jnp.einsum('qp,qh->ph', scalars.astype(jnp.float32), tensor_proj.astype(jnp.float32), precision=lax.Precision.HIGHEST))
    energy = envelope * jnp.dot(hidden + update, energy_proj, precision=lax.Precision.HIGHEST)
    return energy.reshape(atoms, K).sum(axis=1)

def beside(domain, step):
    grid_a = domain // (N_GY * N_GZ)
    grid_b = domain // N_GZ % N_GY
    grid_c = domain % N_GZ
    return ((grid_a + step[0]) % N_GX * N_GY + (grid_b + step[1]) % N_GY) * N_GZ + (grid_c + step[2]) % N_GZ

def reference(latent, positions, species, send_list, neighbour, atom_count, centre_proj, neigh_proj, centre_table, neigh_table, basis_proj, split_proj, update_proj, tensor_proj, energy_proj, species_shift):
    domains = N_GX * N_GY * N_GZ
    width = latent.shape[1]
    proj_c = (jnp.dot(latent, centre_proj, preferred_element_type=jnp.float32) + centre_table[species]).astype(jnp.bfloat16).reshape(domains, A_DEV, width)
    proj_n = (jnp.dot(latent, neigh_proj, preferred_element_type=jnp.float32) + neigh_table[species]).astype(jnp.bfloat16).reshape(domains, A_DEV, width)
    coords = positions.reshape(3, domains, A_DEV).transpose(1, 0, 2)
    kinds = species.reshape(domains, A_DEV)
    lengths = [SX, SX, SY, SY, SZ, SZ]
    starts = [0, SX, 2 * SX, 2 * SX + SY, 2 * SX + 2 * SY, 2 * SX + 2 * SY + SZ]
    plan = [((-1, 0, 0), 1, 0, -LX_FIX), ((1, 0, 0), 0, 0, LX_FIX), ((0, -1, 0), 3, 1, -LY_FIX), ((0, 1, 0), 2, 1, LY_FIX), ((0, 0, -1), 5, 2, -LZ_FIX), ((0, 0, 1), 4, 2, LZ_FIX)]
    ids = jnp.arange(domains, dtype=jnp.int32)
    table = proj_n
    table_coords = coords
    for section in range(3):
        rows_now = table.shape[1]
        flat = table.reshape(-1, width)
        blocks = [table]
        places = [table_coords]
        for block in (2 * section, 2 * section + 1):
            step, segment, coord_axis, offset = plan[block]
            other = beside(ids, step).astype(jnp.int32)
            picked = send_list[other, starts[segment]:starts[segment] + lengths[segment]].astype(jnp.int32)
            blocks.append(flat[other[:, None] * rows_now + picked])
            moved = jnp.take_along_axis(table_coords[other], picked[:, None, :], axis=2)
            places.append(moved.at[:, coord_axis].add(offset))
        table = jnp.concatenate(blocks, axis=1)
        table_coords = jnp.concatenate(places, axis=2)
    total_rows = table.shape[1]

    def one_domain(domain):
        listed = lax.dynamic_slice_in_dim(neighbour, domain * (A_DEV * K), A_DEV * K)
        delta = (table_coords[domain][:, listed] - jnp.repeat(coords[domain], K, axis=1)).astype(jnp.float32) * (1.0 / 64.0)
        live = (jnp.arange(A_DEV) < atom_count[domain]).astype(jnp.float32)
        valid_pair = jnp.repeat(live, K)
        neigh_rows = table[domain][listed].astype(jnp.float32)
        centre_rows = proj_c[domain].astype(jnp.float32)

        def energy_of(delta_in, neigh_in, centre_in):
            return pair_energy(delta_in, neigh_in, centre_in, valid_pair, basis_proj, split_proj, update_proj, tensor_proj, energy_proj)
        sums, pull = jax.vjp(energy_of, delta, neigh_rows, centre_rows)
        grad_delta, grad_neigh, grad_centre = pull(jnp.ones_like(sums))
        pos_table = jax.ops.segment_sum(grad_delta.T, listed, num_segments=total_rows).T
        pos_table = pos_table.at[:, :A_DEV].add(-grad_delta.reshape(3, A_DEV, K).sum(axis=2))
        row_table = jax.ops.segment_sum(grad_neigh, listed, num_segments=total_rows)
        energies = live * (species_shift[kinds[domain]] + sums)
        return (energies, pos_table, grad_centre, row_table)
    energies, pos_table, grad_centre, row_table = lax.map(one_domain, ids)
    for block in (4, 5, 2, 3, 0, 1):
        step, segment, coord_axis, offset = plan[block]
        holder = beside(ids, (-step[0], -step[1], -step[2])).astype(jnp.int32)
        begin = A_DEV + starts[block]
        got_rows = row_table[holder, begin:begin + lengths[block]]
        got_pos = pos_table[holder][:, :, begin:begin + lengths[block]]
        picked = send_list[:, starts[segment]:starts[segment] + lengths[segment]].astype(jnp.int32)
        row_table = jax.vmap(lambda base, target, extra: base.at[target].add(extra))(row_table, picked, got_rows)
        pos_table = jax.vmap(lambda base, target, extra: base.at[:, target].add(extra))(pos_table, picked, got_pos)
    latent_grad = jnp.dot(grad_centre.reshape(-1, width), centre_proj.astype(jnp.float32).T, precision=lax.Precision.HIGHEST)
    latent_grad = latent_grad + jnp.dot(row_table[:, :A_DEV].reshape(-1, width), neigh_proj.astype(jnp.float32).T, precision=lax.Precision.HIGHEST)
    forces = -pos_table[:, :, :A_DEV].transpose(1, 0, 2).reshape(3, -1)
    return (energies.reshape(-1), forces, latent_grad)
```

```python
import math

import jax
import jax.numpy as jnp
from jax import lax
from jax.sharding import PartitionSpec as P

K = 8
CH = 64
NB = 8
NSPEC = 5
LX_FIX = 1024
LY_FIX = 512
LZ_FIX = 1280


CUTOFF = 6.0
SOFTEN = 0.25


def shortened(shard):
    return jax.tree.map(lambda a: a.astype(jnp.bfloat16) if a.dtype == jnp.float32 else a, shard)


def passed_along(block, axis, distance):
    devices = range(lax.axis_size(axis))
    route = [((i - distance) % len(devices), i) for i in devices]
    return lax.ppermute(block, axis, route)


def by_order(values):
    count = values.shape[1]
    pairs = values.shape[2]
    return jnp.concatenate(
        [
            values[0:1],
            jnp.broadcast_to(values[1:2], (3, count, pairs)),
            jnp.broadcast_to(values[2:3], (5, count, pairs)),
        ],
        axis=0,
    )


def pair_energy(
    delta,
    neigh_rows,
    centre_rows,
    valid_pair,
    basis_proj,
    split_proj,
    update_proj,
    tensor_proj,
    energy_proj,
):
    atoms = centre_rows.shape[0]
    pairs = delta.shape[1]
    radius = jnp.sqrt(jnp.sum(delta * delta, axis=0) + SOFTEN)
    unit = delta / radius
    ratio = radius / CUTOFF
    envelope = jnp.where(ratio < 1.0, (1.0 - ratio * ratio) ** 2, 0.0) * valid_pair
    orders = jnp.arange(1, NB + 1).astype(jnp.float32)
    basis = (
        jnp.sin(orders[:, None] * (math.pi / CUTOFF) * radius[None, :])
        * (envelope / radius)[None, :]
    )
    radial = jnp.einsum(
        "kp,kh->ph", basis, basis_proj.astype(jnp.float32), precision=lax.Precision.HIGHEST
    )
    hidden = (
        jax.nn.silu(jnp.tile(centre_rows, (K, 1)) + neigh_rows + radial) * envelope[:, None]
    )
    hidden_low = hidden.astype(jnp.bfloat16)
    mixed = jnp.einsum("ph,hq->qp", hidden_low, split_proj, preferred_element_type=jnp.float32)
    amplitude = mixed[: 3 * CH].reshape(3, CH, pairs)
    weights = mixed[3 * CH :].reshape(3, CH, pairs)
    unit_x = unit[0]
    unit_y = unit[1]
    unit_z = unit[2]
    root3 = math.sqrt(3.0)
    root15 = math.sqrt(15.0)
    root5 = math.sqrt(5.0)
    harmonics = jnp.stack(
        [
            jnp.ones_like(unit_x),
            root3 * unit_x,
            root3 * unit_y,
            root3 * unit_z,
            root15 * unit_x * unit_y,
            root15 * unit_y * unit_z,
            0.5 * root5 * (2.0 * unit_z * unit_z - unit_x * unit_x - unit_y * unit_y),
            root15 * unit_x * unit_z,
            0.5 * root15 * (unit_x * unit_x - unit_y * unit_y),
        ],
        axis=0,
    )
    gathered = by_order(weights) * harmonics[:, None, :]
    environment = gathered.reshape(9, CH, K, atoms).sum(axis=2) / math.sqrt(K)
    expanded = jnp.tile(environment, (1, 1, K))
    products = by_order(amplitude) * harmonics[:, None, :] * expanded
    scalars = jnp.stack([products[0], products[1:4].sum(axis=0), products[4:9].sum(axis=0)], axis=0)
    scalars = scalars.reshape(3 * CH, pairs).astype(jnp.bfloat16)
    update = jax.nn.silu(
        jnp.dot(hidden_low, update_proj, preferred_element_type=jnp.float32)
        + jnp.einsum("qp,qh->ph", scalars, tensor_proj, preferred_element_type=jnp.float32)
    )
    energy = envelope * jnp.dot(hidden + update, energy_proj, precision=lax.Precision.HIGHEST)
    return energy.reshape(K, atoms).sum(axis=0)


def shards(
    latent,
    positions,
    species,
    send_list,
    neighbour,
    atom_count,
    centre_proj,
    neigh_proj,
    centre_table,
    neigh_table,
    basis_proj,
    split_proj,
    update_proj,
    tensor_proj,
    energy_proj,
    species_shift,
):
    atoms = latent.shape[0]
    face_x = atoms // 8
    face_y = atoms // 2
    face_z = atoms // 8
    lengths = [face_x, face_x, face_y, face_y, face_z, face_z]
    starts = [
        0,
        face_x,
        2 * face_x,
        2 * face_x + face_y,
        2 * face_x + 2 * face_y,
        2 * face_x + 2 * face_y + face_z,
    ]
    kinds = jnp.arange(NSPEC, dtype=jnp.int32)

    def lookup(codes, table):
        onehot = (codes[:, None] == kinds[None, :]).astype(jnp.float32)
        return jnp.dot(onehot, table, precision=lax.Precision.HIGHEST)

    def project(rows, codes, weight, table):
        return (
            jnp.dot(rows, weight, preferred_element_type=jnp.float32) + lookup(codes, table)
        ).astype(jnp.bfloat16)

    proj_c = project(latent, species, centre_proj, centre_table)
    proj_n = project(latent, species, neigh_proj, neigh_table)
    send_rows = send_list[0]
    coded = jnp.concatenate([positions, species[None, :]], axis=0)
    source_tab = latent
    coded_tab = coded
    offsets = [(0, -LX_FIX), (0, LX_FIX), (1, -LY_FIX), (1, LY_FIX), (2, -LZ_FIX), (2, LZ_FIX)]

    def outgoing(segment, rows_tab, codes_tab):
        picked = send_rows[starts[segment] : starts[segment] + lengths[segment]]
        return (jnp.take(rows_tab, picked, axis=0), jnp.take(codes_tab, picked, axis=1))

    def extend(rows_tab, codes_tab, arrivals, first):
        rows_list = [rows_tab]
        codes_list = [codes_tab]
        for number in range(2):
            rows, codes = arrivals[number]
            coord_axis, offset = offsets[first + number]
            rows_list.append(rows)
            codes_list.append(codes.at[coord_axis].add(offset))
        return (jnp.concatenate(rows_list, axis=0), jnp.concatenate(codes_list, axis=1))

    arrivals = []
    for segment, direction in ((1, 1), (0, -1)):
        arrivals.append(
            passed_along(shortened(outgoing(segment, source_tab, coded_tab)), "gx", direction)
        )
    source_tab, coded_tab = extend(source_tab, coded_tab, arrivals, 0)
    arrivals = []
    for segment, direction in ((3, 1), (2, -1)):
        arrivals.append(
            passed_along(shortened(outgoing(segment, source_tab, coded_tab)), "gy", direction)
        )
    source_tab, coded_tab = extend(source_tab, coded_tab, arrivals, 2)
    arrivals = []
    for segment, direction in ((5, 1), (4, -1)):
        arrivals.append(
            passed_along(shortened(outgoing(segment, source_tab, coded_tab)), "gz", direction)
        )
    source_tab, coded_tab = extend(source_tab, coded_tab, arrivals, 4)
    table = jnp.concatenate(
        [proj_n, project(source_tab[atoms:], coded_tab[3, atoms:], neigh_proj, neigh_table)], axis=0
    )
    coords_all = coded_tab[:3]
    total_rows = table.shape[0]
    neighbour = neighbour.reshape(atoms, K).T.reshape(-1)
    select = neighbour[:, None] == jnp.arange(total_rows, dtype=jnp.int32)[None, :]
    neigh_rows = jnp.dot(select.astype(jnp.bfloat16), table, preferred_element_type=jnp.float32)
    delta = (jnp.take(coords_all, neighbour, axis=1) - jnp.tile(positions, (1, K))).astype(
        jnp.float32
    ) * (1.0 / 64.0)
    live = (jnp.arange(atoms) < atom_count[0]).astype(jnp.float32)
    valid_pair = jnp.tile(live, K)

    def energy_of(delta_in, neigh_in, centre_in):
        return pair_energy(
            delta_in,
            neigh_in,
            centre_in,
            valid_pair,
            basis_proj,
            split_proj,
            update_proj,
            tensor_proj,
            energy_proj,
        )

    sums, pull = jax.vjp(energy_of, delta, neigh_rows, proj_c.astype(jnp.float32))
    grad_delta, grad_neigh, grad_centre = pull(jnp.ones_like(sums))
    spread_map = select.astype(jnp.float32)
    row_table = jnp.einsum("pt,ph->th", spread_map, grad_neigh, precision=lax.Precision.HIGHEST)
    pos_table = jnp.dot(grad_delta, spread_map, precision=lax.Precision.HIGHEST)
    pos_table = pos_table.at[:, :atoms].add(-grad_delta.reshape(3, K, atoms).sum(axis=1))
    back_neigh = neigh_proj.astype(jnp.float32).T
    back_centre = centre_proj.astype(jnp.float32).T

    def returning(block, state):
        begin = atoms + starts[block]
        rows = state[0][begin : begin + lengths[block]]
        return (rows, state[1][:, begin : begin + lengths[block]])

    def settle(state, segment, arrived):
        picked = send_rows[starts[segment] : starts[segment] + lengths[segment]]
        moved_pos = state[1].at[:, picked].add(arrived[1])
        return (state[0].at[picked].add(arrived[0]), moved_pos)

    state = (row_table, pos_table)
    plan = ((1, 1), (0, -1), (3, 1), (2, -1), (5, 1), (4, -1))
    for block in (4, 5):
        segment, direction = plan[block]
        state = settle(state, segment, passed_along(returning(block, state), "gz", -direction))
    for block in (2, 3):
        segment, direction = plan[block]
        state = settle(state, segment, passed_along(returning(block, state), "gy", -direction))
    for block in (0, 1):
        segment, direction = plan[block]
        state = settle(state, segment, passed_along(returning(block, state), "gx", -direction))
    latent_grad = jnp.dot(grad_centre, back_centre, precision=lax.Precision.HIGHEST)
    latent_grad = latent_grad + jnp.dot(
        state[0][:atoms], back_neigh, precision=lax.Precision.HIGHEST
    )
    forces = -state[1][:, :atoms]
    energies = live * (lookup(species, species_shift[:, None])[:, 0] + sums)
    return (energies, forces, latent_grad)


def solution(mesh):
    in_specs = (
        P(("gx", "gy", "gz"), None),
        P(None, ("gx", "gy", "gz")),
        P(("gx", "gy", "gz")),
        P(("gx", "gy", "gz"), None),
        P(("gx", "gy", "gz")),
        P(("gx", "gy", "gz")),
        P(),
        P(),
        P(),
        P(),
        P(),
        P(),
        P(),
        P(),
        P(),
        P(),
    )
    out_specs = (P(("gx", "gy", "gz")), P(None, ("gx", "gy", "gz")), P(("gx", "gy", "gz"), None))
    return jax.shard_map(shards, mesh=mesh, in_specs=in_specs, out_specs=out_specs, check_vma=False)
```

```python
import math

import jax
import jax.numpy as jnp
from jax import lax
from jax.sharding import PartitionSpec as P

K = 8
CH = 64
NB = 8
NSPEC = 5
LX_FIX = 1024
LY_FIX = 512
LZ_FIX = 1280


CUTOFF = 6.0
SOFTEN = 0.25


def shortened(shard):
    return jax.tree.map(lambda a: a.astype(jnp.bfloat16) if a.dtype == jnp.float32 else a, shard)


def passed_along(block, axis, distance):
    devices = range(lax.axis_size(axis))
    route = [((i - distance) % len(devices), i) for i in devices]
    return lax.ppermute(block, axis, route)


def by_order(values):
    count = values.shape[1]
    pairs = values.shape[2]
    return jnp.concatenate(
        [
            values[0:1],
            jnp.broadcast_to(values[1:2], (3, count, pairs)),
            jnp.broadcast_to(values[2:3], (5, count, pairs)),
        ],
        axis=0,
    )


def pair_energy(
    delta,
    neigh_rows,
    centre_rows,
    valid_pair,
    basis_proj,
    split_proj,
    update_proj,
    tensor_proj,
    energy_proj,
):
    atoms = centre_rows.shape[0]
    pairs = delta.shape[1]
    radius = jnp.sqrt(jnp.sum(delta * delta, axis=0) + SOFTEN)
    unit = delta / radius
    ratio = radius / CUTOFF
    envelope = jnp.where(ratio < 1.0, (1.0 - ratio * ratio) ** 2, 0.0) * valid_pair
    orders = jnp.arange(1, NB + 1).astype(jnp.float32)
    basis = (
        jnp.sin(orders[:, None] * (math.pi / CUTOFF) * radius[None, :])
        * (envelope / radius)[None, :]
    )
    radial = jnp.einsum(
        "kp,kh->ph", basis, basis_proj.astype(jnp.float32), precision=lax.Precision.HIGHEST
    )
    hidden = (
        jax.nn.silu(jnp.tile(centre_rows, (K, 1)) + neigh_rows + radial) * envelope[:, None]
    )
    hidden_low = hidden.astype(jnp.bfloat16)
    mixed = jnp.einsum("ph,hq->qp", hidden_low, split_proj, preferred_element_type=jnp.float32)
    amplitude = mixed[: 3 * CH].reshape(3, CH, pairs)
    weights = mixed[3 * CH :].reshape(3, CH, pairs)
    unit_x = unit[0]
    unit_y = unit[1]
    unit_z = unit[2]
    root3 = math.sqrt(3.0)
    root15 = math.sqrt(15.0)
    root5 = math.sqrt(5.0)
    harmonics = jnp.stack(
        [
            jnp.ones_like(unit_x),
            root3 * unit_x,
            root3 * unit_y,
            root3 * unit_z,
            root15 * unit_x * unit_y,
            root15 * unit_y * unit_z,
            0.5 * root5 * (2.0 * unit_z * unit_z - unit_x * unit_x - unit_y * unit_y),
            root15 * unit_x * unit_z,
            0.5 * root15 * (unit_x * unit_x - unit_y * unit_y),
        ],
        axis=0,
    )
    gathered = by_order(weights) * harmonics[:, None, :]
    environment = gathered.reshape(9, CH, K, atoms).sum(axis=2) / math.sqrt(K)
    expanded = jnp.tile(environment, (1, 1, K))
    products = by_order(amplitude) * harmonics[:, None, :] * expanded
    scalars = jnp.stack([products[0], products[1:4].sum(axis=0), products[4:9].sum(axis=0)], axis=0)
    scalars = scalars.reshape(3 * CH, pairs).astype(jnp.bfloat16)
    update = jax.nn.silu(
        jnp.dot(hidden_low, update_proj, preferred_element_type=jnp.float32)
        + jnp.einsum("qp,qh->ph", scalars, tensor_proj, preferred_element_type=jnp.float32)
    )
    energy = envelope * jnp.dot(hidden + update, energy_proj, precision=lax.Precision.HIGHEST)
    return energy.reshape(K, atoms).sum(axis=0)


def shards(
    latent,
    positions,
    species,
    send_list,
    neighbour,
    atom_count,
    centre_proj,
    neigh_proj,
    centre_table,
    neigh_table,
    basis_proj,
    split_proj,
    update_proj,
    tensor_proj,
    energy_proj,
    species_shift,
):
    atoms, width = latent.shape
    extra = 128
    face_x = atoms // 8
    face_y = atoms // 2
    face_z = atoms // 8
    lengths = [face_x, face_x, face_y, face_y, face_z, face_z]
    starts = [
        0,
        face_x,
        2 * face_x,
        2 * face_x + face_y,
        2 * face_x + 2 * face_y,
        2 * face_x + 2 * face_y + face_z,
    ]
    kinds = jnp.arange(NSPEC, dtype=jnp.int32)

    def lookup(codes, table):
        onehot = (codes[:, None] == kinds[None, :]).astype(jnp.float32)
        return jnp.dot(onehot, table, precision=lax.Precision.HIGHEST)

    def project(rows, codes, weight, table):
        return (
            jnp.dot(rows, weight, preferred_element_type=jnp.float32) + lookup(codes, table)
        ).astype(jnp.bfloat16)

    def spread(onehot, values):
        high = values.astype(jnp.bfloat16)
        low = (values - high.astype(jnp.float32)).astype(jnp.bfloat16)
        return jnp.einsum(
            "nr,nw->rw", onehot, high, preferred_element_type=jnp.float32
        ) + jnp.einsum("nr,nw->rw", onehot, low, preferred_element_type=jnp.float32)

    proj_c = project(latent, species, centre_proj, centre_table)
    proj_n = project(latent, species, neigh_proj, neigh_table)
    send_rows = send_list[0]
    coarse = positions // 16
    fine = positions - coarse * 16
    coord_cols = jnp.concatenate([coarse, fine], axis=0).T.astype(jnp.bfloat16)
    table = jnp.concatenate(
        [proj_n, coord_cols, jnp.zeros((atoms, extra - 6), jnp.bfloat16)], axis=1
    )
    shifts = [(0, -LX_FIX), (0, LX_FIX), (1, -LY_FIX), (1, LY_FIX), (2, -LZ_FIX), (2, LZ_FIX)]
    sections = (("gx", (1, 0)), ("gy", (3, 2)), ("gz", (5, 4)))
    pickers = {}
    base_rows = []
    for section, (axis, segs) in enumerate(sections):
        rows_now = table.shape[0]
        base_rows.append(rows_now)
        parts = [table]
        for number, (segment, direction) in enumerate(((segs[0], 1), (segs[1], -1))):
            picked = send_rows[starts[segment] : starts[segment] + lengths[segment]]
            onehot = (
                picked[:, None] == jnp.arange(rows_now, dtype=jnp.int32)[None, :]
            ).astype(jnp.bfloat16)
            pickers[segment] = onehot
            out = jnp.dot(onehot, table, preferred_element_type=jnp.float32).astype(jnp.bfloat16)
            got = passed_along(out, axis, direction)
            coord_axis, offset = shifts[2 * section + number]
            shift = jnp.zeros((1, width + extra), jnp.bfloat16).at[0, width + coord_axis].set(
                offset // 16
            )
            parts.append(got + shift)
        table = jnp.concatenate(parts, axis=0)
    total_rows = table.shape[0]
    neighbour = neighbour.reshape(atoms, K).T.reshape(-1)
    select = (neighbour[:, None] == jnp.arange(total_rows, dtype=jnp.int32)[None, :]).astype(
        jnp.bfloat16
    )
    gathered = jnp.dot(select, table, preferred_element_type=jnp.float32)
    neigh_rows = gathered[:, :width]
    coords_n = (gathered[:, width : width + 3] * 16.0 + gathered[:, width + 3 : width + 6]).T
    delta = (coords_n - jnp.tile(positions.astype(jnp.float32), (1, K))) * (1.0 / 64.0)
    live = (jnp.arange(atoms) < atom_count[0]).astype(jnp.float32)
    valid_pair = jnp.tile(live, K)

    def energy_of(delta_in, neigh_in, centre_in):
        return pair_energy(
            delta_in,
            neigh_in,
            centre_in,
            valid_pair,
            basis_proj,
            split_proj,
            update_proj,
            tensor_proj,
            energy_proj,
        )

    atom_energy, pull = jax.vjp(energy_of, delta, neigh_rows, proj_c.astype(jnp.float32))
    grad_delta, grad_neigh, grad_centre = pull(jnp.ones_like(atom_energy))
    pairs = grad_neigh.shape[0]
    grads = jnp.concatenate(
        [grad_neigh, grad_delta.T, jnp.zeros((pairs, extra - 3), jnp.float32)], axis=1
    )
    sums = spread(select, grads)
    own_pos = grad_delta.reshape(3, K, atoms).sum(axis=1)
    sums = sums.at[:atoms, width : width + 3].add(-own_pos.T)
    for section in (2, 1, 0):
        axis, segs = sections[section]
        rows_now = base_rows[section]
        first = atoms + starts[2 * section]
        second = atoms + starts[2 * section + 1]
        back_first = passed_along(sums[first : first + lengths[2 * section]], axis, -1)
        back_second = passed_along(sums[second : second + lengths[2 * section + 1]], axis, 1)
        sums = (
            sums[:rows_now]
            + spread(pickers[segs[0]], back_first)
            + spread(pickers[segs[1]], back_second)
        )
    back_neigh = neigh_proj.astype(jnp.float32).T
    back_centre = centre_proj.astype(jnp.float32).T
    latent_grad = jnp.dot(grad_centre, back_centre, precision=lax.Precision.HIGHEST)
    latent_grad = latent_grad + jnp.dot(
        sums[:, :width], back_neigh, precision=lax.Precision.HIGHEST
    )
    forces = -sums[:, width : width + 3].T
    energies = live * (lookup(species, species_shift[:, None])[:, 0] + atom_energy)
    return (energies, forces, latent_grad)


def solution(mesh):
    in_specs = (
        P(("gx", "gy", "gz"), None),
        P(None, ("gx", "gy", "gz")),
        P(("gx", "gy", "gz")),
        P(("gx", "gy", "gz"), None),
        P(("gx", "gy", "gz")),
        P(("gx", "gy", "gz")),
        P(),
        P(),
        P(),
        P(),
        P(),
        P(),
        P(),
        P(),
        P(),
        P(),
    )
    out_specs = (P(("gx", "gy", "gz")), P(None, ("gx", "gy", "gz")), P(("gx", "gy", "gz"), None))
    return jax.shard_map(shards, mesh=mesh, in_specs=in_specs, out_specs=out_specs, check_vma=False)
```

```python
import math

import jax
import jax.numpy as jnp
from jax import lax
from jax.sharding import PartitionSpec as P

K = 8
CH = 64
NB = 8
NSPEC = 5
LX_FIX = 1024
LY_FIX = 512
LZ_FIX = 1280


CUTOFF = 6.0
SOFTEN = 0.25


def shortened(shard):
    return jax.tree.map(lambda a: a.astype(jnp.bfloat16) if a.dtype == jnp.float32 else a, shard)


def passed_along(block, axis, distance):
    devices = range(lax.axis_size(axis))
    route = [((i - distance) % len(devices), i) for i in devices]
    return lax.ppermute(block, axis, route)


def by_order(values):
    count = values.shape[1]
    pairs = values.shape[2]
    return jnp.concatenate(
        [
            values[0:1],
            jnp.broadcast_to(values[1:2], (3, count, pairs)),
            jnp.broadcast_to(values[2:3], (5, count, pairs)),
        ],
        axis=0,
    )


def pair_energy(
    delta,
    neigh_rows,
    centre_rows,
    valid_pair,
    basis_proj,
    split_proj,
    update_proj,
    tensor_proj,
    energy_proj,
):
    atoms = centre_rows.shape[0]
    width = centre_rows.shape[1]
    radius = jnp.sqrt(jnp.sum(delta * delta, axis=0) + SOFTEN)
    unit = delta / radius
    ratio = radius / CUTOFF
    envelope = jnp.where(ratio < 1.0, (1.0 - ratio * ratio) ** 2, 0.0) * valid_pair
    orders = jnp.arange(1, NB + 1).astype(jnp.float32)
    basis = (
        jnp.sin(orders[:, None, None] * (math.pi / CUTOFF) * radius[None])
        * (envelope / radius)[None]
    )
    radial = jnp.einsum(
        "nka,nh->kah", basis, basis_proj.astype(jnp.float32), precision=lax.Precision.HIGHEST
    )
    hidden = (
        jax.nn.silu(centre_rows[None] + neigh_rows.reshape(K, atoms, width) + radial)
        * envelope[:, :, None]
    )
    hidden_low = hidden.astype(jnp.bfloat16)
    mixed = jnp.einsum("kah,hq->qka", hidden_low, split_proj, preferred_element_type=jnp.float32)
    amplitude = mixed[: 3 * CH].reshape(3, CH, K, atoms)
    weights = mixed[3 * CH :].reshape(3, CH, K, atoms)
    unit_x = unit[0]
    unit_y = unit[1]
    unit_z = unit[2]
    root3 = math.sqrt(3.0)
    root15 = math.sqrt(15.0)
    root5 = math.sqrt(5.0)
    harmonics = [
        [jnp.ones_like(unit_x)],
        [root3 * unit_x, root3 * unit_y, root3 * unit_z],
        [
            root15 * unit_x * unit_y,
            root15 * unit_y * unit_z,
            0.5 * root5 * (2.0 * unit_z * unit_z - unit_x * unit_x - unit_y * unit_y),
            root15 * unit_x * unit_z,
            0.5 * root15 * (unit_x * unit_x - unit_y * unit_y),
        ],
    ]
    scalars = []
    for order in range(3):
        total = 0.0
        for harmonic in harmonics[order]:
            environment = (weights[order] * harmonic[None]).sum(axis=1) / math.sqrt(K)
            total = total + harmonic[None] * environment[:, None, :]
        scalars.append(amplitude[order] * total)
    scalars = jnp.stack(scalars, axis=0).reshape(3 * CH, K * atoms).astype(jnp.bfloat16)
    flat_low = hidden_low.reshape(K * atoms, width)
    update = jax.nn.silu(
        jnp.dot(flat_low, update_proj, preferred_element_type=jnp.float32)
        + jnp.einsum("qp,qh->ph", scalars, tensor_proj, preferred_element_type=jnp.float32)
    )
    energy = envelope * jnp.sum(
        (hidden + update.reshape(K, atoms, width)) * energy_proj, axis=-1
    )
    return energy.sum(axis=0)


def shards(
    latent,
    positions,
    species,
    send_list,
    neighbour,
    atom_count,
    centre_proj,
    neigh_proj,
    centre_table,
    neigh_table,
    basis_proj,
    split_proj,
    update_proj,
    tensor_proj,
    energy_proj,
    species_shift,
):
    atoms, width = latent.shape
    extra = 128
    face_x = atoms // 8
    face_y = atoms // 2
    face_z = atoms // 8
    lengths = [face_x, face_x, face_y, face_y, face_z, face_z]
    starts = [
        0,
        face_x,
        2 * face_x,
        2 * face_x + face_y,
        2 * face_x + 2 * face_y,
        2 * face_x + 2 * face_y + face_z,
    ]
    kinds = jnp.arange(NSPEC, dtype=jnp.int32)

    def lookup(codes, table):
        onehot = (codes[:, None] == kinds[None, :]).astype(jnp.float32)
        return jnp.dot(onehot, table, precision=lax.Precision.HIGHEST)

    def project(rows, codes, weight, table):
        return (
            jnp.dot(rows, weight, preferred_element_type=jnp.float32) + lookup(codes, table)
        ).astype(jnp.bfloat16)

    def spread(onehot, values):
        high = values.astype(jnp.bfloat16)
        low = (values - high.astype(jnp.float32)).astype(jnp.bfloat16)
        return jnp.einsum(
            "nr,nw->rw", onehot, high, preferred_element_type=jnp.float32
        ) + jnp.einsum("nr,nw->rw", onehot, low, preferred_element_type=jnp.float32)

    proj_c = project(latent, species, centre_proj, centre_table)
    proj_n = project(latent, species, neigh_proj, neigh_table)
    send_rows = send_list[0]
    coarse = positions // 16
    fine = positions - coarse * 16
    coord_cols = jnp.concatenate([coarse, fine], axis=0).T.astype(jnp.bfloat16)
    table = jnp.concatenate(
        [proj_n, coord_cols, jnp.zeros((atoms, extra - 6), jnp.bfloat16)], axis=1
    )
    shifts = [(0, -LX_FIX), (0, LX_FIX), (1, -LY_FIX), (1, LY_FIX), (2, -LZ_FIX), (2, LZ_FIX)]
    sections = (("gx", (1, 0)), ("gy", (3, 2)), ("gz", (5, 4)))
    pickers = {}
    base_rows = []
    for section, (axis, segs) in enumerate(sections):
        rows_now = table.shape[0]
        base_rows.append(rows_now)
        parts = [table]
        for number, (segment, direction) in enumerate(((segs[0], 1), (segs[1], -1))):
            picked = send_rows[starts[segment] : starts[segment] + lengths[segment]]
            onehot = (
                picked[:, None] == jnp.arange(rows_now, dtype=jnp.int32)[None, :]
            ).astype(jnp.bfloat16)
            pickers[segment] = onehot
            out = jnp.dot(onehot, table, preferred_element_type=jnp.float32).astype(jnp.bfloat16)
            got = passed_along(out, axis, direction)
            coord_axis, offset = shifts[2 * section + number]
            columns = jnp.arange(width + extra, dtype=jnp.int32)[None, :]
            shift = jnp.where(columns == width + coord_axis, offset // 16, 0).astype(jnp.bfloat16)
            parts.append(got + shift)
        table = jnp.concatenate(parts, axis=0)
    total_rows = table.shape[0]
    neighbour = neighbour.reshape(atoms, K).T.reshape(-1)
    select = (neighbour[:, None] == jnp.arange(total_rows, dtype=jnp.int32)[None, :]).astype(
        jnp.bfloat16
    )
    gathered = jnp.dot(select, table, preferred_element_type=jnp.float32)
    neigh_rows = gathered[:, :width]
    coords_n = (gathered[:, width : width + 3] * 16.0 + gathered[:, width + 3 : width + 6]).T
    delta = (coords_n.reshape(3, K, atoms) - positions.astype(jnp.float32)[:, None, :]) * (
        1.0 / 64.0
    )
    live = (jnp.arange(atoms) < atom_count[0]).astype(jnp.float32)
    valid_pair = live[None, :]

    def energy_of(delta_in, neigh_in, centre_in):
        return pair_energy(
            delta_in,
            neigh_in,
            centre_in,
            valid_pair,
            basis_proj,
            split_proj,
            update_proj,
            tensor_proj,
            energy_proj,
        )

    atom_energy, pull = jax.vjp(energy_of, delta, neigh_rows, proj_c.astype(jnp.float32))
    grad_delta, grad_neigh, grad_centre = pull(jnp.ones_like(atom_energy))
    pairs = grad_neigh.shape[0]
    grads = jnp.concatenate(
        [
            grad_neigh,
            grad_delta.reshape(3, pairs).T,
            jnp.zeros((pairs, extra - 3), jnp.float32),
        ],
        axis=1,
    )
    sums = spread(select, grads)
    own_pos = grad_delta.sum(axis=1)
    sums = sums - jnp.pad(own_pos.T, ((0, total_rows - atoms), (width, extra - 3)))
    for section in (2, 1, 0):
        axis, segs = sections[section]
        rows_now = base_rows[section]
        first = atoms + starts[2 * section]
        second = atoms + starts[2 * section + 1]
        back_first = passed_along(sums[first : first + lengths[2 * section]], axis, -1)
        back_second = passed_along(sums[second : second + lengths[2 * section + 1]], axis, 1)
        sums = (
            sums[:rows_now]
            + spread(pickers[segs[0]], back_first)
            + spread(pickers[segs[1]], back_second)
        )
    back_neigh = neigh_proj.astype(jnp.float32).T
    back_centre = centre_proj.astype(jnp.float32).T
    latent_grad = jnp.dot(grad_centre, back_centre, precision=lax.Precision.HIGHEST)
    latent_grad = latent_grad + jnp.dot(
        sums[:, :width], back_neigh, precision=lax.Precision.HIGHEST
    )
    forces = -sums[:, width : width + 3].T
    energies = live * (lookup(species, species_shift[:, None])[:, 0] + atom_energy)
    return (energies, forces, latent_grad)


def solution(mesh):
    in_specs = (
        P(("gx", "gy", "gz"), None),
        P(None, ("gx", "gy", "gz")),
        P(("gx", "gy", "gz")),
        P(("gx", "gy", "gz"), None),
        P(("gx", "gy", "gz")),
        P(("gx", "gy", "gz")),
        P(),
        P(),
        P(),
        P(),
        P(),
        P(),
        P(),
        P(),
        P(),
        P(),
    )
    out_specs = (P(("gx", "gy", "gz")), P(None, ("gx", "gy", "gz")), P(("gx", "gy", "gz"), None))
    return jax.shard_map(shards, mesh=mesh, in_specs=in_specs, out_specs=out_specs, check_vma=False)
```

```python
import math

import jax
import jax.numpy as jnp
from jax import lax
from jax.sharding import PartitionSpec as P

K = 8
CH = 64
NB = 8
NSPEC = 5
LX_FIX = 1024
LY_FIX = 512
LZ_FIX = 1280


CUTOFF = 6.0
SOFTEN = 0.25


def shortened(shard):
    return jax.tree.map(lambda a: a.astype(jnp.bfloat16) if a.dtype == jnp.float32 else a, shard)


def passed_along(block, axis, distance):
    devices = range(lax.axis_size(axis))
    route = [((i - distance) % len(devices), i) for i in devices]
    return lax.ppermute(block, axis, route)


def by_order(values):
    rest = values.shape[1:]
    return jnp.concatenate(
        [
            values[0:1],
            jnp.broadcast_to(values[1:2], (3,) + rest),
            jnp.broadcast_to(values[2:3], (5,) + rest),
        ],
        axis=0,
    )


def pair_energy(
    delta,
    neigh_rows,
    centre_rows,
    valid_pair,
    basis_proj,
    split_proj,
    update_proj,
    tensor_proj,
    energy_proj,
):
    atoms = centre_rows.shape[0]
    width = centre_rows.shape[1]
    radius = jnp.sqrt(jnp.sum(delta * delta, axis=0) + SOFTEN)
    unit = delta / radius
    ratio = radius / CUTOFF
    envelope = jnp.where(ratio < 1.0, (1.0 - ratio * ratio) ** 2, 0.0) * valid_pair
    orders = jnp.arange(1, NB + 1).astype(jnp.float32)
    basis = (
        jnp.sin(orders[:, None, None] * (math.pi / CUTOFF) * radius[None])
        * (envelope / radius)[None]
    )
    radial = jnp.einsum(
        "nka,nh->kah", basis, basis_proj.astype(jnp.float32), precision=lax.Precision.HIGHEST
    )
    hidden = (
        jax.nn.silu(centre_rows[None] + neigh_rows.reshape(K, atoms, width) + radial)
        * envelope[:, :, None]
    )
    hidden_low = hidden.astype(jnp.bfloat16)
    mixed = jnp.einsum("kah,hq->qka", hidden_low, split_proj, preferred_element_type=jnp.float32)
    amplitude = mixed[: 3 * CH].reshape(3, CH, K, atoms)
    weights = mixed[3 * CH :].reshape(3, CH, K, atoms)
    unit_x = unit[0]
    unit_y = unit[1]
    unit_z = unit[2]
    root3 = math.sqrt(3.0)
    root15 = math.sqrt(15.0)
    root5 = math.sqrt(5.0)
    harmonics = jnp.stack(
        [
            jnp.ones_like(unit_x),
            root3 * unit_x,
            root3 * unit_y,
            root3 * unit_z,
            root15 * unit_x * unit_y,
            root15 * unit_y * unit_z,
            0.5 * root5 * (2.0 * unit_z * unit_z - unit_x * unit_x - unit_y * unit_y),
            root15 * unit_x * unit_z,
            0.5 * root15 * (unit_x * unit_x - unit_y * unit_y),
        ],
        axis=0,
    )
    gathered = by_order(weights) * harmonics[:, None]
    environment = gathered.sum(axis=2) / math.sqrt(K)
    products = by_order(amplitude) * harmonics[:, None] * environment[:, :, None, :]
    scalars = jnp.stack([products[0], products[1:4].sum(axis=0), products[4:9].sum(axis=0)], axis=0)
    scalars = scalars.reshape(3 * CH, K * atoms).astype(jnp.bfloat16)
    flat_low = hidden_low.reshape(K * atoms, width)
    update = jax.nn.silu(
        jnp.dot(flat_low, update_proj, preferred_element_type=jnp.float32)
        + jnp.einsum("qp,qh->ph", scalars, tensor_proj, preferred_element_type=jnp.float32)
    )
    energy = envelope * jnp.sum(
        (hidden + update.reshape(K, atoms, width)) * energy_proj, axis=-1
    )
    return energy.sum(axis=0)


def shards(
    latent,
    positions,
    species,
    send_list,
    neighbour,
    atom_count,
    centre_proj,
    neigh_proj,
    centre_table,
    neigh_table,
    basis_proj,
    split_proj,
    update_proj,
    tensor_proj,
    energy_proj,
    species_shift,
):
    atoms, width = latent.shape
    extra = 128
    face_x = atoms // 8
    face_y = atoms // 2
    face_z = atoms // 8
    lengths = [face_x, face_x, face_y, face_y, face_z, face_z]
    starts = [
        0,
        face_x,
        2 * face_x,
        2 * face_x + face_y,
        2 * face_x + 2 * face_y,
        2 * face_x + 2 * face_y + face_z,
    ]
    kinds = jnp.arange(NSPEC, dtype=jnp.int32)

    def lookup(codes, table):
        onehot = (codes[:, None] == kinds[None, :]).astype(jnp.float32)
        return jnp.dot(onehot, table, precision=lax.Precision.HIGHEST)

    def project(rows, codes, weight, table):
        return (
            jnp.dot(rows, weight, preferred_element_type=jnp.float32) + lookup(codes, table)
        ).astype(jnp.bfloat16)

    def spread(onehot, values):
        high = values.astype(jnp.bfloat16)
        low = (values - high.astype(jnp.float32)).astype(jnp.bfloat16)
        return jnp.einsum(
            "nr,nw->rw", onehot, high, preferred_element_type=jnp.float32
        ) + jnp.einsum("nr,nw->rw", onehot, low, preferred_element_type=jnp.float32)

    proj_c = project(latent, species, centre_proj, centre_table)
    proj_n = project(latent, species, neigh_proj, neigh_table)
    send_rows = send_list[0]
    coarse = positions // 16
    fine = positions - coarse * 16
    coord_cols = jnp.concatenate([coarse, fine], axis=0).T.astype(jnp.bfloat16)
    table = jnp.concatenate(
        [proj_n, coord_cols, jnp.zeros((atoms, extra - 6), jnp.bfloat16)], axis=1
    )
    shifts = [(0, -LX_FIX), (0, LX_FIX), (1, -LY_FIX), (1, LY_FIX), (2, -LZ_FIX), (2, LZ_FIX)]
    sections = (("gx", (1, 0)), ("gy", (3, 2)), ("gz", (5, 4)))
    pickers = {}
    base_rows = []
    for section, (axis, segs) in enumerate(sections):
        rows_now = table.shape[0]
        base_rows.append(rows_now)
        parts = [table]
        for number, (segment, direction) in enumerate(((segs[0], 1), (segs[1], -1))):
            picked = send_rows[starts[segment] : starts[segment] + lengths[segment]]
            onehot = (
                picked[:, None] == jnp.arange(rows_now, dtype=jnp.int32)[None, :]
            ).astype(jnp.bfloat16)
            pickers[segment] = onehot
            out = jnp.dot(onehot, table, preferred_element_type=jnp.float32).astype(jnp.bfloat16)
            got = passed_along(out, axis, direction)
            coord_axis, offset = shifts[2 * section + number]
            columns = jnp.arange(width + extra, dtype=jnp.int32)[None, :]
            shift = jnp.where(columns == width + coord_axis, offset // 16, 0).astype(jnp.bfloat16)
            parts.append(got + shift)
        table = jnp.concatenate(parts, axis=0)
    total_rows = table.shape[0]
    neighbour = neighbour.reshape(atoms, K).T.reshape(-1)
    select = (neighbour[:, None] == jnp.arange(total_rows, dtype=jnp.int32)[None, :]).astype(
        jnp.bfloat16
    )
    gathered = jnp.dot(select, table, preferred_element_type=jnp.float32)
    neigh_rows = gathered[:, :width]
    coords_n = (gathered[:, width : width + 3] * 16.0 + gathered[:, width + 3 : width + 6]).T
    delta = (coords_n.reshape(3, K, atoms) - positions.astype(jnp.float32)[:, None, :]) * (
        1.0 / 64.0
    )
    live = (jnp.arange(atoms) < atom_count[0]).astype(jnp.float32)
    valid_pair = live[None, :]

    def energy_of(delta_in, neigh_in, centre_in):
        return pair_energy(
            delta_in,
            neigh_in,
            centre_in,
            valid_pair,
            basis_proj,
            split_proj,
            update_proj,
            tensor_proj,
            energy_proj,
        )

    atom_energy, pull = jax.vjp(energy_of, delta, neigh_rows, proj_c.astype(jnp.float32))
    grad_delta, grad_neigh, grad_centre = pull(jnp.ones_like(atom_energy))
    pairs = grad_neigh.shape[0]
    grads = jnp.concatenate(
        [
            grad_neigh,
            grad_delta.reshape(3, pairs).T,
            jnp.zeros((pairs, extra - 3), jnp.float32),
        ],
        axis=1,
    )
    sums = spread(select, grads)
    own_pos = grad_delta.sum(axis=1)
    sums = sums - jnp.pad(own_pos.T, ((0, total_rows - atoms), (width, extra - 3)))
    for section in (2, 1, 0):
        axis, segs = sections[section]
        rows_now = base_rows[section]
        first = atoms + starts[2 * section]
        second = atoms + starts[2 * section + 1]
        back_first = passed_along(sums[first : first + lengths[2 * section]], axis, -1)
        back_second = passed_along(sums[second : second + lengths[2 * section + 1]], axis, 1)
        sums = (
            sums[:rows_now]
            + spread(pickers[segs[0]], back_first)
            + spread(pickers[segs[1]], back_second)
        )
    back_neigh = neigh_proj.astype(jnp.float32).T
    back_centre = centre_proj.astype(jnp.float32).T
    latent_grad = jnp.dot(grad_centre, back_centre, precision=lax.Precision.HIGHEST)
    latent_grad = latent_grad + jnp.dot(
        sums[:, :width], back_neigh, precision=lax.Precision.HIGHEST
    )
    forces = -sums[:, width : width + 3].T
    energies = live * (lookup(species, species_shift[:, None])[:, 0] + atom_energy)
    return (energies, forces, latent_grad)


def solution(mesh):
    in_specs = (
        P(("gx", "gy", "gz"), None),
        P(None, ("gx", "gy", "gz")),
        P(("gx", "gy", "gz")),
        P(("gx", "gy", "gz"), None),
        P(("gx", "gy", "gz")),
        P(("gx", "gy", "gz")),
        P(),
        P(),
        P(),
        P(),
        P(),
        P(),
        P(),
        P(),
        P(),
        P(),
    )
    out_specs = (P(("gx", "gy", "gz")), P(None, ("gx", "gy", "gz")), P(("gx", "gy", "gz"), None))
    return jax.shard_map(shards, mesh=mesh, in_specs=in_specs, out_specs=out_specs, check_vma=False)
```

```python
import math

import jax
import jax.numpy as jnp
from jax import lax
from jax.sharding import PartitionSpec as P

K = 8
CH = 64
NB = 8
NSPEC = 5
LX_FIX = 1024
LY_FIX = 512
LZ_FIX = 1280


CUTOFF = 6.0
SOFTEN = 0.25


def shortened(shard):
    return jax.tree.map(lambda a: a.astype(jnp.bfloat16) if a.dtype == jnp.float32 else a, shard)


def passed_along(block, axis, distance):
    devices = range(lax.axis_size(axis))
    route = [((i - distance) % len(devices), i) for i in devices]
    return lax.ppermute(block, axis, route)


def by_order(values):
    rest = values.shape[1:]
    return jnp.concatenate(
        [
            values[0:1],
            jnp.broadcast_to(values[1:2], (3,) + rest),
            jnp.broadcast_to(values[2:3], (5,) + rest),
        ],
        axis=0,
    )


def pair_energy(
    delta,
    neigh_rows,
    centre_rows,
    valid_pair,
    basis_proj,
    split_proj,
    update_proj,
    tensor_proj,
    energy_proj,
):
    atoms = centre_rows.shape[0]
    width = centre_rows.shape[1]
    radius = jnp.sqrt(jnp.sum(delta * delta, axis=0) + SOFTEN)
    unit = delta / radius
    ratio = radius / CUTOFF
    envelope = jnp.where(ratio < 1.0, (1.0 - ratio * ratio) ** 2, 0.0) * valid_pair
    orders = jnp.arange(1, NB + 1).astype(jnp.float32)
    basis = (
        jnp.sin(orders[:, None, None] * (math.pi / CUTOFF) * radius[None])
        * (envelope / radius)[None]
    )
    basis_rows = basis_proj.astype(jnp.float32)
    radial = basis[0][:, :, None] * basis_rows[0]
    for order in range(1, NB):
        radial = radial + basis[order][:, :, None] * basis_rows[order]
    hidden = (
        jax.nn.silu(centre_rows[None] + neigh_rows.reshape(K, atoms, width) + radial)
        * envelope[:, :, None]
    )
    hidden_low = hidden.astype(jnp.bfloat16)
    mixed = jnp.einsum("kah,hq->qka", hidden_low, split_proj, preferred_element_type=jnp.float32)
    amplitude = mixed[: 3 * CH].reshape(3, CH, K, atoms)
    weights = mixed[3 * CH :].reshape(3, CH, K, atoms)
    unit_x = unit[0]
    unit_y = unit[1]
    unit_z = unit[2]
    root3 = math.sqrt(3.0)
    root15 = math.sqrt(15.0)
    root5 = math.sqrt(5.0)
    harmonics = jnp.stack(
        [
            jnp.ones_like(unit_x),
            root3 * unit_x,
            root3 * unit_y,
            root3 * unit_z,
            root15 * unit_x * unit_y,
            root15 * unit_y * unit_z,
            0.5 * root5 * (2.0 * unit_z * unit_z - unit_x * unit_x - unit_y * unit_y),
            root15 * unit_x * unit_z,
            0.5 * root15 * (unit_x * unit_x - unit_y * unit_y),
        ],
        axis=0,
    )
    gathered = by_order(weights) * harmonics[:, None]
    environment = gathered.sum(axis=2) / math.sqrt(K)
    products = by_order(amplitude) * harmonics[:, None] * environment[:, :, None, :]
    scalars = jnp.stack([products[0], products[1:4].sum(axis=0), products[4:9].sum(axis=0)], axis=0)
    scalars = scalars.reshape(3 * CH, K * atoms).astype(jnp.bfloat16)
    flat_low = hidden_low.reshape(K * atoms, width)
    update = jax.nn.silu(
        jnp.dot(flat_low, update_proj, preferred_element_type=jnp.float32)
        + jnp.einsum("qp,qh->ph", scalars, tensor_proj, preferred_element_type=jnp.float32)
    )
    energy = envelope * jnp.sum(
        (hidden + update.reshape(K, atoms, width)) * energy_proj, axis=-1
    )
    return energy.sum(axis=0)


def shards(
    latent,
    positions,
    species,
    send_list,
    neighbour,
    atom_count,
    centre_proj,
    neigh_proj,
    centre_table,
    neigh_table,
    basis_proj,
    split_proj,
    update_proj,
    tensor_proj,
    energy_proj,
    species_shift,
):
    atoms, width = latent.shape
    extra = 128
    face_x = atoms // 8
    face_y = atoms // 2
    face_z = atoms // 8
    lengths = [face_x, face_x, face_y, face_y, face_z, face_z]
    starts = [
        0,
        face_x,
        2 * face_x,
        2 * face_x + face_y,
        2 * face_x + 2 * face_y,
        2 * face_x + 2 * face_y + face_z,
    ]
    kinds = jnp.arange(NSPEC, dtype=jnp.int32)

    def lookup(codes, table):
        found = jnp.zeros((codes.shape[0], table.shape[1]), jnp.float32)
        for kind in range(NSPEC):
            found = jnp.where(codes[:, None] == kind, table[kind][None, :], found)
        return found

    def project(rows, codes, weight, table):
        return (
            jnp.dot(rows, weight, preferred_element_type=jnp.float32) + lookup(codes, table)
        ).astype(jnp.bfloat16)

    def spread(onehot, values):
        high = values.astype(jnp.bfloat16)
        low = (values - high.astype(jnp.float32)).astype(jnp.bfloat16)
        return jnp.einsum(
            "nr,nw->rw", onehot, high, preferred_element_type=jnp.float32
        ) + jnp.einsum("nr,nw->rw", onehot, low, preferred_element_type=jnp.float32)

    proj_c = project(latent, species, centre_proj, centre_table)
    proj_n = project(latent, species, neigh_proj, neigh_table)
    send_rows = send_list[0]
    coarse = positions // 16
    fine = positions - coarse * 16
    coord_cols = jnp.concatenate([coarse, fine], axis=0).T.astype(jnp.bfloat16)
    table = jnp.concatenate(
        [proj_n, coord_cols, jnp.zeros((atoms, extra - 6), jnp.bfloat16)], axis=1
    )
    shifts = [(0, -LX_FIX), (0, LX_FIX), (1, -LY_FIX), (1, LY_FIX), (2, -LZ_FIX), (2, LZ_FIX)]
    sections = (("gx", (1, 0)), ("gy", (3, 2)), ("gz", (5, 4)))
    pickers = {}
    base_rows = []
    for section, (axis, segs) in enumerate(sections):
        rows_now = table.shape[0]
        base_rows.append(rows_now)
        parts = [table]
        outs = []
        for segment in segs:
            picked = send_rows[starts[segment] : starts[segment] + lengths[segment]]
            onehot = (
                picked[:, None] == jnp.arange(rows_now, dtype=jnp.int32)[None, :]
            ).astype(jnp.bfloat16)
            pickers[segment] = onehot
            outs.append(
                jnp.dot(onehot, table, preferred_element_type=jnp.float32).astype(jnp.bfloat16)
            )
        if lax.axis_size(axis) == 2:
            both = passed_along(jnp.concatenate(outs, axis=0), axis, 1)
            arrived = [both[: outs[0].shape[0]], both[outs[0].shape[0] :]]
        else:
            arrived = [passed_along(outs[0], axis, 1), passed_along(outs[1], axis, -1)]
        for number in range(2):
            got = arrived[number]
            coord_axis, offset = shifts[2 * section + number]
            columns = jnp.arange(width + extra, dtype=jnp.int32)[None, :]
            shift = jnp.where(columns == width + coord_axis, offset // 16, 0).astype(jnp.bfloat16)
            parts.append(got + shift)
        table = jnp.concatenate(parts, axis=0)
    total_rows = table.shape[0]
    neighbour = neighbour.reshape(atoms, K).T.reshape(-1)
    select = (neighbour[:, None] == jnp.arange(total_rows, dtype=jnp.int32)[None, :]).astype(
        jnp.bfloat16
    )
    neigh_rows = jnp.dot(select, table[:, :width], preferred_element_type=jnp.float32)
    gathered = jnp.dot(select, table[:, width:], preferred_element_type=jnp.float32)
    coords_n = (gathered[:, 0:3] * 16.0 + gathered[:, 3:6]).T
    delta = (coords_n.reshape(3, K, atoms) - positions.astype(jnp.float32)[:, None, :]) * (
        1.0 / 64.0
    )
    live = (jnp.arange(atoms) < atom_count[0]).astype(jnp.float32)
    valid_pair = live[None, :]

    def energy_of(delta_in, neigh_in, centre_in):
        return pair_energy(
            delta_in,
            neigh_in,
            centre_in,
            valid_pair,
            basis_proj,
            split_proj,
            update_proj,
            tensor_proj,
            energy_proj,
        )

    atom_energy, pull = jax.vjp(energy_of, delta, neigh_rows, proj_c.astype(jnp.float32))
    grad_delta, grad_neigh, grad_centre = pull(jnp.ones_like(atom_energy))
    pairs = grad_neigh.shape[0]
    pos_grads = jnp.concatenate(
        [grad_delta.reshape(3, pairs).T, jnp.zeros((pairs, extra - 3), jnp.float32)], axis=1
    )
    sums = jnp.concatenate([spread(select, grad_neigh), spread(select, pos_grads)], axis=1)
    own_pos = grad_delta.sum(axis=1)
    sums = sums - jnp.pad(own_pos.T, ((0, total_rows - atoms), (width, extra - 3)))
    for section in (2, 1, 0):
        axis, segs = sections[section]
        rows_now = base_rows[section]
        first = atoms + starts[2 * section]
        second = atoms + starts[2 * section + 1]
        if lax.axis_size(axis) == 2:
            both = passed_along(sums[first : second + lengths[2 * section + 1]], axis, 1)
            back_first = both[: lengths[2 * section]]
            back_second = both[lengths[2 * section] :]
        else:
            back_first = passed_along(sums[first : first + lengths[2 * section]], axis, -1)
            back_second = passed_along(sums[second : second + lengths[2 * section + 1]], axis, 1)
        sums = (
            sums[:rows_now]
            + spread(pickers[segs[0]], back_first)
            + spread(pickers[segs[1]], back_second)
        )
    back_neigh = neigh_proj.astype(jnp.float32).T
    back_centre = centre_proj.astype(jnp.float32).T
    latent_grad = jnp.dot(grad_centre, back_centre, precision=lax.Precision.HIGHEST)
    latent_grad = latent_grad + jnp.dot(
        sums[:, :width], back_neigh, precision=lax.Precision.HIGHEST
    )
    forces = -sums[:, width : width + 3].T
    energies = live * (lookup(species, species_shift[:, None])[:, 0] + atom_energy)
    return (energies, forces, latent_grad)


def solution(mesh):
    in_specs = (
        P(("gx", "gy", "gz"), None),
        P(None, ("gx", "gy", "gz")),
        P(("gx", "gy", "gz")),
        P(("gx", "gy", "gz"), None),
        P(("gx", "gy", "gz")),
        P(("gx", "gy", "gz")),
        P(),
        P(),
        P(),
        P(),
        P(),
        P(),
        P(),
        P(),
        P(),
        P(),
    )
    out_specs = (P(("gx", "gy", "gz")), P(None, ("gx", "gy", "gz")), P(("gx", "gy", "gz"), None))
    return jax.shard_map(shards, mesh=mesh, in_specs=in_specs, out_specs=out_specs, check_vma=False)
```

```python
import math

import jax
import jax.numpy as jnp
from jax import lax
from jax.sharding import PartitionSpec as P

K = 8
CH = 64
NB = 8
NSPEC = 5
LX_FIX = 1024
LY_FIX = 512
LZ_FIX = 1280


CUTOFF = 6.0
SOFTEN = 0.25


def shortened(shard):
    return jax.tree.map(lambda a: a.astype(jnp.bfloat16) if a.dtype == jnp.float32 else a, shard)


def passed_along(block, axis, distance):
    devices = range(lax.axis_size(axis))
    route = [((i - distance) % len(devices), i) for i in devices]
    return lax.ppermute(block, axis, route)


def by_order(values):
    rest = values.shape[1:]
    return jnp.concatenate(
        [
            values[0:1],
            jnp.broadcast_to(values[1:2], (3,) + rest),
            jnp.broadcast_to(values[2:3], (5,) + rest),
        ],
        axis=0,
    )


def pair_energy(
    delta,
    neigh_cols,
    centre_cols,
    valid_pair,
    basis_proj,
    split_proj,
    update_proj,
    tensor_proj,
    energy_proj,
):
    atoms = centre_cols.shape[1]
    radius = jnp.sqrt(jnp.sum(delta * delta, axis=0) + SOFTEN)
    unit = delta / radius
    ratio = radius / CUTOFF
    envelope = jnp.where(ratio < 1.0, (1.0 - ratio * ratio) ** 2, 0.0) * valid_pair
    orders = jnp.arange(1, NB + 1).astype(jnp.float32)
    basis = (
        jnp.sin(orders[:, None, None] * (math.pi / CUTOFF) * radius[None])
        * (envelope / radius)[None]
    )
    radial = jnp.einsum(
        "nka,nh->hka", basis, basis_proj.astype(jnp.float32), precision=lax.Precision.HIGHEST
    )
    hidden = jax.nn.silu(centre_cols[:, None, :] + neigh_cols + radial) * envelope[None]
    hidden_low = hidden.astype(jnp.bfloat16)
    mixed = jnp.einsum("hka,hq->qka", hidden_low, split_proj, preferred_element_type=jnp.float32)
    amplitude = mixed[: 3 * CH].reshape(3, CH, K, atoms)
    weights = mixed[3 * CH :].reshape(3, CH, K, atoms)
    unit_x = unit[0]
    unit_y = unit[1]
    unit_z = unit[2]
    root3 = math.sqrt(3.0)
    root15 = math.sqrt(15.0)
    root5 = math.sqrt(5.0)
    harmonics = jnp.stack(
        [
            jnp.ones_like(unit_x),
            root3 * unit_x,
            root3 * unit_y,
            root3 * unit_z,
            root15 * unit_x * unit_y,
            root15 * unit_y * unit_z,
            0.5 * root5 * (2.0 * unit_z * unit_z - unit_x * unit_x - unit_y * unit_y),
            root15 * unit_x * unit_z,
            0.5 * root15 * (unit_x * unit_x - unit_y * unit_y),
        ],
        axis=0,
    )
    gathered = by_order(weights) * harmonics[:, None]
    environment = gathered.sum(axis=2) / math.sqrt(K)
    products = by_order(amplitude) * harmonics[:, None] * environment[:, :, None, :]
    scalars = jnp.stack([products[0], products[1:4].sum(axis=0), products[4:9].sum(axis=0)], axis=0)
    scalars = scalars.reshape(3 * CH, K, atoms).astype(jnp.bfloat16)
    update = jax.nn.silu(
        jnp.einsum("hka,hi->ika", hidden_low, update_proj, preferred_element_type=jnp.float32)
        + jnp.einsum("qka,qi->ika", scalars, tensor_proj, preferred_element_type=jnp.float32)
    )
    energy = envelope * jnp.sum((hidden + update) * energy_proj[:, None, None], axis=0)
    return energy.sum(axis=0)


def shards(
    latent,
    positions,
    species,
    send_list,
    neighbour,
    atom_count,
    centre_proj,
    neigh_proj,
    centre_table,
    neigh_table,
    basis_proj,
    split_proj,
    update_proj,
    tensor_proj,
    energy_proj,
    species_shift,
):
    atoms, width = latent.shape
    extra = 128
    face_x = atoms // 8
    face_y = atoms // 2
    face_z = atoms // 8
    lengths = [face_x, face_x, face_y, face_y, face_z, face_z]
    starts = [
        0,
        face_x,
        2 * face_x,
        2 * face_x + face_y,
        2 * face_x + 2 * face_y,
        2 * face_x + 2 * face_y + face_z,
    ]
    kinds = jnp.arange(NSPEC, dtype=jnp.int32)

    def lookup(codes, table):
        onehot = (codes[:, None] == kinds[None, :]).astype(jnp.float32)
        return jnp.dot(onehot, table, precision=lax.Precision.HIGHEST)

    def project(rows, codes, weight, table):
        return (
            jnp.dot(rows, weight, preferred_element_type=jnp.float32) + lookup(codes, table)
        ).astype(jnp.bfloat16)

    def spread_cols(onehot, values):
        high = values.astype(jnp.bfloat16)
        low = (values - high.astype(jnp.float32)).astype(jnp.bfloat16)
        return jnp.einsum(
            "wn,nr->wr", high, onehot, preferred_element_type=jnp.float32
        ) + jnp.einsum("wn,nr->wr", low, onehot, preferred_element_type=jnp.float32)

    def spread(onehot, values):
        high = values.astype(jnp.bfloat16)
        low = (values - high.astype(jnp.float32)).astype(jnp.bfloat16)
        return jnp.einsum(
            "nr,nw->rw", onehot, high, preferred_element_type=jnp.float32
        ) + jnp.einsum("nr,nw->rw", onehot, low, preferred_element_type=jnp.float32)

    proj_c = project(latent, species, centre_proj, centre_table)
    proj_n = project(latent, species, neigh_proj, neigh_table)
    send_rows = send_list[0]
    coarse = positions // 16
    fine = positions - coarse * 16
    coord_cols = jnp.concatenate([coarse, fine], axis=0).T.astype(jnp.bfloat16)
    table = jnp.concatenate(
        [proj_n, coord_cols, jnp.zeros((atoms, extra - 6), jnp.bfloat16)], axis=1
    )
    shifts = [(0, -LX_FIX), (0, LX_FIX), (1, -LY_FIX), (1, LY_FIX), (2, -LZ_FIX), (2, LZ_FIX)]
    sections = (("gx", (1, 0)), ("gy", (3, 2)), ("gz", (5, 4)))
    pickers = {}
    base_rows = []
    for section, (axis, segs) in enumerate(sections):
        rows_now = table.shape[0]
        base_rows.append(rows_now)
        parts = [table]
        for number, (segment, direction) in enumerate(((segs[0], 1), (segs[1], -1))):
            picked = send_rows[starts[segment] : starts[segment] + lengths[segment]]
            onehot = (
                picked[:, None] == jnp.arange(rows_now, dtype=jnp.int32)[None, :]
            ).astype(jnp.bfloat16)
            pickers[segment] = onehot
            out = jnp.dot(onehot, table, preferred_element_type=jnp.float32).astype(jnp.bfloat16)
            got = passed_along(out, axis, direction)
            coord_axis, offset = shifts[2 * section + number]
            columns = jnp.arange(width + extra, dtype=jnp.int32)[None, :]
            shift = jnp.where(columns == width + coord_axis, offset // 16, 0).astype(jnp.bfloat16)
            parts.append(got + shift)
        table = jnp.concatenate(parts, axis=0)
    total_rows = table.shape[0]
    neighbour = neighbour.reshape(atoms, K).T.reshape(-1)
    select = (neighbour[:, None] == jnp.arange(total_rows, dtype=jnp.int32)[None, :]).astype(
        jnp.bfloat16
    )
    gathered = jnp.einsum("tw,pt->wp", table, select, preferred_element_type=jnp.float32)
    neigh_cols = gathered[:width].reshape(width, K, atoms)
    coords_n = gathered[width : width + 3] * 16.0 + gathered[width + 3 : width + 6]
    delta = (coords_n.reshape(3, K, atoms) - positions.astype(jnp.float32)[:, None, :]) * (
        1.0 / 64.0
    )
    live = (jnp.arange(atoms) < atom_count[0]).astype(jnp.float32)
    valid_pair = live[None, :]

    def energy_of(delta_in, neigh_in, centre_in):
        return pair_energy(
            delta_in,
            neigh_in,
            centre_in,
            valid_pair,
            basis_proj,
            split_proj,
            update_proj,
            tensor_proj,
            energy_proj,
        )

    atom_energy, pull = jax.vjp(energy_of, delta, neigh_cols, proj_c.astype(jnp.float32).T)
    grad_delta, grad_neigh, grad_centre = pull(jnp.ones_like(atom_energy))
    pairs = K * atoms
    grads = jnp.concatenate(
        [
            grad_neigh.reshape(width, pairs),
            grad_delta.reshape(3, pairs),
            jnp.zeros((extra - 3, pairs), jnp.float32),
        ],
        axis=0,
    )
    sums = spread_cols(select, grads).T
    own_pos = grad_delta.sum(axis=1)
    sums = sums - jnp.pad(own_pos.T, ((0, total_rows - atoms), (width, extra - 3)))
    for section in (2, 1, 0):
        axis, segs = sections[section]
        rows_now = base_rows[section]
        first = atoms + starts[2 * section]
        second = atoms + starts[2 * section + 1]
        back_first = passed_along(sums[first : first + lengths[2 * section]], axis, -1)
        back_second = passed_along(sums[second : second + lengths[2 * section + 1]], axis, 1)
        sums = (
            sums[:rows_now]
            + spread(pickers[segs[0]], back_first)
            + spread(pickers[segs[1]], back_second)
        )
    back_neigh = neigh_proj.astype(jnp.float32).T
    back_centre = centre_proj.astype(jnp.float32).T
    latent_grad = jnp.dot(grad_centre.T, back_centre, precision=lax.Precision.HIGHEST)
    latent_grad = latent_grad + jnp.dot(
        sums[:, :width], back_neigh, precision=lax.Precision.HIGHEST
    )
    forces = -sums[:, width : width + 3].T
    energies = live * (lookup(species, species_shift[:, None])[:, 0] + atom_energy)
    return (energies, forces, latent_grad)


def solution(mesh):
    in_specs = (
        P(("gx", "gy", "gz"), None),
        P(None, ("gx", "gy", "gz")),
        P(("gx", "gy", "gz")),
        P(("gx", "gy", "gz"), None),
        P(("gx", "gy", "gz")),
        P(("gx", "gy", "gz")),
        P(),
        P(),
        P(),
        P(),
        P(),
        P(),
        P(),
        P(),
        P(),
        P(),
    )
    out_specs = (P(("gx", "gy", "gz")), P(None, ("gx", "gy", "gz")), P(("gx", "gy", "gz"), None))
    return jax.shard_map(shards, mesh=mesh, in_specs=in_specs, out_specs=out_specs, check_vma=False)
```

```python
import math

import jax
import jax.numpy as jnp
from jax import lax
from jax.experimental import pallas as pl
from jax.experimental.pallas import tpu as pltpu
from jax.sharding import PartitionSpec as P

K = 8
CH = 64
NB = 8
NSPEC = 5
LX_FIX = 1024
LY_FIX = 512
LZ_FIX = 1280


CUTOFF = 6.0
SOFTEN = 0.25


def shortened(shard):
    return jax.tree.map(lambda a: a.astype(jnp.bfloat16) if a.dtype == jnp.float32 else a, shard)


def passed_along(block, axis, distance):
    devices = range(lax.axis_size(axis))
    route = [((i - distance) % len(devices), i) for i in devices]
    return lax.ppermute(block, axis, route)


def by_order(values):
    rest = values.shape[1:]
    return jnp.concatenate(
        [
            values[0:1],
            jnp.broadcast_to(values[1:2], (3,) + rest),
            jnp.broadcast_to(values[2:3], (5,) + rest),
        ],
        axis=0,
    )


ORDER_OF = (0, 1, 1, 1, 2, 2, 2, 2, 2)
GROUPS = ((0,), (1, 2, 3), (4, 5, 6, 7, 8))


def geometry(delta, valid_pair):
    atoms = delta.shape[2]
    radius = jnp.sqrt(jnp.sum(delta * delta, axis=0) + SOFTEN)
    unit = delta / radius
    ratio = radius / CUTOFF
    envelope = jnp.where(ratio < 1.0, (1.0 - ratio * ratio) ** 2, 0.0) * valid_pair
    orders = jnp.arange(1, NB + 1).astype(jnp.float32)
    basis = (
        jnp.sin(orders[:, None, None] * (math.pi / CUTOFF) * radius[None])
        * (envelope / radius)[None]
    )
    ux, uy, uz = unit[0], unit[1], unit[2]
    r3 = math.sqrt(3.0)
    r15 = math.sqrt(15.0)
    r5 = math.sqrt(5.0)
    harmonics = jnp.stack(
        [
            jnp.ones_like(ux),
            r3 * ux,
            r3 * uy,
            r3 * uz,
            r15 * ux * uy,
            r15 * uy * uz,
            0.5 * r5 * (2.0 * uz * uz - ux * ux - uy * uy),
            r15 * ux * uz,
            0.5 * r15 * (ux * ux - uy * uy),
        ],
        axis=0,
    )
    cols = jnp.concatenate([basis, envelope[None], harmonics], axis=0).reshape(18, K * atoms)
    cols = jnp.concatenate([cols, jnp.zeros((128 - 18, K * atoms), jnp.float32)], axis=0)
    return cols.T


def _mm(a, b):
    return jnp.dot(a, b, preferred_element_type=jnp.float32)


def _sigmoid(v):
    return 1.0 / (1.0 + jnp.exp(-v))


def _pair_kernel(
    rows_ref, centre_ref, geo_ref, basis_ref, split_ref, split_t_ref, update_ref,
    update_t_ref, tensor_ref, tensor_t_ref, basis_t_ref, energy_w_ref,
    grad_rows_ref, grad_centre_ref, grad_geo_ref, energy_ref,
    pre_s, hidden_s, mixed_s, damp_s, dlow_s, dgeo_s, env_s, denv_s,
):
    atoms = centre_ref.shape[0]
    f32 = jnp.float32
    bf16 = jnp.bfloat16
    lane = lax.broadcasted_iota(jnp.int32, (atoms, 128), 1)
    inv_root = 1.0 / math.sqrt(K)
    env_s[...] = jnp.zeros_like(env_s)
    denv_s[...] = jnp.zeros_like(denv_s)

    def block(k):
        return pl.ds(pl.multiple_of(k * atoms, atoms), atoms)

    def split_dot(values, weight_ref):
        high = values.astype(bf16)
        low = (values - high.astype(f32)).astype(bf16)
        return _mm(high, weight_ref[...]) + _mm(low, weight_ref[...])

    def first(k, carry):
        at = block(k)
        geo = geo_ref[at, :]
        radial = split_dot(geo, basis_ref)
        pre = centre_ref[...] + rows_ref[at, :].astype(f32) + radial
        envelope = geo[:, 8:9]
        hidden = pre * _sigmoid(pre) * envelope
        pre_s[at, :] = pre
        hidden_s[at, :] = hidden
        mixed = _mm(hidden.astype(bf16), split_ref[...])
        mixed_s[at, :] = mixed
        for m in range(9):
            l = ORDER_OF[m]
            weight = mixed[:, (2 * l + 1) * 128 : (2 * l + 2) * 128]
            env_s[m] = env_s[m] + weight * geo[:, 9 + m : 10 + m] * inv_root
        return carry

    lax.fori_loop(0, K, first, 0)

    def second(k, energy):
        at = block(k)
        geo = geo_ref[at, :]
        envelope = geo[:, 8:9]
        hidden = hidden_s[at, :]
        mixed = mixed_s[at, :]
        parts = []
        totals = []
        for l in range(3):
            total = 0.0
            for m in GROUPS[l]:
                total = total + geo[:, 9 + m : 10 + m] * env_s[m]
            totals.append(total)
            parts.append((mixed[:, 2 * l * 128 : (2 * l + 1) * 128] * total).astype(bf16))
        scalars = jnp.concatenate(parts, axis=1)
        z = _mm(hidden.astype(bf16), update_ref[...]) + _mm(scalars, tensor_ref[...])
        gate = _sigmoid(z)
        update = z * gate
        readout = jnp.sum((hidden + update) * energy_w_ref[...], axis=1, keepdims=True)
        energy = energy + envelope * readout
        grad_sum = envelope * energy_w_ref[...]
        dz = grad_sum * (gate * (1.0 + z * (1.0 - gate)))
        dz_low = dz.astype(bf16)
        dscalars = _mm(dz_low, tensor_t_ref[...])
        dscalars = dscalars.astype(bf16).astype(f32)
        dlow_s[at, :] = _mm(dz_low, update_t_ref[...])
        dgeo = jnp.where(lane == 8, readout, 0.0)
        for l in range(3):
            ds = dscalars[:, l * 128 : (l + 1) * 128]
            damp_s[at, l * 128 : (l + 1) * 128] = ds * totals[l]
            dtotal = ds * mixed[:, 2 * l * 128 : (2 * l + 1) * 128]
            for m in GROUPS[l]:
                dgeo = dgeo + jnp.where(
                    lane == 9 + m, jnp.sum(dtotal * env_s[m], axis=1, keepdims=True), 0.0
                )
                denv_s[m] = denv_s[m] + dtotal * geo[:, 9 + m : 10 + m]
        dgeo_s[at, :] = dgeo
        return energy

    energy = lax.fori_loop(0, K, second, jnp.zeros((atoms, 1), f32))
    energy_ref[...] = jnp.broadcast_to(energy, (atoms, 128))

    def third(k, centre_grad):
        at = block(k)
        geo = geo_ref[at, :]
        envelope = geo[:, 8:9]
        mixed = mixed_s[at, :]
        dgeo = dgeo_s[at, :]
        dmixed = []
        for l in range(3):
            weight = mixed[:, (2 * l + 1) * 128 : (2 * l + 2) * 128]
            dweight = 0.0
            for m in GROUPS[l]:
                y = geo[:, 9 + m : 10 + m]
                dweight = dweight + denv_s[m] * y * inv_root
                dgeo = dgeo + jnp.where(
                    lane == 9 + m,
                    jnp.sum(denv_s[m] * weight, axis=1, keepdims=True) * inv_root,
                    0.0,
                )
            dmixed.append(damp_s[at, l * 128 : (l + 1) * 128])
            dmixed.append(dweight)
        dmixed = jnp.concatenate(dmixed, axis=1).astype(bf16)
        dlow = dlow_s[at, :] + _mm(dmixed, split_t_ref[...])
        dhidden = envelope * energy_w_ref[...] + dlow
        pre = pre_s[at, :]
        sig = _sigmoid(pre)
        act = pre * sig
        dgeo = dgeo + jnp.where(lane == 8, jnp.sum(dhidden * act, axis=1, keepdims=True), 0.0)
        dpre = dhidden * envelope * (sig * (1.0 + pre * (1.0 - sig)))
        grad_rows_ref[at, :] = dpre
        dgeo = dgeo + split_dot(dpre, basis_t_ref)
        grad_geo_ref[at, :] = dgeo
        return centre_grad + dpre

    grad_centre_ref[...] = lax.fori_loop(
        0, K, third, jnp.zeros(grad_centre_ref.shape, f32)
    )


def pair_terms(rows, centre, geo, basis_proj, split_proj, update_proj, tensor_proj, energy_proj):
    pairs, width = rows.shape
    atoms = centre.shape[0]
    f32 = jnp.float32
    bf16 = jnp.bfloat16
    blocks = []
    for l in range(3):
        blocks.append(split_proj[:, l * CH : (l + 1) * CH])
        blocks.append(jnp.zeros((width, 128 - CH), bf16))
        blocks.append(split_proj[:, 3 * CH + l * CH : 3 * CH + (l + 1) * CH])
        blocks.append(jnp.zeros((width, 128 - CH), bf16))
    split_pad = jnp.concatenate(blocks, axis=1)
    tensor_pad = jnp.concatenate(
        sum(
            [
                [tensor_proj[l * CH : (l + 1) * CH], jnp.zeros((128 - CH, width), bf16)]
                for l in range(3)
            ],
            [],
        ),
        axis=0,
    )
    basis_pad = jnp.concatenate(
        [basis_proj, jnp.zeros((128 - NB, width), bf16)], axis=0
    )
    vmem = pl.BlockSpec(memory_space=pltpu.VMEM)
    outs = pl.pallas_call(
        _pair_kernel,
        out_shape=(
            jax.ShapeDtypeStruct((pairs, width), f32),
            jax.ShapeDtypeStruct((atoms, width), f32),
            jax.ShapeDtypeStruct((pairs, 128), f32),
            jax.ShapeDtypeStruct((atoms, 128), f32),
        ),
        in_specs=[vmem] * 12,
        out_specs=(vmem, vmem, vmem, vmem),
        scratch_shapes=[
            pltpu.VMEM((pairs, width), f32),
            pltpu.VMEM((pairs, width), f32),
            pltpu.VMEM((pairs, 6 * 128), f32),
            pltpu.VMEM((pairs, 3 * 128), f32),
            pltpu.VMEM((pairs, width), f32),
            pltpu.VMEM((pairs, 128), f32),
            pltpu.VMEM((9, atoms, 128), f32),
            pltpu.VMEM((9, atoms, 128), f32),
        ],
        compiler_params=pltpu.CompilerParams(vmem_limit_bytes=60 * 1024 * 1024),
        cost_estimate=pl.CostEstimate(
            flops=int(40 * pairs * width * 128), transcendentals=int(3 * pairs * width),
            bytes_accessed=int(16 * pairs * width),
        ),
    )(
        rows,
        centre,
        geo,
        basis_pad,
        split_pad,
        split_pad.T,
        update_proj,
        update_proj.T,
        tensor_pad,
        tensor_pad.T,
        basis_pad.T,
        energy_proj.astype(f32)[None, :],
    )
    grad_rows, grad_centre, grad_geo, energy = outs
    return grad_rows, grad_centre, grad_geo, energy[:, 0]


def shards(
    latent,
    positions,
    species,
    send_list,
    neighbour,
    atom_count,
    centre_proj,
    neigh_proj,
    centre_table,
    neigh_table,
    basis_proj,
    split_proj,
    update_proj,
    tensor_proj,
    energy_proj,
    species_shift,
):
    atoms, width = latent.shape
    extra = 128
    face_x = atoms // 8
    face_y = atoms // 2
    face_z = atoms // 8
    lengths = [face_x, face_x, face_y, face_y, face_z, face_z]
    starts = [
        0,
        face_x,
        2 * face_x,
        2 * face_x + face_y,
        2 * face_x + 2 * face_y,
        2 * face_x + 2 * face_y + face_z,
    ]
    kinds = jnp.arange(NSPEC, dtype=jnp.int32)

    def lookup(codes, table):
        onehot = (codes[:, None] == kinds[None, :]).astype(jnp.float32)
        return jnp.dot(onehot, table, precision=lax.Precision.HIGHEST)

    def project(rows, codes, weight, table):
        return (
            jnp.dot(rows, weight, preferred_element_type=jnp.float32) + lookup(codes, table)
        ).astype(jnp.bfloat16)

    def spread(onehot, values):
        high = values.astype(jnp.bfloat16)
        low = (values - high.astype(jnp.float32)).astype(jnp.bfloat16)
        return jnp.einsum(
            "nr,nw->rw", onehot, high, preferred_element_type=jnp.float32
        ) + jnp.einsum("nr,nw->rw", onehot, low, preferred_element_type=jnp.float32)

    proj_c = project(latent, species, centre_proj, centre_table)
    proj_n = project(latent, species, neigh_proj, neigh_table)
    send_rows = send_list[0]
    coarse = positions // 16
    fine = positions - coarse * 16
    coord_cols = jnp.concatenate([coarse, fine], axis=0).T.astype(jnp.bfloat16)
    table = jnp.concatenate(
        [proj_n, coord_cols, jnp.zeros((atoms, extra - 6), jnp.bfloat16)], axis=1
    )
    shifts = [(0, -LX_FIX), (0, LX_FIX), (1, -LY_FIX), (1, LY_FIX), (2, -LZ_FIX), (2, LZ_FIX)]
    sections = (("gx", (1, 0)), ("gy", (3, 2)), ("gz", (5, 4)))
    pickers = {}
    base_rows = []
    for section, (axis, segs) in enumerate(sections):
        rows_now = table.shape[0]
        base_rows.append(rows_now)
        parts = [table]
        for number, (segment, direction) in enumerate(((segs[0], 1), (segs[1], -1))):
            picked = send_rows[starts[segment] : starts[segment] + lengths[segment]]
            onehot = (
                picked[:, None] == jnp.arange(rows_now, dtype=jnp.int32)[None, :]
            ).astype(jnp.bfloat16)
            pickers[segment] = onehot
            out = jnp.dot(onehot, table, preferred_element_type=jnp.float32).astype(jnp.bfloat16)
            got = passed_along(out, axis, direction)
            coord_axis, offset = shifts[2 * section + number]
            columns = jnp.arange(width + extra, dtype=jnp.int32)[None, :]
            shift = jnp.where(columns == width + coord_axis, offset // 16, 0).astype(jnp.bfloat16)
            parts.append(got + shift)
        table = jnp.concatenate(parts, axis=0)
    total_rows = table.shape[0]
    neighbour = neighbour.reshape(atoms, K).T.reshape(-1)
    select = (neighbour[:, None] == jnp.arange(total_rows, dtype=jnp.int32)[None, :]).astype(
        jnp.bfloat16
    )
    neigh_rows = jnp.dot(select, table[:, :width], preferred_element_type=jnp.float32).astype(
        jnp.bfloat16
    )
    gathered = jnp.dot(select, table[:, width:], preferred_element_type=jnp.float32)
    coords_n = (gathered[:, 0:3] * 16.0 + gathered[:, 3:6]).T
    delta = (coords_n.reshape(3, K, atoms) - positions.astype(jnp.float32)[:, None, :]) * (
        1.0 / 64.0
    )
    live = (jnp.arange(atoms) < atom_count[0]).astype(jnp.float32)
    valid_pair = live[None, :]

    geo, geo_pull = jax.vjp(lambda d: geometry(d, valid_pair), delta)
    grad_neigh, grad_centre, grad_geo, atom_energy = pair_terms(
        neigh_rows,
        proj_c.astype(jnp.float32),
        geo,
        basis_proj,
        split_proj,
        update_proj,
        tensor_proj,
        energy_proj,
    )
    (grad_delta,) = geo_pull(grad_geo)
    pairs = grad_neigh.shape[0]
    grads = jnp.concatenate(
        [
            grad_neigh,
            grad_delta.reshape(3, pairs).T,
            jnp.zeros((pairs, extra - 3), jnp.float32),
        ],
        axis=1,
    )
    sums = spread(select, grads)
    own_pos = grad_delta.sum(axis=1)
    sums = sums - jnp.pad(own_pos.T, ((0, total_rows - atoms), (width, extra - 3)))
    for section in (2, 1, 0):
        axis, segs = sections[section]
        rows_now = base_rows[section]
        first = atoms + starts[2 * section]
        second = atoms + starts[2 * section + 1]
        back_first = passed_along(sums[first : first + lengths[2 * section]], axis, -1)
        back_second = passed_along(sums[second : second + lengths[2 * section + 1]], axis, 1)
        sums = (
            sums[:rows_now]
            + spread(pickers[segs[0]], back_first)
            + spread(pickers[segs[1]], back_second)
        )
    back_neigh = neigh_proj.astype(jnp.float32).T
    back_centre = centre_proj.astype(jnp.float32).T
    latent_grad = jnp.dot(grad_centre, back_centre, precision=lax.Precision.HIGHEST)
    latent_grad = latent_grad + jnp.dot(
        sums[:, :width], back_neigh, precision=lax.Precision.HIGHEST
    )
    forces = -sums[:, width : width + 3].T
    energies = live * (lookup(species, species_shift[:, None])[:, 0] + atom_energy)
    return (energies, forces, latent_grad)


def solution(mesh):
    in_specs = (
        P(("gx", "gy", "gz"), None),
        P(None, ("gx", "gy", "gz")),
        P(("gx", "gy", "gz")),
        P(("gx", "gy", "gz"), None),
        P(("gx", "gy", "gz")),
        P(("gx", "gy", "gz")),
        P(),
        P(),
        P(),
        P(),
        P(),
        P(),
        P(),
        P(),
        P(),
        P(),
    )
    out_specs = (P(("gx", "gy", "gz")), P(None, ("gx", "gy", "gz")), P(("gx", "gy", "gz"), None))
    return jax.shard_map(shards, mesh=mesh, in_specs=in_specs, out_specs=out_specs, check_vma=False)
```

```python
import math

import jax
import jax.numpy as jnp
from jax import lax
from jax.experimental import pallas as pl
from jax.experimental.pallas import tpu as pltpu
from jax.sharding import PartitionSpec as P

K = 8
CH = 64
NB = 8
NSPEC = 5
LX_FIX = 1024
LY_FIX = 512
LZ_FIX = 1280


CUTOFF = 6.0
SOFTEN = 0.25


def shortened(shard):
    return jax.tree.map(lambda a: a.astype(jnp.bfloat16) if a.dtype == jnp.float32 else a, shard)


def passed_along(block, axis, distance):
    devices = range(lax.axis_size(axis))
    route = [((i - distance) % len(devices), i) for i in devices]
    return lax.ppermute(block, axis, route)


def by_order(values):
    rest = values.shape[1:]
    return jnp.concatenate(
        [
            values[0:1],
            jnp.broadcast_to(values[1:2], (3,) + rest),
            jnp.broadcast_to(values[2:3], (5,) + rest),
        ],
        axis=0,
    )


ORDER_OF = (0, 1, 1, 1, 2, 2, 2, 2, 2)
GROUPS = ((0,), (1, 2, 3), (4, 5, 6, 7, 8))


def geometry(delta, valid_pair):
    atoms = delta.shape[2]
    radius = jnp.sqrt(jnp.sum(delta * delta, axis=0) + SOFTEN)
    unit = delta / radius
    ratio = radius / CUTOFF
    envelope = jnp.where(ratio < 1.0, (1.0 - ratio * ratio) ** 2, 0.0) * valid_pair
    orders = jnp.arange(1, NB + 1).astype(jnp.float32)
    basis = (
        jnp.sin(orders[:, None, None] * (math.pi / CUTOFF) * radius[None])
        * (envelope / radius)[None]
    )
    ux, uy, uz = unit[0], unit[1], unit[2]
    r3 = math.sqrt(3.0)
    r15 = math.sqrt(15.0)
    r5 = math.sqrt(5.0)
    harmonics = jnp.stack(
        [
            jnp.ones_like(ux),
            r3 * ux,
            r3 * uy,
            r3 * uz,
            r15 * ux * uy,
            r15 * uy * uz,
            0.5 * r5 * (2.0 * uz * uz - ux * ux - uy * uy),
            r15 * ux * uz,
            0.5 * r15 * (ux * ux - uy * uy),
        ],
        axis=0,
    )
    rows = jnp.concatenate([basis, envelope[None], harmonics], axis=0).reshape(18, K * atoms)
    return jnp.concatenate([rows, jnp.zeros((128 - 18, K * atoms), jnp.float32)], axis=0)


def _mm(a, b):
    return jnp.dot(a, b, preferred_element_type=jnp.float32)


def _sigmoid(v):
    return 1.0 / (1.0 + jnp.exp(-v))


def _pair_kernel(
    rows_ref, centre_ref, geo_ref, basis_t_ref, split_t_ref, split_ref, update_t_ref,
    update_ref, tensor_t_ref, tensor_ref, basis_ref, energy_w_ref,
    grad_rows_ref, grad_centre_ref, grad_geo_ref, energy_ref,
    pre_s, hidden_s, mixed_s, damp_s, dlow_s, dgeo_s, env_s, denv_s,
):
    atoms = centre_ref.shape[1]
    f32 = jnp.float32
    bf16 = jnp.bfloat16
    sub = lax.broadcasted_iota(jnp.int32, (128, atoms), 0)
    inv_root = 1.0 / math.sqrt(K)
    env_s[...] = jnp.zeros_like(env_s)
    denv_s[...] = jnp.zeros_like(denv_s)

    def block(k):
        return pl.ds(pl.multiple_of(k * atoms, atoms), atoms)

    def split_mm(weight, values):
        high = values.astype(bf16)
        low = (values - high.astype(f32)).astype(bf16)
        return _mm(weight, high) + _mm(weight, low)

    def first(k, carry):
        at = block(k)
        geo = geo_ref[:, at]
        radial = split_mm(basis_t_ref[...], geo)
        pre = centre_ref[...] + rows_ref[:, at].astype(f32) + radial
        envelope = geo[8:9, :]
        hidden = pre * _sigmoid(pre) * envelope
        pre_s[:, at] = pre
        hidden_s[:, at] = hidden
        mixed = _mm(split_t_ref[...], hidden.astype(bf16))
        mixed_s[:, at] = mixed
        for m in range(9):
            l = ORDER_OF[m]
            weight = mixed[3 * CH + l * CH : 3 * CH + (l + 1) * CH, :]
            env_s[m] = env_s[m] + weight * (geo[9 + m : 10 + m, :] * inv_root)
        return carry

    lax.fori_loop(0, K, first, 0)

    def second(k, energy):
        at = block(k)
        geo = geo_ref[:, at]
        envelope = geo[8:9, :]
        hidden = hidden_s[:, at]
        mixed = mixed_s[:, at]
        parts = []
        totals = []
        for l in range(3):
            total = 0.0
            for m in GROUPS[l]:
                total = total + geo[9 + m : 10 + m, :] * env_s[m]
            totals.append(total)
            parts.append(mixed[l * CH : (l + 1) * CH, :] * total)
        scalars = jnp.concatenate(parts, axis=0).astype(bf16)
        z = _mm(update_t_ref[...], hidden.astype(bf16)) + _mm(tensor_t_ref[...], scalars)
        gate = _sigmoid(z)
        update = z * gate
        readout = jnp.sum((hidden + update) * energy_w_ref[...], axis=0, keepdims=True)
        energy = energy + envelope * readout
        dz = (envelope * energy_w_ref[...]) * (gate * (1.0 + z * (1.0 - gate)))
        dz_low = dz.astype(bf16)
        dscalars = _mm(tensor_ref[...], dz_low).astype(bf16).astype(f32)
        dlow_s[:, at] = _mm(update_ref[...], dz_low)
        dgeo = jnp.where(sub == 8, readout, 0.0)
        for l in range(3):
            ds = dscalars[l * CH : (l + 1) * CH, :]
            damp_s[l * CH : (l + 1) * CH, at] = ds * totals[l]
            dtotal = ds * mixed[l * CH : (l + 1) * CH, :]
            for m in GROUPS[l]:
                dgeo = dgeo + jnp.where(
                    sub == 9 + m, jnp.sum(dtotal * env_s[m], axis=0, keepdims=True), 0.0
                )
                denv_s[m] = denv_s[m] + dtotal * geo[9 + m : 10 + m, :]
        dgeo_s[:, at] = dgeo
        return energy

    energy = lax.fori_loop(0, K, second, jnp.zeros((1, atoms), f32))
    energy_ref[...] = jnp.broadcast_to(energy, energy_ref.shape)

    def third(k, centre_grad):
        at = block(k)
        geo = geo_ref[:, at]
        envelope = geo[8:9, :]
        mixed = mixed_s[:, at]
        dgeo = dgeo_s[:, at]
        dweights = []
        for l in range(3):
            weight = mixed[3 * CH + l * CH : 3 * CH + (l + 1) * CH, :]
            dweight = 0.0
            for m in GROUPS[l]:
                dweight = dweight + denv_s[m] * (geo[9 + m : 10 + m, :] * inv_root)
                dgeo = dgeo + jnp.where(
                    sub == 9 + m,
                    jnp.sum(denv_s[m] * weight, axis=0, keepdims=True) * inv_root,
                    0.0,
                )
            dweights.append(dweight)
        dmixed = jnp.concatenate([damp_s[:, at]] + dweights, axis=0).astype(bf16)
        dlow = dlow_s[:, at] + _mm(split_ref[...], dmixed)
        dhidden = envelope * energy_w_ref[...] + dlow
        pre = pre_s[:, at]
        sig = _sigmoid(pre)
        act = pre * sig
        dgeo = dgeo + jnp.where(sub == 8, jnp.sum(dhidden * act, axis=0, keepdims=True), 0.0)
        dpre = dhidden * envelope * (sig * (1.0 + pre * (1.0 - sig)))
        grad_rows_ref[:, at] = dpre
        dgeo = dgeo + split_mm(basis_ref[...], dpre)
        grad_geo_ref[:, at] = dgeo
        return centre_grad + dpre

    grad_centre_ref[...] = lax.fori_loop(0, K, third, jnp.zeros(grad_centre_ref.shape, f32))


def pair_terms(rows_t, centre_t, geo, basis_proj, split_proj, update_proj, tensor_proj, energy_proj):
    width, pairs = rows_t.shape
    atoms = centre_t.shape[1]
    f32 = jnp.float32
    bf16 = jnp.bfloat16
    basis_pad = jnp.concatenate([basis_proj, jnp.zeros((128 - NB, width), bf16)], axis=0)
    vmem = pl.BlockSpec(memory_space=pltpu.VMEM)
    outs = pl.pallas_call(
        _pair_kernel,
        out_shape=(
            jax.ShapeDtypeStruct((width, pairs), f32),
            jax.ShapeDtypeStruct((width, atoms), f32),
            jax.ShapeDtypeStruct((128, pairs), f32),
            jax.ShapeDtypeStruct((8, atoms), f32),
        ),
        in_specs=[vmem] * 12,
        out_specs=(vmem, vmem, vmem, vmem),
        scratch_shapes=[
            pltpu.VMEM((width, pairs), f32),
            pltpu.VMEM((width, pairs), f32),
            pltpu.VMEM((6 * CH, pairs), f32),
            pltpu.VMEM((3 * CH, pairs), f32),
            pltpu.VMEM((width, pairs), f32),
            pltpu.VMEM((128, pairs), f32),
            pltpu.VMEM((9, CH, atoms), f32),
            pltpu.VMEM((9, CH, atoms), f32),
        ],
        compiler_params=pltpu.CompilerParams(vmem_limit_bytes=60 * 1024 * 1024),
        cost_estimate=pl.CostEstimate(
            flops=int(24 * pairs * width * 128),
            transcendentals=int(3 * pairs * width),
            bytes_accessed=int(16 * pairs * width),
        ),
    )(
        rows_t,
        centre_t,
        geo,
        basis_pad.T,
        split_proj.T,
        split_proj,
        update_proj.T,
        update_proj,
        tensor_proj.T,
        tensor_proj,
        basis_pad,
        jnp.broadcast_to(energy_proj.astype(f32)[:, None], (width, atoms)),
    )
    grad_rows_t, grad_centre_t, grad_geo, energy = outs
    return grad_rows_t, grad_centre_t, grad_geo, energy[0]


def shards(
    latent,
    positions,
    species,
    send_list,
    neighbour,
    atom_count,
    centre_proj,
    neigh_proj,
    centre_table,
    neigh_table,
    basis_proj,
    split_proj,
    update_proj,
    tensor_proj,
    energy_proj,
    species_shift,
):
    atoms, width = latent.shape
    extra = 128
    face_x = atoms // 8
    face_y = atoms // 2
    face_z = atoms // 8
    lengths = [face_x, face_x, face_y, face_y, face_z, face_z]
    starts = [
        0,
        face_x,
        2 * face_x,
        2 * face_x + face_y,
        2 * face_x + 2 * face_y,
        2 * face_x + 2 * face_y + face_z,
    ]
    kinds = jnp.arange(NSPEC, dtype=jnp.int32)

    def lookup(codes, table):
        onehot = (codes[:, None] == kinds[None, :]).astype(jnp.float32)
        return jnp.dot(onehot, table, precision=lax.Precision.HIGHEST)

    def project(rows, codes, weight, table):
        return (
            jnp.dot(rows, weight, preferred_element_type=jnp.float32) + lookup(codes, table)
        ).astype(jnp.bfloat16)

    def spread_cols(onehot, values):
        high = values.astype(jnp.bfloat16)
        low = (values - high.astype(jnp.float32)).astype(jnp.bfloat16)
        return jnp.einsum(
            "wn,nr->wr", high, onehot, preferred_element_type=jnp.float32
        ) + jnp.einsum("wn,nr->wr", low, onehot, preferred_element_type=jnp.float32)

    def spread(onehot, values):
        high = values.astype(jnp.bfloat16)
        low = (values - high.astype(jnp.float32)).astype(jnp.bfloat16)
        return jnp.einsum(
            "nr,nw->rw", onehot, high, preferred_element_type=jnp.float32
        ) + jnp.einsum("nr,nw->rw", onehot, low, preferred_element_type=jnp.float32)

    proj_c = project(latent, species, centre_proj, centre_table)
    proj_n = project(latent, species, neigh_proj, neigh_table)
    send_rows = send_list[0]
    coarse = positions // 16
    fine = positions - coarse * 16
    coord_cols = jnp.concatenate([coarse, fine], axis=0).T.astype(jnp.bfloat16)
    table = jnp.concatenate(
        [proj_n, coord_cols, jnp.zeros((atoms, extra - 6), jnp.bfloat16)], axis=1
    )
    shifts = [(0, -LX_FIX), (0, LX_FIX), (1, -LY_FIX), (1, LY_FIX), (2, -LZ_FIX), (2, LZ_FIX)]
    sections = (("gx", (1, 0)), ("gy", (3, 2)), ("gz", (5, 4)))
    pickers = {}
    base_rows = []
    for section, (axis, segs) in enumerate(sections):
        rows_now = table.shape[0]
        base_rows.append(rows_now)
        parts = [table]
        for number, (segment, direction) in enumerate(((segs[0], 1), (segs[1], -1))):
            picked = send_rows[starts[segment] : starts[segment] + lengths[segment]]
            onehot = (
                picked[:, None] == jnp.arange(rows_now, dtype=jnp.int32)[None, :]
            ).astype(jnp.bfloat16)
            pickers[segment] = onehot
            out = jnp.dot(onehot, table, preferred_element_type=jnp.float32).astype(jnp.bfloat16)
            got = passed_along(out, axis, direction)
            coord_axis, offset = shifts[2 * section + number]
            columns = jnp.arange(width + extra, dtype=jnp.int32)[None, :]
            shift = jnp.where(columns == width + coord_axis, offset // 16, 0).astype(jnp.bfloat16)
            parts.append(got + shift)
        table = jnp.concatenate(parts, axis=0)
    total_rows = table.shape[0]
    neighbour = neighbour.reshape(atoms, K).T.reshape(-1)
    select = (neighbour[:, None] == jnp.arange(total_rows, dtype=jnp.int32)[None, :]).astype(
        jnp.bfloat16
    )
    gathered = jnp.einsum("tw,pt->wp", table, select, preferred_element_type=jnp.float32)
    neigh_cols = gathered[:width].astype(jnp.bfloat16)
    coords_n = gathered[width : width + 3] * 16.0 + gathered[width + 3 : width + 6]
    delta = (coords_n.reshape(3, K, atoms) - positions.astype(jnp.float32)[:, None, :]) * (
        1.0 / 64.0
    )
    live = (jnp.arange(atoms) < atom_count[0]).astype(jnp.float32)
    valid_pair = live[None, :]

    geo, geo_pull = jax.vjp(lambda d: geometry(d, valid_pair), delta)
    grad_neigh, grad_centre, grad_geo, atom_energy = pair_terms(
        neigh_cols,
        proj_c.astype(jnp.float32).T,
        geo,
        basis_proj,
        split_proj,
        update_proj,
        tensor_proj,
        energy_proj,
    )
    (grad_delta,) = geo_pull(grad_geo)
    pairs = grad_neigh.shape[1]
    grads = jnp.concatenate(
        [
            grad_neigh,
            grad_delta.reshape(3, pairs),
            jnp.zeros((extra - 3, pairs), jnp.float32),
        ],
        axis=0,
    )
    sums = spread_cols(select, grads).T
    own_pos = grad_delta.sum(axis=1)
    sums = sums - jnp.pad(own_pos.T, ((0, total_rows - atoms), (width, extra - 3)))
    for section in (2, 1, 0):
        axis, segs = sections[section]
        rows_now = base_rows[section]
        first = atoms + starts[2 * section]
        second = atoms + starts[2 * section + 1]
        back_first = passed_along(sums[first : first + lengths[2 * section]], axis, -1)
        back_second = passed_along(sums[second : second + lengths[2 * section + 1]], axis, 1)
        sums = (
            sums[:rows_now]
            + spread(pickers[segs[0]], back_first)
            + spread(pickers[segs[1]], back_second)
        )
    back_neigh = neigh_proj.astype(jnp.float32).T
    back_centre = centre_proj.astype(jnp.float32).T
    latent_grad = jnp.dot(grad_centre.T, back_centre, precision=lax.Precision.HIGHEST)
    latent_grad = latent_grad + jnp.dot(
        sums[:, :width], back_neigh, precision=lax.Precision.HIGHEST
    )
    forces = -sums[:, width : width + 3].T
    energies = live * (lookup(species, species_shift[:, None])[:, 0] + atom_energy)
    return (energies, forces, latent_grad)


def solution(mesh):
    in_specs = (
        P(("gx", "gy", "gz"), None),
        P(None, ("gx", "gy", "gz")),
        P(("gx", "gy", "gz")),
        P(("gx", "gy", "gz"), None),
        P(("gx", "gy", "gz")),
        P(("gx", "gy", "gz")),
        P(),
        P(),
        P(),
        P(),
        P(),
        P(),
        P(),
        P(),
        P(),
        P(),
    )
    out_specs = (P(("gx", "gy", "gz")), P(None, ("gx", "gy", "gz")), P(("gx", "gy", "gz"), None))
    return jax.shard_map(shards, mesh=mesh, in_specs=in_specs, out_specs=out_specs, check_vma=False)
```

```python
import math

import jax
import jax.numpy as jnp
from jax import lax
from jax.experimental import pallas as pl
from jax.experimental.pallas import tpu as pltpu
from jax.sharding import PartitionSpec as P

K = 8
CH = 64
NB = 8
NSPEC = 5
LX_FIX = 1024
LY_FIX = 512
LZ_FIX = 1280


CUTOFF = 6.0
SOFTEN = 0.25


def shortened(shard):
    return jax.tree.map(lambda a: a.astype(jnp.bfloat16) if a.dtype == jnp.float32 else a, shard)


def passed_along(block, axis, distance):
    devices = range(lax.axis_size(axis))
    route = [((i - distance) % len(devices), i) for i in devices]
    return lax.ppermute(block, axis, route)


def by_order(values):
    rest = values.shape[1:]
    return jnp.concatenate(
        [
            values[0:1],
            jnp.broadcast_to(values[1:2], (3,) + rest),
            jnp.broadcast_to(values[2:3], (5,) + rest),
        ],
        axis=0,
    )


ORDER_OF = (0, 1, 1, 1, 2, 2, 2, 2, 2)
GROUPS = ((0,), (1, 2, 3), (4, 5, 6, 7, 8))


def geometry(delta, valid_pair):
    atoms = delta.shape[2]
    radius = jnp.sqrt(jnp.sum(delta * delta, axis=0) + SOFTEN)
    unit = delta / radius
    ratio = radius / CUTOFF
    envelope = jnp.where(ratio < 1.0, (1.0 - ratio * ratio) ** 2, 0.0) * valid_pair
    orders = jnp.arange(1, NB + 1).astype(jnp.float32)
    basis = (
        jnp.sin(orders[:, None, None] * (math.pi / CUTOFF) * radius[None])
        * (envelope / radius)[None]
    )
    ux, uy, uz = unit[0], unit[1], unit[2]
    r3 = math.sqrt(3.0)
    r15 = math.sqrt(15.0)
    r5 = math.sqrt(5.0)
    harmonics = jnp.stack(
        [
            jnp.ones_like(ux),
            r3 * ux,
            r3 * uy,
            r3 * uz,
            r15 * ux * uy,
            r15 * uy * uz,
            0.5 * r5 * (2.0 * uz * uz - ux * ux - uy * uy),
            r15 * ux * uz,
            0.5 * r15 * (ux * ux - uy * uy),
        ],
        axis=0,
    )
    rows = jnp.concatenate([basis, envelope[None], harmonics], axis=0).reshape(18, K * atoms)
    return jnp.concatenate([rows, jnp.zeros((128 - 18, K * atoms), jnp.float32)], axis=0)


def _mm(a, b):
    return jnp.dot(a, b, preferred_element_type=jnp.float32)


def _sigmoid(v):
    return 0.5 + 0.5 * jnp.tanh(0.5 * v)


def _pair_kernel(
    rows_ref, centre_ref, geo_ref, basis_t_ref, split_t_ref, split_ref, update_t_ref,
    update_ref, tensor_t_ref, tensor_ref, basis_ref, energy_w_ref,
    grad_rows_ref, grad_centre_ref, grad_geo_ref, energy_ref,
    pre_s, hidden_s, mixed_s, damp_s, dlow_s, dgeo_s, env_s, denv_s,
):
    atoms = centre_ref.shape[1]
    f32 = jnp.float32
    bf16 = jnp.bfloat16
    span = 2 * atoms
    sub = lax.broadcasted_iota(jnp.int32, (128, span), 0)
    inv_root = 1.0 / math.sqrt(K)
    env_s[...] = jnp.zeros_like(env_s)
    denv_s[...] = jnp.zeros_like(denv_s)

    def block(k):
        return pl.ds(pl.multiple_of(k * span, span), span)

    def twice(v):
        return jnp.concatenate([v, v], axis=1)

    def fold(v):
        return v[:, :atoms] + v[:, atoms:]

    def split_mm(weight, values):
        high = values.astype(bf16)
        low = (values - high.astype(f32)).astype(bf16)
        return _mm(weight, high) + _mm(weight, low)

    def first(k, carry):
        at = block(k)
        geo = geo_ref[:, at]
        radial = split_mm(basis_t_ref[...], geo)
        pre = twice(centre_ref[...]) + rows_ref[:, at].astype(f32) + radial
        envelope = geo[8:9, :]
        hidden = pre * _sigmoid(pre) * envelope
        pre_s[:, at] = pre
        hidden_s[:, at] = hidden
        mixed = _mm(split_t_ref[...], hidden.astype(bf16))
        mixed_s[:, at] = mixed
        for m in range(9):
            l = ORDER_OF[m]
            weight = mixed[3 * CH + l * CH : 3 * CH + (l + 1) * CH, :]
            env_s[m] = env_s[m] + fold(weight * (geo[9 + m : 10 + m, :] * inv_root))
        return carry

    lax.fori_loop(0, K // 2, first, 0)

    def second(k, energy):
        at = block(k)
        geo = geo_ref[:, at]
        envelope = geo[8:9, :]
        hidden = hidden_s[:, at]
        mixed = mixed_s[:, at]
        parts = []
        totals = []
        for l in range(3):
            total = 0.0
            for m in GROUPS[l]:
                total = total + geo[9 + m : 10 + m, :] * twice(env_s[m])
            totals.append(total)
            parts.append(mixed[l * CH : (l + 1) * CH, :] * total)
        scalars = jnp.concatenate(parts, axis=0).astype(bf16)
        z = _mm(update_t_ref[...], hidden.astype(bf16)) + _mm(tensor_t_ref[...], scalars)
        gate = _sigmoid(z)
        update = z * gate
        readout = jnp.sum((hidden + update) * energy_w_ref[...], axis=0, keepdims=True)
        energy = energy + envelope * readout
        dz = (envelope * energy_w_ref[...]) * (gate * (1.0 + z * (1.0 - gate)))
        dz_low = dz.astype(bf16)
        dscalars = _mm(tensor_ref[...], dz_low).astype(bf16).astype(f32)
        dlow_s[:, at] = _mm(update_ref[...], dz_low)
        dgeo = jnp.where(sub == 8, readout, 0.0)
        for l in range(3):
            ds = dscalars[l * CH : (l + 1) * CH, :]
            damp_s[l * CH : (l + 1) * CH, at] = ds * totals[l]
            dtotal = ds * mixed[l * CH : (l + 1) * CH, :]
            for m in GROUPS[l]:
                dgeo = dgeo + jnp.where(
                    sub == 9 + m, jnp.sum(dtotal * twice(env_s[m]), axis=0, keepdims=True), 0.0
                )
                denv_s[m] = denv_s[m] + fold(dtotal * geo[9 + m : 10 + m, :])
        dgeo_s[:, at] = dgeo
        return energy

    energy = lax.fori_loop(0, K // 2, second, jnp.zeros((1, span), f32))
    energy_ref[...] = jnp.broadcast_to(fold(energy), energy_ref.shape)

    def third(k, centre_grad):
        at = block(k)
        geo = geo_ref[:, at]
        envelope = geo[8:9, :]
        mixed = mixed_s[:, at]
        dgeo = dgeo_s[:, at]
        dweights = []
        for l in range(3):
            weight = mixed[3 * CH + l * CH : 3 * CH + (l + 1) * CH, :]
            dweight = 0.0
            for m in GROUPS[l]:
                denv = twice(denv_s[m])
                dweight = dweight + denv * (geo[9 + m : 10 + m, :] * inv_root)
                dgeo = dgeo + jnp.where(
                    sub == 9 + m,
                    jnp.sum(denv * weight, axis=0, keepdims=True) * inv_root,
                    0.0,
                )
            dweights.append(dweight)
        dmixed = jnp.concatenate([damp_s[:, at]] + dweights, axis=0).astype(bf16)
        dlow = dlow_s[:, at] + _mm(split_ref[...], dmixed)
        dhidden = envelope * energy_w_ref[...] + dlow
        pre = pre_s[:, at]
        sig = _sigmoid(pre)
        act = pre * sig
        dgeo = dgeo + jnp.where(sub == 8, jnp.sum(dhidden * act, axis=0, keepdims=True), 0.0)
        dpre = dhidden * envelope * (sig * (1.0 + pre * (1.0 - sig)))
        grad_rows_ref[:, at] = dpre
        dgeo = dgeo + split_mm(basis_ref[...], dpre)
        grad_geo_ref[:, at] = dgeo
        return centre_grad + fold(dpre)

    grad_centre_ref[...] = lax.fori_loop(
        0, K // 2, third, jnp.zeros(grad_centre_ref.shape, f32)
    )


def pair_terms(rows_t, centre_t, geo, basis_proj, split_proj, update_proj, tensor_proj, energy_proj):
    width, pairs = rows_t.shape
    atoms = centre_t.shape[1]
    f32 = jnp.float32
    bf16 = jnp.bfloat16
    basis_pad = jnp.concatenate([basis_proj, jnp.zeros((128 - NB, width), bf16)], axis=0)
    vmem = pl.BlockSpec(memory_space=pltpu.VMEM)
    outs = pl.pallas_call(
        _pair_kernel,
        out_shape=(
            jax.ShapeDtypeStruct((width, pairs), f32),
            jax.ShapeDtypeStruct((width, atoms), f32),
            jax.ShapeDtypeStruct((128, pairs), f32),
            jax.ShapeDtypeStruct((8, atoms), f32),
        ),
        in_specs=[vmem] * 12,
        out_specs=(vmem, vmem, vmem, vmem),
        scratch_shapes=[
            pltpu.VMEM((width, pairs), f32),
            pltpu.VMEM((width, pairs), f32),
            pltpu.VMEM((6 * CH, pairs), f32),
            pltpu.VMEM((3 * CH, pairs), f32),
            pltpu.VMEM((width, pairs), f32),
            pltpu.VMEM((128, pairs), f32),
            pltpu.VMEM((9, CH, atoms), f32),
            pltpu.VMEM((9, CH, atoms), f32),
        ],
        compiler_params=pltpu.CompilerParams(vmem_limit_bytes=60 * 1024 * 1024),
        cost_estimate=pl.CostEstimate(
            flops=int(24 * pairs * width * 128),
            transcendentals=int(3 * pairs * width),
            bytes_accessed=int(16 * pairs * width),
        ),
    )(
        rows_t,
        centre_t,
        geo,
        basis_pad.T,
        split_proj.T,
        split_proj,
        update_proj.T,
        update_proj,
        tensor_proj.T,
        tensor_proj,
        basis_pad,
        jnp.broadcast_to(energy_proj.astype(f32)[:, None], (width, 2 * atoms)),
    )
    grad_rows_t, grad_centre_t, grad_geo, energy = outs
    return grad_rows_t, grad_centre_t, grad_geo, energy[0]


def shards(
    latent,
    positions,
    species,
    send_list,
    neighbour,
    atom_count,
    centre_proj,
    neigh_proj,
    centre_table,
    neigh_table,
    basis_proj,
    split_proj,
    update_proj,
    tensor_proj,
    energy_proj,
    species_shift,
):
    atoms, width = latent.shape
    extra = 128
    face_x = atoms // 8
    face_y = atoms // 2
    face_z = atoms // 8
    lengths = [face_x, face_x, face_y, face_y, face_z, face_z]
    starts = [
        0,
        face_x,
        2 * face_x,
        2 * face_x + face_y,
        2 * face_x + 2 * face_y,
        2 * face_x + 2 * face_y + face_z,
    ]
    kinds = jnp.arange(NSPEC, dtype=jnp.int32)

    def lookup(codes, table):
        onehot = (codes[:, None] == kinds[None, :]).astype(jnp.float32)
        return jnp.dot(onehot, table, precision=lax.Precision.HIGHEST)

    def project(rows, codes, weight, table):
        return (
            jnp.dot(rows, weight, preferred_element_type=jnp.float32) + lookup(codes, table)
        ).astype(jnp.bfloat16)

    def spread_cols(onehot, values):
        high = values.astype(jnp.bfloat16)
        low = (values - high.astype(jnp.float32)).astype(jnp.bfloat16)
        return jnp.einsum(
            "wn,nr->wr", high, onehot, preferred_element_type=jnp.float32
        ) + jnp.einsum("wn,nr->wr", low, onehot, preferred_element_type=jnp.float32)

    def spread(onehot, values):
        high = values.astype(jnp.bfloat16)
        low = (values - high.astype(jnp.float32)).astype(jnp.bfloat16)
        return jnp.einsum(
            "nr,nw->rw", onehot, high, preferred_element_type=jnp.float32
        ) + jnp.einsum("nr,nw->rw", onehot, low, preferred_element_type=jnp.float32)

    proj_c = project(latent, species, centre_proj, centre_table)
    proj_n = project(latent, species, neigh_proj, neigh_table)
    send_rows = send_list[0]
    coarse = positions // 16
    fine = positions - coarse * 16
    coord_cols = jnp.concatenate([coarse, fine], axis=0).T.astype(jnp.bfloat16)
    table = jnp.concatenate(
        [proj_n, coord_cols, jnp.zeros((atoms, extra - 6), jnp.bfloat16)], axis=1
    )
    shifts = [(0, -LX_FIX), (0, LX_FIX), (1, -LY_FIX), (1, LY_FIX), (2, -LZ_FIX), (2, LZ_FIX)]
    sections = (("gx", (1, 0)), ("gy", (3, 2)), ("gz", (5, 4)))
    pickers = {}
    base_rows = []
    for section, (axis, segs) in enumerate(sections):
        rows_now = table.shape[0]
        base_rows.append(rows_now)
        parts = [table]
        for number, (segment, direction) in enumerate(((segs[0], 1), (segs[1], -1))):
            picked = send_rows[starts[segment] : starts[segment] + lengths[segment]]
            onehot = (
                picked[:, None] == jnp.arange(rows_now, dtype=jnp.int32)[None, :]
            ).astype(jnp.bfloat16)
            pickers[segment] = onehot
            out = jnp.dot(onehot, table, preferred_element_type=jnp.float32).astype(jnp.bfloat16)
            got = passed_along(out, axis, direction)
            coord_axis, offset = shifts[2 * section + number]
            columns = jnp.arange(width + extra, dtype=jnp.int32)[None, :]
            shift = jnp.where(columns == width + coord_axis, offset // 16, 0).astype(jnp.bfloat16)
            parts.append(got + shift)
        table = jnp.concatenate(parts, axis=0)
    total_rows = table.shape[0]
    neighbour = neighbour.reshape(atoms, K).T.reshape(-1)
    select = (neighbour[:, None] == jnp.arange(total_rows, dtype=jnp.int32)[None, :]).astype(
        jnp.bfloat16
    )
    gathered = jnp.einsum("tw,pt->wp", table, select, preferred_element_type=jnp.float32)
    neigh_cols = gathered[:width].astype(jnp.bfloat16)
    coords_n = gathered[width : width + 3] * 16.0 + gathered[width + 3 : width + 6]
    delta = (coords_n.reshape(3, K, atoms) - positions.astype(jnp.float32)[:, None, :]) * (
        1.0 / 64.0
    )
    live = (jnp.arange(atoms) < atom_count[0]).astype(jnp.float32)
    valid_pair = live[None, :]

    geo, geo_pull = jax.vjp(lambda d: geometry(d, valid_pair), delta)
    grad_neigh, grad_centre, grad_geo, atom_energy = pair_terms(
        neigh_cols,
        proj_c.astype(jnp.float32).T,
        geo,
        basis_proj,
        split_proj,
        update_proj,
        tensor_proj,
        energy_proj,
    )
    (grad_delta,) = geo_pull(grad_geo)
    pairs = grad_neigh.shape[1]
    grads = jnp.concatenate(
        [
            grad_neigh,
            grad_delta.reshape(3, pairs),
            jnp.zeros((extra - 3, pairs), jnp.float32),
        ],
        axis=0,
    )
    sums = spread_cols(select, grads).T
    own_pos = grad_delta.sum(axis=1)
    sums = sums - jnp.pad(own_pos.T, ((0, total_rows - atoms), (width, extra - 3)))
    for section in (2, 1, 0):
        axis, segs = sections[section]
        rows_now = base_rows[section]
        first = atoms + starts[2 * section]
        second = atoms + starts[2 * section + 1]
        back_first = passed_along(sums[first : first + lengths[2 * section]], axis, -1)
        back_second = passed_along(sums[second : second + lengths[2 * section + 1]], axis, 1)
        sums = (
            sums[:rows_now]
            + spread(pickers[segs[0]], back_first)
            + spread(pickers[segs[1]], back_second)
        )
    back_neigh = neigh_proj.astype(jnp.float32).T
    back_centre = centre_proj.astype(jnp.float32).T
    latent_grad = jnp.dot(grad_centre.T, back_centre, precision=lax.Precision.HIGHEST)
    latent_grad = latent_grad + jnp.dot(
        sums[:, :width], back_neigh, precision=lax.Precision.HIGHEST
    )
    forces = -sums[:, width : width + 3].T
    energies = live * (lookup(species, species_shift[:, None])[:, 0] + atom_energy)
    return (energies, forces, latent_grad)


def solution(mesh):
    in_specs = (
        P(("gx", "gy", "gz"), None),
        P(None, ("gx", "gy", "gz")),
        P(("gx", "gy", "gz")),
        P(("gx", "gy", "gz"), None),
        P(("gx", "gy", "gz")),
        P(("gx", "gy", "gz")),
        P(),
        P(),
        P(),
        P(),
        P(),
        P(),
        P(),
        P(),
        P(),
        P(),
    )
    out_specs = (P(("gx", "gy", "gz")), P(None, ("gx", "gy", "gz")), P(("gx", "gy", "gz"), None))
    return jax.shard_map(shards, mesh=mesh, in_specs=in_specs, out_specs=out_specs, check_vma=False)
```

```python
import math

import jax
import jax.numpy as jnp
from jax import lax
from jax.experimental import pallas as pl
from jax.experimental.pallas import tpu as pltpu
from jax.sharding import PartitionSpec as P

K = 8
CH = 64
NB = 8
NSPEC = 5
LX_FIX = 1024
LY_FIX = 512
LZ_FIX = 1280


CUTOFF = 6.0
SOFTEN = 0.25


def shortened(shard):
    return jax.tree.map(lambda a: a.astype(jnp.bfloat16) if a.dtype == jnp.float32 else a, shard)


def passed_along(block, axis, distance):
    devices = range(lax.axis_size(axis))
    route = [((i - distance) % len(devices), i) for i in devices]
    return lax.ppermute(block, axis, route)


def by_order(values):
    rest = values.shape[1:]
    return jnp.concatenate(
        [
            values[0:1],
            jnp.broadcast_to(values[1:2], (3,) + rest),
            jnp.broadcast_to(values[2:3], (5,) + rest),
        ],
        axis=0,
    )


SLOTS = 4
ORDER_OF = (0, 1, 1, 1, 2, 2, 2, 2, 2)
GROUPS = ((0,), (1, 2, 3), (4, 5, 6, 7, 8))


def geometry(delta, valid_pair):
    atoms = delta.shape[2]
    radius = jnp.sqrt(jnp.sum(delta * delta, axis=0) + SOFTEN)
    unit = delta / radius
    ratio = radius / CUTOFF
    envelope = jnp.where(ratio < 1.0, (1.0 - ratio * ratio) ** 2, 0.0) * valid_pair
    orders = jnp.arange(1, NB + 1).astype(jnp.float32)
    basis = (
        jnp.sin(orders[:, None, None] * (math.pi / CUTOFF) * radius[None])
        * (envelope / radius)[None]
    )
    ux, uy, uz = unit[0], unit[1], unit[2]
    r3 = math.sqrt(3.0)
    r15 = math.sqrt(15.0)
    r5 = math.sqrt(5.0)
    harmonics = jnp.stack(
        [
            jnp.ones_like(ux),
            r3 * ux,
            r3 * uy,
            r3 * uz,
            r15 * ux * uy,
            r15 * uy * uz,
            0.5 * r5 * (2.0 * uz * uz - ux * ux - uy * uy),
            r15 * ux * uz,
            0.5 * r15 * (ux * ux - uy * uy),
        ],
        axis=0,
    )
    rows = jnp.concatenate([basis, envelope[None], harmonics], axis=0).reshape(18, K * atoms)
    return jnp.concatenate([rows, jnp.zeros((128 - 18, K * atoms), jnp.float32)], axis=0)


def _mm(a, b):
    return jnp.dot(a, b, preferred_element_type=jnp.float32)


def _sigmoid(v):
    return 0.5 + 0.5 * jnp.tanh(0.5 * v)


def _pair_kernel(
    rows_ref, centre_ref, geo_ref, basis_t_ref, split_t_ref, split_ref, update_t_ref,
    update_ref, tensor_t_ref, tensor_ref, basis_ref, energy_w_ref,
    grad_rows_ref, grad_centre_ref, grad_geo_ref, energy_ref,
    pre_s, hidden_s, mixed_s, damp_s, dlow_s, dgeo_s, env_s, denv_s,
):
    atoms = centre_ref.shape[1]
    f32 = jnp.float32
    bf16 = jnp.bfloat16
    span = SLOTS * atoms
    sub = lax.broadcasted_iota(jnp.int32, (128, span), 0)
    inv_root = 1.0 / math.sqrt(K)
    env_s[...] = jnp.zeros_like(env_s)
    denv_s[...] = jnp.zeros_like(denv_s)

    def block(k):
        return pl.ds(pl.multiple_of(k * span, span), span)

    def twice(v):
        return jnp.concatenate([v] * SLOTS, axis=1)

    def fold(v):
        total = v[:, :atoms]
        for slot in range(1, SLOTS):
            total = total + v[:, slot * atoms : (slot + 1) * atoms]
        return total

    def split_mm(weight, values):
        high = values.astype(bf16)
        low = (values - high.astype(f32)).astype(bf16)
        return _mm(weight, high) + _mm(weight, low)

    def first(k, carry):
        at = block(k)
        geo = geo_ref[:, at]
        radial = split_mm(basis_t_ref[...], geo)
        pre = twice(centre_ref[...]) + rows_ref[:, at].astype(f32) + radial
        envelope = geo[8:9, :]
        hidden = pre * _sigmoid(pre) * envelope
        pre_s[:, at] = pre
        hidden_s[:, at] = hidden
        mixed = _mm(split_t_ref[...], hidden.astype(bf16))
        mixed_s[:, at] = mixed
        for m in range(9):
            l = ORDER_OF[m]
            weight = mixed[3 * CH + l * CH : 3 * CH + (l + 1) * CH, :]
            env_s[m] = env_s[m] + fold(weight * (geo[9 + m : 10 + m, :] * inv_root))
        return carry

    lax.fori_loop(0, K // SLOTS, first, 0)

    def second(k, energy):
        at = block(k)
        geo = geo_ref[:, at]
        envelope = geo[8:9, :]
        hidden = hidden_s[:, at]
        mixed = mixed_s[:, at]
        parts = []
        totals = []
        for l in range(3):
            total = 0.0
            for m in GROUPS[l]:
                total = total + geo[9 + m : 10 + m, :] * twice(env_s[m])
            totals.append(total)
            parts.append(mixed[l * CH : (l + 1) * CH, :] * total)
        scalars = jnp.concatenate(parts, axis=0).astype(bf16)
        z = _mm(update_t_ref[...], hidden.astype(bf16)) + _mm(tensor_t_ref[...], scalars)
        gate = _sigmoid(z)
        update = z * gate
        readout = jnp.sum((hidden + update) * energy_w_ref[...], axis=0, keepdims=True)
        energy = energy + envelope * readout
        dz = (envelope * energy_w_ref[...]) * (gate * (1.0 + z * (1.0 - gate)))
        dz_low = dz.astype(bf16)
        dscalars = _mm(tensor_ref[...], dz_low).astype(bf16).astype(f32)
        dlow_s[:, at] = _mm(update_ref[...], dz_low)
        dgeo = jnp.where(sub == 8, readout, 0.0)
        for l in range(3):
            ds = dscalars[l * CH : (l + 1) * CH, :]
            damp_s[l * CH : (l + 1) * CH, at] = ds * totals[l]
            dtotal = ds * mixed[l * CH : (l + 1) * CH, :]
            for m in GROUPS[l]:
                dgeo = dgeo + jnp.where(
                    sub == 9 + m, jnp.sum(dtotal * twice(env_s[m]), axis=0, keepdims=True), 0.0
                )
                denv_s[m] = denv_s[m] + fold(dtotal * geo[9 + m : 10 + m, :])
        dgeo_s[:, at] = dgeo
        return energy

    energy = lax.fori_loop(0, K // SLOTS, second, jnp.zeros((1, span), f32))
    energy_ref[...] = jnp.broadcast_to(fold(energy), energy_ref.shape)

    def third(k, centre_grad):
        at = block(k)
        geo = geo_ref[:, at]
        envelope = geo[8:9, :]
        mixed = mixed_s[:, at]
        dgeo = dgeo_s[:, at]
        dweights = []
        for l in range(3):
            weight = mixed[3 * CH + l * CH : 3 * CH + (l + 1) * CH, :]
            dweight = 0.0
            for m in GROUPS[l]:
                denv = twice(denv_s[m])
                dweight = dweight + denv * (geo[9 + m : 10 + m, :] * inv_root)
                dgeo = dgeo + jnp.where(
                    sub == 9 + m,
                    jnp.sum(denv * weight, axis=0, keepdims=True) * inv_root,
                    0.0,
                )
            dweights.append(dweight)
        dmixed = jnp.concatenate([damp_s[:, at]] + dweights, axis=0).astype(bf16)
        dlow = dlow_s[:, at] + _mm(split_ref[...], dmixed)
        dhidden = envelope * energy_w_ref[...] + dlow
        pre = pre_s[:, at]
        sig = _sigmoid(pre)
        act = pre * sig
        dgeo = dgeo + jnp.where(sub == 8, jnp.sum(dhidden * act, axis=0, keepdims=True), 0.0)
        dpre = dhidden * envelope * (sig * (1.0 + pre * (1.0 - sig)))
        grad_rows_ref[:, at] = dpre
        dgeo = dgeo + split_mm(basis_ref[...], dpre)
        grad_geo_ref[:, at] = dgeo
        return centre_grad + fold(dpre)

    grad_centre_ref[...] = lax.fori_loop(
        0, K // SLOTS, third, jnp.zeros(grad_centre_ref.shape, f32)
    )


def pair_terms(rows_t, centre_t, geo, basis_proj, split_proj, update_proj, tensor_proj, energy_proj):
    width, pairs = rows_t.shape
    atoms = centre_t.shape[1]
    f32 = jnp.float32
    bf16 = jnp.bfloat16
    basis_pad = jnp.concatenate([basis_proj, jnp.zeros((128 - NB, width), bf16)], axis=0)
    vmem = pl.BlockSpec(memory_space=pltpu.VMEM)
    outs = pl.pallas_call(
        _pair_kernel,
        out_shape=(
            jax.ShapeDtypeStruct((width, pairs), f32),
            jax.ShapeDtypeStruct((width, atoms), f32),
            jax.ShapeDtypeStruct((128, pairs), f32),
            jax.ShapeDtypeStruct((8, atoms), f32),
        ),
        in_specs=[vmem] * 12,
        out_specs=(vmem, vmem, vmem, vmem),
        scratch_shapes=[
            pltpu.VMEM((width, pairs), f32),
            pltpu.VMEM((width, pairs), f32),
            pltpu.VMEM((6 * CH, pairs), f32),
            pltpu.VMEM((3 * CH, pairs), f32),
            pltpu.VMEM((width, pairs), f32),
            pltpu.VMEM((128, pairs), f32),
            pltpu.VMEM((9, CH, atoms), f32),
            pltpu.VMEM((9, CH, atoms), f32),
        ],
        compiler_params=pltpu.CompilerParams(vmem_limit_bytes=60 * 1024 * 1024),
        cost_estimate=pl.CostEstimate(
            flops=int(24 * pairs * width * 128),
            transcendentals=int(3 * pairs * width),
            bytes_accessed=int(16 * pairs * width),
        ),
    )(
        rows_t,
        centre_t,
        geo,
        basis_pad.T,
        split_proj.T,
        split_proj,
        update_proj.T,
        update_proj,
        tensor_proj.T,
        tensor_proj,
        basis_pad,
        jnp.broadcast_to(energy_proj.astype(f32)[:, None], (width, SLOTS * atoms)),
    )
    grad_rows_t, grad_centre_t, grad_geo, energy = outs
    return grad_rows_t, grad_centre_t, grad_geo, energy[0]


def shards(
    latent,
    positions,
    species,
    send_list,
    neighbour,
    atom_count,
    centre_proj,
    neigh_proj,
    centre_table,
    neigh_table,
    basis_proj,
    split_proj,
    update_proj,
    tensor_proj,
    energy_proj,
    species_shift,
):
    atoms, width = latent.shape
    extra = 128
    face_x = atoms // 8
    face_y = atoms // 2
    face_z = atoms // 8
    lengths = [face_x, face_x, face_y, face_y, face_z, face_z]
    starts = [
        0,
        face_x,
        2 * face_x,
        2 * face_x + face_y,
        2 * face_x + 2 * face_y,
        2 * face_x + 2 * face_y + face_z,
    ]
    kinds = jnp.arange(NSPEC, dtype=jnp.int32)

    def lookup(codes, table):
        onehot = (codes[:, None] == kinds[None, :]).astype(jnp.float32)
        return jnp.dot(onehot, table, precision=lax.Precision.HIGHEST)

    def project(rows, codes, weight, table):
        return (
            jnp.dot(rows, weight, preferred_element_type=jnp.float32) + lookup(codes, table)
        ).astype(jnp.bfloat16)

    def spread_cols(onehot, values):
        high = values.astype(jnp.bfloat16)
        low = (values - high.astype(jnp.float32)).astype(jnp.bfloat16)
        return jnp.einsum(
            "wn,nr->wr", high, onehot, preferred_element_type=jnp.float32
        ) + jnp.einsum("wn,nr->wr", low, onehot, preferred_element_type=jnp.float32)

    def spread(onehot, values):
        high = values.astype(jnp.bfloat16)
        low = (values - high.astype(jnp.float32)).astype(jnp.bfloat16)
        return jnp.einsum(
            "nr,nw->rw", onehot, high, preferred_element_type=jnp.float32
        ) + jnp.einsum("nr,nw->rw", onehot, low, preferred_element_type=jnp.float32)

    proj_c = project(latent, species, centre_proj, centre_table)
    proj_n = project(latent, species, neigh_proj, neigh_table)
    send_rows = send_list[0]
    coarse = positions // 16
    fine = positions - coarse * 16
    coord_cols = jnp.concatenate([coarse, fine], axis=0).T.astype(jnp.bfloat16)
    table = jnp.concatenate(
        [proj_n, coord_cols, jnp.zeros((atoms, extra - 6), jnp.bfloat16)], axis=1
    )
    shifts = [(0, -LX_FIX), (0, LX_FIX), (1, -LY_FIX), (1, LY_FIX), (2, -LZ_FIX), (2, LZ_FIX)]
    sections = (("gx", (1, 0)), ("gy", (3, 2)), ("gz", (5, 4)))
    pickers = {}
    base_rows = []
    for section, (axis, segs) in enumerate(sections):
        rows_now = table.shape[0]
        base_rows.append(rows_now)
        parts = [table]
        for number, (segment, direction) in enumerate(((segs[0], 1), (segs[1], -1))):
            picked = send_rows[starts[segment] : starts[segment] + lengths[segment]]
            onehot = (
                picked[:, None] == jnp.arange(rows_now, dtype=jnp.int32)[None, :]
            ).astype(jnp.bfloat16)
            pickers[segment] = onehot
            out = jnp.dot(onehot, table, preferred_element_type=jnp.float32).astype(jnp.bfloat16)
            got = passed_along(out, axis, direction)
            coord_axis, offset = shifts[2 * section + number]
            columns = jnp.arange(width + extra, dtype=jnp.int32)[None, :]
            shift = jnp.where(columns == width + coord_axis, offset // 16, 0).astype(jnp.bfloat16)
            parts.append(got + shift)
        table = jnp.concatenate(parts, axis=0)
    total_rows = table.shape[0]
    neighbour = neighbour.reshape(atoms, K).T.reshape(-1)
    select = (neighbour[:, None] == jnp.arange(total_rows, dtype=jnp.int32)[None, :]).astype(
        jnp.bfloat16
    )
    gathered = jnp.einsum("tw,pt->wp", table, select, preferred_element_type=jnp.float32)
    neigh_cols = gathered[:width].astype(jnp.bfloat16)
    coords_n = gathered[width : width + 3] * 16.0 + gathered[width + 3 : width + 6]
    delta = (coords_n.reshape(3, K, atoms) - positions.astype(jnp.float32)[:, None, :]) * (
        1.0 / 64.0
    )
    live = (jnp.arange(atoms) < atom_count[0]).astype(jnp.float32)
    valid_pair = live[None, :]

    geo, geo_pull = jax.vjp(lambda d: geometry(d, valid_pair), delta)
    grad_neigh, grad_centre, grad_geo, atom_energy = pair_terms(
        neigh_cols,
        proj_c.astype(jnp.float32).T,
        geo,
        basis_proj,
        split_proj,
        update_proj,
        tensor_proj,
        energy_proj,
    )
    (grad_delta,) = geo_pull(grad_geo)
    pairs = grad_neigh.shape[1]
    grads = jnp.concatenate(
        [
            grad_neigh,
            grad_delta.reshape(3, pairs),
            jnp.zeros((extra - 3, pairs), jnp.float32),
        ],
        axis=0,
    )
    sums = spread_cols(select, grads).T
    own_pos = grad_delta.sum(axis=1)
    sums = sums - jnp.pad(own_pos.T, ((0, total_rows - atoms), (width, extra - 3)))
    for section in (2, 1, 0):
        axis, segs = sections[section]
        rows_now = base_rows[section]
        first = atoms + starts[2 * section]
        second = atoms + starts[2 * section + 1]
        back_first = passed_along(sums[first : first + lengths[2 * section]], axis, -1)
        back_second = passed_along(sums[second : second + lengths[2 * section + 1]], axis, 1)
        sums = (
            sums[:rows_now]
            + spread(pickers[segs[0]], back_first)
            + spread(pickers[segs[1]], back_second)
        )
    back_neigh = neigh_proj.astype(jnp.float32).T
    back_centre = centre_proj.astype(jnp.float32).T
    latent_grad = jnp.dot(grad_centre.T, back_centre, precision=lax.Precision.HIGHEST)
    latent_grad = latent_grad + jnp.dot(
        sums[:, :width], back_neigh, precision=lax.Precision.HIGHEST
    )
    forces = -sums[:, width : width + 3].T
    energies = live * (lookup(species, species_shift[:, None])[:, 0] + atom_energy)
    return (energies, forces, latent_grad)


def solution(mesh):
    in_specs = (
        P(("gx", "gy", "gz"), None),
        P(None, ("gx", "gy", "gz")),
        P(("gx", "gy", "gz")),
        P(("gx", "gy", "gz"), None),
        P(("gx", "gy", "gz")),
        P(("gx", "gy", "gz")),
        P(),
        P(),
        P(),
        P(),
        P(),
        P(),
        P(),
        P(),
        P(),
        P(),
    )
    out_specs = (P(("gx", "gy", "gz")), P(None, ("gx", "gy", "gz")), P(("gx", "gy", "gz"), None))
    return jax.shard_map(shards, mesh=mesh, in_specs=in_specs, out_specs=out_specs, check_vma=False)
```

```python
import math

import jax
import jax.numpy as jnp
from jax import lax
from jax.experimental import pallas as pl
from jax.experimental.pallas import tpu as pltpu
from jax.sharding import PartitionSpec as P

K = 8
CH = 64
NB = 8
NSPEC = 5
LX_FIX = 1024
LY_FIX = 512
LZ_FIX = 1280


CUTOFF = 6.0
SOFTEN = 0.25


def shortened(shard):
    return jax.tree.map(lambda a: a.astype(jnp.bfloat16) if a.dtype == jnp.float32 else a, shard)


def passed_along(block, axis, distance):
    devices = range(lax.axis_size(axis))
    route = [((i - distance) % len(devices), i) for i in devices]
    return lax.ppermute(block, axis, route)


def by_order(values):
    rest = values.shape[1:]
    return jnp.concatenate(
        [
            values[0:1],
            jnp.broadcast_to(values[1:2], (3,) + rest),
            jnp.broadcast_to(values[2:3], (5,) + rest),
        ],
        axis=0,
    )


SLOTS = 8
ORDER_OF = (0, 1, 1, 1, 2, 2, 2, 2, 2)
GROUPS = ((0,), (1, 2, 3), (4, 5, 6, 7, 8))


def geometry(delta, valid_pair):
    atoms = delta.shape[2]
    radius = jnp.sqrt(jnp.sum(delta * delta, axis=0) + SOFTEN)
    unit = delta / radius
    ratio = radius / CUTOFF
    envelope = jnp.where(ratio < 1.0, (1.0 - ratio * ratio) ** 2, 0.0) * valid_pair
    orders = jnp.arange(1, NB + 1).astype(jnp.float32)
    basis = (
        jnp.sin(orders[:, None, None] * (math.pi / CUTOFF) * radius[None])
        * (envelope / radius)[None]
    )
    ux, uy, uz = unit[0], unit[1], unit[2]
    r3 = math.sqrt(3.0)
    r15 = math.sqrt(15.0)
    r5 = math.sqrt(5.0)
    harmonics = jnp.stack(
        [
            jnp.ones_like(ux),
            r3 * ux,
            r3 * uy,
            r3 * uz,
            r15 * ux * uy,
            r15 * uy * uz,
            0.5 * r5 * (2.0 * uz * uz - ux * ux - uy * uy),
            r15 * ux * uz,
            0.5 * r15 * (ux * ux - uy * uy),
        ],
        axis=0,
    )
    rows = jnp.concatenate([basis, envelope[None], harmonics], axis=0).reshape(18, K * atoms)
    return jnp.concatenate([rows, jnp.zeros((128 - 18, K * atoms), jnp.float32)], axis=0)


def _mm(a, b):
    return jnp.dot(a, b, preferred_element_type=jnp.float32)


def _sigmoid(v):
    return 0.5 + 0.5 * jnp.tanh(0.5 * v)


def _pair_kernel(
    rows_ref, centre_ref, geo_ref, basis_t_ref, split_t_ref, split_ref, update_t_ref,
    update_ref, tensor_t_ref, tensor_ref, basis_ref, energy_w_ref,
    grad_rows_ref, grad_centre_ref, grad_geo_ref, energy_ref,
    pre_s, hidden_s, mixed_s, damp_s, dlow_s, dgeo_s, env_s, denv_s,
):
    atoms = centre_ref.shape[1]
    f32 = jnp.float32
    bf16 = jnp.bfloat16
    span = SLOTS * atoms
    sub = lax.broadcasted_iota(jnp.int32, (128, span), 0)
    inv_root = 1.0 / math.sqrt(K)
    env_s[...] = jnp.zeros_like(env_s)
    denv_s[...] = jnp.zeros_like(denv_s)

    def block(k):
        return pl.ds(pl.multiple_of(k * span, span), span)

    def twice(v):
        return jnp.concatenate([v] * SLOTS, axis=1)

    def fold(v):
        total = v[:, :atoms]
        for slot in range(1, SLOTS):
            total = total + v[:, slot * atoms : (slot + 1) * atoms]
        return total

    def split_mm(weight, values):
        high = values.astype(bf16)
        low = (values - high.astype(f32)).astype(bf16)
        return _mm(weight, high) + _mm(weight, low)

    def first(k, carry):
        at = block(k)
        geo = geo_ref[:, at]
        radial = split_mm(basis_t_ref[...], geo)
        pre = twice(centre_ref[...]) + rows_ref[:, at].astype(f32) + radial
        envelope = geo[8:9, :]
        hidden = pre * _sigmoid(pre) * envelope
        pre_s[:, at] = pre
        hidden_s[:, at] = hidden
        mixed = _mm(split_t_ref[...], hidden.astype(bf16))
        mixed_s[:, at] = mixed
        for m in range(9):
            l = ORDER_OF[m]
            weight = mixed[3 * CH + l * CH : 3 * CH + (l + 1) * CH, :]
            env_s[m] = env_s[m] + fold(weight * (geo[9 + m : 10 + m, :] * inv_root))
        return carry

    lax.fori_loop(0, K // SLOTS, first, 0)

    def second(k, energy):
        at = block(k)
        geo = geo_ref[:, at]
        envelope = geo[8:9, :]
        hidden = hidden_s[:, at]
        mixed = mixed_s[:, at]
        parts = []
        totals = []
        for l in range(3):
            total = 0.0
            for m in GROUPS[l]:
                total = total + geo[9 + m : 10 + m, :] * twice(env_s[m])
            totals.append(total)
            parts.append(mixed[l * CH : (l + 1) * CH, :] * total)
        scalars = jnp.concatenate(parts, axis=0).astype(bf16)
        z = _mm(update_t_ref[...], hidden.astype(bf16)) + _mm(tensor_t_ref[...], scalars)
        gate = _sigmoid(z)
        update = z * gate
        readout = jnp.sum((hidden + update) * energy_w_ref[...], axis=0, keepdims=True)
        energy = energy + envelope * readout
        dz = (envelope * energy_w_ref[...]) * (gate * (1.0 + z * (1.0 - gate)))
        dz_low = dz.astype(bf16)
        dscalars = _mm(tensor_ref[...], dz_low).astype(bf16).astype(f32)
        dlow_s[:, at] = _mm(update_ref[...], dz_low)
        dgeo = jnp.where(sub == 8, readout, 0.0)
        for l in range(3):
            ds = dscalars[l * CH : (l + 1) * CH, :]
            damp_s[l * CH : (l + 1) * CH, at] = ds * totals[l]
            dtotal = ds * mixed[l * CH : (l + 1) * CH, :]
            for m in GROUPS[l]:
                dgeo = dgeo + jnp.where(
                    sub == 9 + m, jnp.sum(dtotal * twice(env_s[m]), axis=0, keepdims=True), 0.0
                )
                denv_s[m] = denv_s[m] + fold(dtotal * geo[9 + m : 10 + m, :])
        dgeo_s[:, at] = dgeo
        return energy

    energy = lax.fori_loop(0, K // SLOTS, second, jnp.zeros((1, span), f32))
    energy_ref[...] = jnp.broadcast_to(fold(energy), energy_ref.shape)

    def third(k, centre_grad):
        at = block(k)
        geo = geo_ref[:, at]
        envelope = geo[8:9, :]
        mixed = mixed_s[:, at]
        dgeo = dgeo_s[:, at]
        dweights = []
        for l in range(3):
            weight = mixed[3 * CH + l * CH : 3 * CH + (l + 1) * CH, :]
            dweight = 0.0
            for m in GROUPS[l]:
                denv = twice(denv_s[m])
                dweight = dweight + denv * (geo[9 + m : 10 + m, :] * inv_root)
                dgeo = dgeo + jnp.where(
                    sub == 9 + m,
                    jnp.sum(denv * weight, axis=0, keepdims=True) * inv_root,
                    0.0,
                )
            dweights.append(dweight)
        dmixed = jnp.concatenate([damp_s[:, at]] + dweights, axis=0).astype(bf16)
        dlow = dlow_s[:, at] + _mm(split_ref[...], dmixed)
        dhidden = envelope * energy_w_ref[...] + dlow
        pre = pre_s[:, at]
        sig = _sigmoid(pre)
        act = pre * sig
        dgeo = dgeo + jnp.where(sub == 8, jnp.sum(dhidden * act, axis=0, keepdims=True), 0.0)
        dpre = dhidden * envelope * (sig * (1.0 + pre * (1.0 - sig)))
        grad_rows_ref[:, at] = dpre
        dgeo = dgeo + split_mm(basis_ref[...], dpre)
        grad_geo_ref[:, at] = dgeo
        return centre_grad + fold(dpre)

    grad_centre_ref[...] = lax.fori_loop(
        0, K // SLOTS, third, jnp.zeros(grad_centre_ref.shape, f32)
    )


def pair_terms(rows_t, centre_t, geo, basis_proj, split_proj, update_proj, tensor_proj, energy_proj):
    width, pairs = rows_t.shape
    atoms = centre_t.shape[1]
    f32 = jnp.float32
    bf16 = jnp.bfloat16
    basis_pad = jnp.concatenate([basis_proj, jnp.zeros((128 - NB, width), bf16)], axis=0)
    vmem = pl.BlockSpec(memory_space=pltpu.VMEM)
    outs = pl.pallas_call(
        _pair_kernel,
        out_shape=(
            jax.ShapeDtypeStruct((width, pairs), f32),
            jax.ShapeDtypeStruct((width, atoms), f32),
            jax.ShapeDtypeStruct((128, pairs), f32),
            jax.ShapeDtypeStruct((8, atoms), f32),
        ),
        in_specs=[vmem] * 12,
        out_specs=(vmem, vmem, vmem, vmem),
        scratch_shapes=[
            pltpu.VMEM((width, pairs), f32),
            pltpu.VMEM((width, pairs), f32),
            pltpu.VMEM((6 * CH, pairs), f32),
            pltpu.VMEM((3 * CH, pairs), f32),
            pltpu.VMEM((width, pairs), f32),
            pltpu.VMEM((128, pairs), f32),
            pltpu.VMEM((9, CH, atoms), f32),
            pltpu.VMEM((9, CH, atoms), f32),
        ],
        compiler_params=pltpu.CompilerParams(vmem_limit_bytes=60 * 1024 * 1024),
        cost_estimate=pl.CostEstimate(
            flops=int(24 * pairs * width * 128),
            transcendentals=int(3 * pairs * width),
            bytes_accessed=int(16 * pairs * width),
        ),
    )(
        rows_t,
        centre_t,
        geo,
        basis_pad.T,
        split_proj.T,
        split_proj,
        update_proj.T,
        update_proj,
        tensor_proj.T,
        tensor_proj,
        basis_pad,
        jnp.broadcast_to(energy_proj.astype(f32)[:, None], (width, SLOTS * atoms)),
    )
    grad_rows_t, grad_centre_t, grad_geo, energy = outs
    return grad_rows_t, grad_centre_t, grad_geo, energy[0]


def shards(
    latent,
    positions,
    species,
    send_list,
    neighbour,
    atom_count,
    centre_proj,
    neigh_proj,
    centre_table,
    neigh_table,
    basis_proj,
    split_proj,
    update_proj,
    tensor_proj,
    energy_proj,
    species_shift,
):
    atoms, width = latent.shape
    extra = 128
    face_x = atoms // 8
    face_y = atoms // 2
    face_z = atoms // 8
    lengths = [face_x, face_x, face_y, face_y, face_z, face_z]
    starts = [
        0,
        face_x,
        2 * face_x,
        2 * face_x + face_y,
        2 * face_x + 2 * face_y,
        2 * face_x + 2 * face_y + face_z,
    ]
    kinds = jnp.arange(NSPEC, dtype=jnp.int32)

    def lookup(codes, table):
        onehot = (codes[:, None] == kinds[None, :]).astype(jnp.float32)
        return jnp.dot(onehot, table, precision=lax.Precision.HIGHEST)

    def project(rows, codes, weight, table):
        return (
            jnp.dot(rows, weight, preferred_element_type=jnp.float32) + lookup(codes, table)
        ).astype(jnp.bfloat16)

    def spread_cols(onehot, values):
        high = values.astype(jnp.bfloat16)
        low = (values - high.astype(jnp.float32)).astype(jnp.bfloat16)
        return jnp.einsum(
            "wn,nr->wr", high, onehot, preferred_element_type=jnp.float32
        ) + jnp.einsum("wn,nr->wr", low, onehot, preferred_element_type=jnp.float32)

    def spread(onehot, values):
        high = values.astype(jnp.bfloat16)
        low = (values - high.astype(jnp.float32)).astype(jnp.bfloat16)
        return jnp.einsum(
            "nr,nw->rw", onehot, high, preferred_element_type=jnp.float32
        ) + jnp.einsum("nr,nw->rw", onehot, low, preferred_element_type=jnp.float32)

    proj_c = project(latent, species, centre_proj, centre_table)
    proj_n = project(latent, species, neigh_proj, neigh_table)
    send_rows = send_list[0]
    coarse = positions // 16
    fine = positions - coarse * 16
    coord_cols = jnp.concatenate([coarse, fine], axis=0).T.astype(jnp.bfloat16)
    table = jnp.concatenate(
        [proj_n, coord_cols, jnp.zeros((atoms, extra - 6), jnp.bfloat16)], axis=1
    )
    shifts = [(0, -LX_FIX), (0, LX_FIX), (1, -LY_FIX), (1, LY_FIX), (2, -LZ_FIX), (2, LZ_FIX)]
    sections = (("gx", (1, 0)), ("gy", (3, 2)), ("gz", (5, 4)))
    pickers = {}
    base_rows = []
    for section, (axis, segs) in enumerate(sections):
        rows_now = table.shape[0]
        base_rows.append(rows_now)
        parts = [table]
        for number, (segment, direction) in enumerate(((segs[0], 1), (segs[1], -1))):
            picked = send_rows[starts[segment] : starts[segment] + lengths[segment]]
            onehot = (
                picked[:, None] == jnp.arange(rows_now, dtype=jnp.int32)[None, :]
            ).astype(jnp.bfloat16)
            pickers[segment] = onehot
            out = jnp.dot(onehot, table, preferred_element_type=jnp.float32).astype(jnp.bfloat16)
            got = passed_along(out, axis, direction)
            coord_axis, offset = shifts[2 * section + number]
            columns = jnp.arange(width + extra, dtype=jnp.int32)[None, :]
            shift = jnp.where(columns == width + coord_axis, offset // 16, 0).astype(jnp.bfloat16)
            parts.append(got + shift)
        table = jnp.concatenate(parts, axis=0)
    total_rows = table.shape[0]
    neighbour = neighbour.reshape(atoms, K).T.reshape(-1)
    select = (neighbour[:, None] == jnp.arange(total_rows, dtype=jnp.int32)[None, :]).astype(
        jnp.bfloat16
    )
    gathered = jnp.einsum("tw,pt->wp", table, select, preferred_element_type=jnp.float32)
    neigh_cols = gathered[:width].astype(jnp.bfloat16)
    coords_n = gathered[width : width + 3] * 16.0 + gathered[width + 3 : width + 6]
    delta = (coords_n.reshape(3, K, atoms) - positions.astype(jnp.float32)[:, None, :]) * (
        1.0 / 64.0
    )
    live = (jnp.arange(atoms) < atom_count[0]).astype(jnp.float32)
    valid_pair = live[None, :]

    geo, geo_pull = jax.vjp(lambda d: geometry(d, valid_pair), delta)
    grad_neigh, grad_centre, grad_geo, atom_energy = pair_terms(
        neigh_cols,
        proj_c.astype(jnp.float32).T,
        geo,
        basis_proj,
        split_proj,
        update_proj,
        tensor_proj,
        energy_proj,
    )
    (grad_delta,) = geo_pull(grad_geo)
    pairs = grad_neigh.shape[1]
    grads = jnp.concatenate(
        [
            grad_neigh,
            grad_delta.reshape(3, pairs),
            jnp.zeros((extra - 3, pairs), jnp.float32),
        ],
        axis=0,
    )
    sums = spread_cols(select, grads).T
    own_pos = grad_delta.sum(axis=1)
    sums = sums - jnp.pad(own_pos.T, ((0, total_rows - atoms), (width, extra - 3)))
    for section in (2, 1, 0):
        axis, segs = sections[section]
        rows_now = base_rows[section]
        first = atoms + starts[2 * section]
        second = atoms + starts[2 * section + 1]
        back_first = passed_along(sums[first : first + lengths[2 * section]], axis, -1)
        back_second = passed_along(sums[second : second + lengths[2 * section + 1]], axis, 1)
        sums = (
            sums[:rows_now]
            + spread(pickers[segs[0]], back_first)
            + spread(pickers[segs[1]], back_second)
        )
    back_neigh = neigh_proj.astype(jnp.float32).T
    back_centre = centre_proj.astype(jnp.float32).T
    latent_grad = jnp.dot(grad_centre.T, back_centre, precision=lax.Precision.HIGHEST)
    latent_grad = latent_grad + jnp.dot(
        sums[:, :width], back_neigh, precision=lax.Precision.HIGHEST
    )
    forces = -sums[:, width : width + 3].T
    energies = live * (lookup(species, species_shift[:, None])[:, 0] + atom_energy)
    return (energies, forces, latent_grad)


def solution(mesh):
    in_specs = (
        P(("gx", "gy", "gz"), None),
        P(None, ("gx", "gy", "gz")),
        P(("gx", "gy", "gz")),
        P(("gx", "gy", "gz"), None),
        P(("gx", "gy", "gz")),
        P(("gx", "gy", "gz")),
        P(),
        P(),
        P(),
        P(),
        P(),
        P(),
        P(),
        P(),
        P(),
        P(),
    )
    out_specs = (P(("gx", "gy", "gz")), P(None, ("gx", "gy", "gz")), P(("gx", "gy", "gz"), None))
    return jax.shard_map(shards, mesh=mesh, in_specs=in_specs, out_specs=out_specs, check_vma=False)
```

```python
import math

import jax
import jax.numpy as jnp
from jax import lax
from jax.experimental import pallas as pl
from jax.experimental.pallas import tpu as pltpu
from jax.sharding import PartitionSpec as P

K = 8
CH = 64
NB = 8
NSPEC = 5
LX_FIX = 1024
LY_FIX = 512
LZ_FIX = 1280


CUTOFF = 6.0
SOFTEN = 0.25


def shortened(shard):
    return jax.tree.map(lambda a: a.astype(jnp.bfloat16) if a.dtype == jnp.float32 else a, shard)


def passed_along(block, axis, distance):
    devices = range(lax.axis_size(axis))
    route = [((i - distance) % len(devices), i) for i in devices]
    return lax.ppermute(block, axis, route)


def by_order(values):
    rest = values.shape[1:]
    return jnp.concatenate(
        [
            values[0:1],
            jnp.broadcast_to(values[1:2], (3,) + rest),
            jnp.broadcast_to(values[2:3], (5,) + rest),
        ],
        axis=0,
    )


SLOTS = 8
ORDER_OF = (0, 1, 1, 1, 2, 2, 2, 2, 2)
GROUPS = ((0,), (1, 2, 3), (4, 5, 6, 7, 8))


def geometry(delta, valid_pair):
    atoms = delta.shape[2]
    radius = jnp.sqrt(jnp.sum(delta * delta, axis=0) + SOFTEN)
    unit = delta / radius
    ratio = radius / CUTOFF
    envelope = jnp.where(ratio < 1.0, (1.0 - ratio * ratio) ** 2, 0.0) * valid_pair
    orders = jnp.arange(1, NB + 1).astype(jnp.float32)
    basis = (
        jnp.sin(orders[:, None, None] * (math.pi / CUTOFF) * radius[None])
        * (envelope / radius)[None]
    )
    ux, uy, uz = unit[0], unit[1], unit[2]
    r3 = math.sqrt(3.0)
    r15 = math.sqrt(15.0)
    r5 = math.sqrt(5.0)
    harmonics = jnp.stack(
        [
            jnp.ones_like(ux),
            r3 * ux,
            r3 * uy,
            r3 * uz,
            r15 * ux * uy,
            r15 * uy * uz,
            0.5 * r5 * (2.0 * uz * uz - ux * ux - uy * uy),
            r15 * ux * uz,
            0.5 * r15 * (ux * ux - uy * uy),
        ],
        axis=0,
    )
    rows = jnp.concatenate([basis, envelope[None], harmonics], axis=0).reshape(18, K * atoms)
    return jnp.concatenate([rows, jnp.zeros((128 - 18, K * atoms), jnp.float32)], axis=0)


def _mm(a, b):
    return jnp.dot(a, b, preferred_element_type=jnp.float32)


def _sigmoid(v):
    return 0.5 + 0.5 * jnp.tanh(0.5 * v)


def _pair_kernel(
    rows_ref, centre_ref, geo_ref, basis_t_ref, split_t_ref, split_ref, update_t_ref,
    update_ref, tensor_t_ref, tensor_ref, basis_ref, energy_w_ref,
    grad_rows_ref, grad_centre_ref, grad_geo_ref, energy_ref,
    pre_s, hidden_s, mixed_s, damp_s, dlow_s, dgeo_s, env_s, denv_s,
):
    atoms = centre_ref.shape[1]
    f32 = jnp.float32
    bf16 = jnp.bfloat16
    span = SLOTS * atoms
    sub = lax.broadcasted_iota(jnp.int32, (128, span), 0)
    inv_root = 1.0 / math.sqrt(K)
    env_s[...] = jnp.zeros_like(env_s)
    denv_s[...] = jnp.zeros_like(denv_s)

    def block(k):
        return pl.ds(pl.multiple_of(k * span, span), span)

    def twice(v):
        return jnp.concatenate([v] * SLOTS, axis=1)

    def fold(v):
        total = v[:, :atoms]
        for slot in range(1, SLOTS):
            total = total + v[:, slot * atoms : (slot + 1) * atoms]
        return total

    def split_mm(weight, values):
        high = values.astype(bf16)
        low = (values - high.astype(f32)).astype(bf16)
        return _mm(weight, high) + _mm(weight, low)

    def first(k, carry):
        at = block(k)
        geo = geo_ref[:, at]
        radial = split_mm(basis_t_ref[...], geo)
        pre = twice(centre_ref[...]) + rows_ref[0 : centre_ref.shape[0], at] + radial
        envelope = geo[8:9, :]
        hidden = pre * _sigmoid(pre) * envelope
        pre_s[:, at] = pre
        hidden_s[:, at] = hidden
        mixed = _mm(split_t_ref[...], hidden.astype(bf16))
        mixed_s[:, at] = mixed
        for m in range(9):
            l = ORDER_OF[m]
            weight = mixed[3 * CH + l * CH : 3 * CH + (l + 1) * CH, :]
            env_s[m] = env_s[m] + fold(weight * (geo[9 + m : 10 + m, :] * inv_root))
        return carry

    lax.fori_loop(0, K // SLOTS, first, 0)

    def second(k, energy):
        at = block(k)
        geo = geo_ref[:, at]
        envelope = geo[8:9, :]
        hidden = hidden_s[:, at]
        mixed = mixed_s[:, at]
        parts = []
        totals = []
        for l in range(3):
            total = 0.0
            for m in GROUPS[l]:
                total = total + geo[9 + m : 10 + m, :] * twice(env_s[m])
            totals.append(total)
            parts.append(mixed[l * CH : (l + 1) * CH, :] * total)
        scalars = jnp.concatenate(parts, axis=0).astype(bf16)
        z = _mm(update_t_ref[...], hidden.astype(bf16)) + _mm(tensor_t_ref[...], scalars)
        gate = _sigmoid(z)
        update = z * gate
        readout = jnp.sum((hidden + update) * twice(energy_w_ref[...]), axis=0, keepdims=True)
        energy = energy + envelope * readout
        dz = (envelope * twice(energy_w_ref[...])) * (gate * (1.0 + z * (1.0 - gate)))
        dz_low = dz.astype(bf16)
        dscalars = _mm(tensor_ref[...], dz_low).astype(bf16).astype(f32)
        dlow_s[:, at] = _mm(update_ref[...], dz_low)
        dgeo = jnp.where(sub == 8, readout, 0.0)
        for l in range(3):
            ds = dscalars[l * CH : (l + 1) * CH, :]
            damp_s[l * CH : (l + 1) * CH, at] = ds * totals[l]
            dtotal = ds * mixed[l * CH : (l + 1) * CH, :]
            for m in GROUPS[l]:
                dgeo = dgeo + jnp.where(
                    sub == 9 + m, jnp.sum(dtotal * twice(env_s[m]), axis=0, keepdims=True), 0.0
                )
                denv_s[m] = denv_s[m] + fold(dtotal * geo[9 + m : 10 + m, :])
        dgeo_s[:, at] = dgeo
        return energy

    energy = lax.fori_loop(0, K // SLOTS, second, jnp.zeros((1, span), f32))
    energy_ref[...] = jnp.broadcast_to(fold(energy), energy_ref.shape)

    def third(k, centre_grad):
        at = block(k)
        geo = geo_ref[:, at]
        envelope = geo[8:9, :]
        mixed = mixed_s[:, at]
        dgeo = dgeo_s[:, at]
        dweights = []
        for l in range(3):
            weight = mixed[3 * CH + l * CH : 3 * CH + (l + 1) * CH, :]
            dweight = 0.0
            for m in GROUPS[l]:
                denv = twice(denv_s[m])
                dweight = dweight + denv * (geo[9 + m : 10 + m, :] * inv_root)
                dgeo = dgeo + jnp.where(
                    sub == 9 + m,
                    jnp.sum(denv * weight, axis=0, keepdims=True) * inv_root,
                    0.0,
                )
            dweights.append(dweight)
        dmixed = jnp.concatenate([damp_s[:, at]] + dweights, axis=0).astype(bf16)
        dlow = dlow_s[:, at] + _mm(split_ref[...], dmixed)
        dhidden = envelope * twice(energy_w_ref[...]) + dlow
        pre = pre_s[:, at]
        sig = _sigmoid(pre)
        act = pre * sig
        dgeo = dgeo + jnp.where(sub == 8, jnp.sum(dhidden * act, axis=0, keepdims=True), 0.0)
        dpre = dhidden * envelope * (sig * (1.0 + pre * (1.0 - sig)))
        grad_rows_ref[:, at] = dpre
        dgeo = dgeo + split_mm(basis_ref[...], dpre)
        grad_geo_ref[:, at] = dgeo
        return centre_grad + fold(dpre)

    grad_centre_ref[...] = lax.fori_loop(
        0, K // SLOTS, third, jnp.zeros(grad_centre_ref.shape, f32)
    )


def pair_terms(rows_t, centre_t, geo, basis_proj, split_proj, update_proj, tensor_proj, energy_proj):
    width, atoms = centre_t.shape
    pairs = rows_t.shape[1]
    f32 = jnp.float32
    bf16 = jnp.bfloat16
    basis_pad = jnp.concatenate([basis_proj, jnp.zeros((128 - NB, width), bf16)], axis=0)
    vmem = pl.BlockSpec(memory_space=pltpu.VMEM)
    outs = pl.pallas_call(
        _pair_kernel,
        out_shape=(
            jax.ShapeDtypeStruct((width, pairs), f32),
            jax.ShapeDtypeStruct((width, atoms), f32),
            jax.ShapeDtypeStruct((128, pairs), f32),
            jax.ShapeDtypeStruct((8, atoms), f32),
        ),
        in_specs=[vmem] * 12,
        out_specs=(vmem, vmem, vmem, vmem),
        scratch_shapes=[
            pltpu.VMEM((width, pairs), f32),
            pltpu.VMEM((width, pairs), f32),
            pltpu.VMEM((6 * CH, pairs), f32),
            pltpu.VMEM((3 * CH, pairs), f32),
            pltpu.VMEM((width, pairs), f32),
            pltpu.VMEM((128, pairs), f32),
            pltpu.VMEM((9, CH, atoms), f32),
            pltpu.VMEM((9, CH, atoms), f32),
        ],
        compiler_params=pltpu.CompilerParams(vmem_limit_bytes=60 * 1024 * 1024),
        cost_estimate=pl.CostEstimate(
            flops=int(24 * pairs * width * 128),
            transcendentals=int(3 * pairs * width),
            bytes_accessed=int(16 * pairs * width),
        ),
    )(
        rows_t,
        centre_t,
        geo,
        basis_pad.T,
        split_proj.T,
        split_proj,
        update_proj.T,
        update_proj,
        tensor_proj.T,
        tensor_proj,
        basis_pad,
        jnp.broadcast_to(energy_proj.astype(f32)[:, None], (width, atoms)),
    )
    grad_rows_t, grad_centre_t, grad_geo, energy = outs
    return grad_rows_t, grad_centre_t, grad_geo, energy[0]


def shards(
    latent,
    positions,
    species,
    send_list,
    neighbour,
    atom_count,
    centre_proj,
    neigh_proj,
    centre_table,
    neigh_table,
    basis_proj,
    split_proj,
    update_proj,
    tensor_proj,
    energy_proj,
    species_shift,
):
    atoms, width = latent.shape
    extra = 128
    face_x = atoms // 8
    face_y = atoms // 2
    face_z = atoms // 8
    lengths = [face_x, face_x, face_y, face_y, face_z, face_z]
    starts = [
        0,
        face_x,
        2 * face_x,
        2 * face_x + face_y,
        2 * face_x + 2 * face_y,
        2 * face_x + 2 * face_y + face_z,
    ]
    kinds = jnp.arange(NSPEC, dtype=jnp.int32)

    def lookup(codes, table):
        onehot = (codes[:, None] == kinds[None, :]).astype(jnp.float32)
        return jnp.dot(onehot, table, precision=lax.Precision.HIGHEST)

    def project(rows, codes, weight, table):
        return (
            jnp.dot(rows, weight, preferred_element_type=jnp.float32) + lookup(codes, table)
        ).astype(jnp.bfloat16)

    def spread_cols(onehot, values):
        high = values.astype(jnp.bfloat16)
        low = (values - high.astype(jnp.float32)).astype(jnp.bfloat16)
        return jnp.einsum(
            "wn,nr->wr", high, onehot, preferred_element_type=jnp.float32
        ) + jnp.einsum("wn,nr->wr", low, onehot, preferred_element_type=jnp.float32)

    def spread(onehot, values):
        high = values.astype(jnp.bfloat16)
        low = (values - high.astype(jnp.float32)).astype(jnp.bfloat16)
        return jnp.einsum(
            "nr,nw->rw", onehot, high, preferred_element_type=jnp.float32
        ) + jnp.einsum("nr,nw->rw", onehot, low, preferred_element_type=jnp.float32)

    proj_c = project(latent, species, centre_proj, centre_table)
    proj_n = project(latent, species, neigh_proj, neigh_table)
    send_rows = send_list[0]
    coarse = positions // 16
    fine = positions - coarse * 16
    coord_cols = jnp.concatenate([coarse, fine], axis=0).T.astype(jnp.bfloat16)
    table = jnp.concatenate(
        [proj_n, coord_cols, jnp.zeros((atoms, extra - 6), jnp.bfloat16)], axis=1
    )
    shifts = [(0, -LX_FIX), (0, LX_FIX), (1, -LY_FIX), (1, LY_FIX), (2, -LZ_FIX), (2, LZ_FIX)]
    sections = (("gx", (1, 0)), ("gy", (3, 2)), ("gz", (5, 4)))
    pickers = {}
    base_rows = []
    for section, (axis, segs) in enumerate(sections):
        rows_now = table.shape[0]
        base_rows.append(rows_now)
        parts = [table]
        for number, (segment, direction) in enumerate(((segs[0], 1), (segs[1], -1))):
            picked = send_rows[starts[segment] : starts[segment] + lengths[segment]]
            onehot = (
                picked[:, None] == jnp.arange(rows_now, dtype=jnp.int32)[None, :]
            ).astype(jnp.bfloat16)
            pickers[segment] = onehot
            out = jnp.dot(onehot, table, preferred_element_type=jnp.float32).astype(jnp.bfloat16)
            got = passed_along(out, axis, direction)
            coord_axis, offset = shifts[2 * section + number]
            columns = jnp.arange(width + extra, dtype=jnp.int32)[None, :]
            shift = jnp.where(columns == width + coord_axis, offset // 16, 0).astype(jnp.bfloat16)
            parts.append(got + shift)
        table = jnp.concatenate(parts, axis=0)
    total_rows = table.shape[0]
    neighbour = neighbour.reshape(atoms, K).T.reshape(-1)
    select = (neighbour[:, None] == jnp.arange(total_rows, dtype=jnp.int32)[None, :]).astype(
        jnp.bfloat16
    )
    gathered = jnp.einsum("tw,pt->wp", table, select, preferred_element_type=jnp.float32)
    neigh_cols = gathered
    coords_n = gathered[width : width + 3] * 16.0 + gathered[width + 3 : width + 6]
    delta = (coords_n.reshape(3, K, atoms) - positions.astype(jnp.float32)[:, None, :]) * (
        1.0 / 64.0
    )
    live = (jnp.arange(atoms) < atom_count[0]).astype(jnp.float32)
    valid_pair = live[None, :]

    geo, geo_pull = jax.vjp(lambda d: geometry(d, valid_pair), delta)
    grad_neigh, grad_centre, grad_geo, atom_energy = pair_terms(
        neigh_cols,
        proj_c.astype(jnp.float32).T,
        geo,
        basis_proj,
        split_proj,
        update_proj,
        tensor_proj,
        energy_proj,
    )
    (grad_delta,) = geo_pull(grad_geo)
    pairs = grad_neigh.shape[1]
    grads = jnp.concatenate(
        [
            grad_neigh,
            grad_delta.reshape(3, pairs),
            jnp.zeros((extra - 3, pairs), jnp.float32),
        ],
        axis=0,
    )
    sums = spread_cols(select, grads).T
    own_pos = grad_delta.sum(axis=1)
    sums = sums - jnp.pad(own_pos.T, ((0, total_rows - atoms), (width, extra - 3)))
    for section in (2, 1, 0):
        axis, segs = sections[section]
        rows_now = base_rows[section]
        first = atoms + starts[2 * section]
        second = atoms + starts[2 * section + 1]
        back_first = passed_along(sums[first : first + lengths[2 * section]], axis, -1)
        back_second = passed_along(sums[second : second + lengths[2 * section + 1]], axis, 1)
        sums = (
            sums[:rows_now]
            + spread(pickers[segs[0]], back_first)
            + spread(pickers[segs[1]], back_second)
        )
    back_neigh = neigh_proj.astype(jnp.float32).T
    back_centre = centre_proj.astype(jnp.float32).T
    latent_grad = jnp.dot(grad_centre.T, back_centre, precision=lax.Precision.HIGHEST)
    latent_grad = latent_grad + jnp.dot(
        sums[:, :width], back_neigh, precision=lax.Precision.HIGHEST
    )
    forces = -sums[:, width : width + 3].T
    energies = live * (lookup(species, species_shift[:, None])[:, 0] + atom_energy)
    return (energies, forces, latent_grad)


def solution(mesh):
    in_specs = (
        P(("gx", "gy", "gz"), None),
        P(None, ("gx", "gy", "gz")),
        P(("gx", "gy", "gz")),
        P(("gx", "gy", "gz"), None),
        P(("gx", "gy", "gz")),
        P(("gx", "gy", "gz")),
        P(),
        P(),
        P(),
        P(),
        P(),
        P(),
        P(),
        P(),
        P(),
        P(),
    )
    out_specs = (P(("gx", "gy", "gz")), P(None, ("gx", "gy", "gz")), P(("gx", "gy", "gz"), None))
    return jax.shard_map(shards, mesh=mesh, in_specs=in_specs, out_specs=out_specs, check_vma=False)
```

```python
import math

import jax
import jax.numpy as jnp
from jax import lax
from jax.experimental import pallas as pl
from jax.experimental.pallas import tpu as pltpu
from jax.sharding import PartitionSpec as P

K = 8
CH = 64
NB = 8
NSPEC = 5
LX_FIX = 1024
LY_FIX = 512
LZ_FIX = 1280


CUTOFF = 6.0
SOFTEN = 0.25


def shortened(shard):
    return jax.tree.map(lambda a: a.astype(jnp.bfloat16) if a.dtype == jnp.float32 else a, shard)


def passed_along(block, axis, distance):
    devices = range(lax.axis_size(axis))
    route = [((i - distance) % len(devices), i) for i in devices]
    return lax.ppermute(block, axis, route)


def by_order(values):
    rest = values.shape[1:]
    return jnp.concatenate(
        [
            values[0:1],
            jnp.broadcast_to(values[1:2], (3,) + rest),
            jnp.broadcast_to(values[2:3], (5,) + rest),
        ],
        axis=0,
    )


SLOTS = 8
ORDER_OF = (0, 1, 1, 1, 2, 2, 2, 2, 2)
GROUPS = ((0,), (1, 2, 3), (4, 5, 6, 7, 8))


def geometry(delta, valid_pair):
    atoms = delta.shape[2]
    radius = jnp.sqrt(jnp.sum(delta * delta, axis=0) + SOFTEN)
    unit = delta / radius
    ratio = radius / CUTOFF
    envelope = jnp.where(ratio < 1.0, (1.0 - ratio * ratio) ** 2, 0.0) * valid_pair
    orders = jnp.arange(1, NB + 1).astype(jnp.float32)
    basis = (
        jnp.sin(orders[:, None, None] * (math.pi / CUTOFF) * radius[None])
        * (envelope / radius)[None]
    )
    ux, uy, uz = unit[0], unit[1], unit[2]
    r3 = math.sqrt(3.0)
    r15 = math.sqrt(15.0)
    r5 = math.sqrt(5.0)
    harmonics = jnp.stack(
        [
            jnp.ones_like(ux),
            r3 * ux,
            r3 * uy,
            r3 * uz,
            r15 * ux * uy,
            r15 * uy * uz,
            0.5 * r5 * (2.0 * uz * uz - ux * ux - uy * uy),
            r15 * ux * uz,
            0.5 * r15 * (ux * ux - uy * uy),
        ],
        axis=0,
    )
    rows = jnp.concatenate([basis, envelope[None], harmonics], axis=0).reshape(18, K * atoms)
    return jnp.concatenate([rows, jnp.zeros((128 - 18, K * atoms), jnp.float32)], axis=0)


def _mm(a, b):
    return jnp.dot(a, b, preferred_element_type=jnp.float32)


def _sigmoid(v):
    return 0.5 + 0.5 * jnp.tanh(0.5 * v)


def _pair_kernel(
    rows_ref, centre_ref, geo_ref, basis_t_ref, split_t_ref, split_ref, update_t_ref,
    update_ref, tensor_t_ref, tensor_ref, basis_ref, energy_w_ref,
    grad_rows_ref, grad_centre_ref, grad_geo_ref, energy_ref,
    pre_s, hidden_s, mixed_s, damp_s, dlow_s, dgeo_s, env_s, denv_s,
):
    atoms = centre_ref.shape[1]
    f32 = jnp.float32
    bf16 = jnp.bfloat16
    span = SLOTS * atoms
    sub = lax.broadcasted_iota(jnp.int32, (128, span), 0)
    inv_root = 1.0 / math.sqrt(K)
    env_s[...] = jnp.zeros_like(env_s)
    denv_s[...] = jnp.zeros_like(denv_s)

    def block(k):
        return pl.ds(pl.multiple_of(k * span, span), span)

    def twice(v):
        return jnp.concatenate([v] * SLOTS, axis=1)

    def fold(v):
        total = v[:, :atoms]
        for slot in range(1, SLOTS):
            total = total + v[:, slot * atoms : (slot + 1) * atoms]
        return total

    def split_mm(weight, values):
        high = values.astype(bf16)
        low = (values - high.astype(f32)).astype(bf16)
        return _mm(weight, high) + _mm(weight, low)

    def first(k, carry):
        at = block(k)
        geo = geo_ref[:, at]
        radial = split_mm(basis_t_ref[...], geo)
        pre = twice(centre_ref[...]) + rows_ref[:, at].astype(f32) + radial
        envelope = geo[8:9, :]
        hidden = pre * _sigmoid(pre) * envelope
        pre_s[:, at] = pre
        hidden_s[:, at] = hidden
        mixed = _mm(split_t_ref[...], hidden.astype(bf16))
        mixed_s[:, at] = mixed
        for m in range(9):
            l = ORDER_OF[m]
            weight = mixed[3 * CH + l * CH : 3 * CH + (l + 1) * CH, :]
            env_s[m] = env_s[m] + fold(weight * (geo[9 + m : 10 + m, :] * inv_root))
        return carry

    lax.fori_loop(0, K // SLOTS, first, 0)

    def second(k, energy):
        at = block(k)
        geo = geo_ref[:, at]
        envelope = geo[8:9, :]
        hidden = hidden_s[:, at]
        mixed = mixed_s[:, at]
        parts = []
        totals = []
        for l in range(3):
            total = 0.0
            for m in GROUPS[l]:
                total = total + geo[9 + m : 10 + m, :] * twice(env_s[m])
            totals.append(total)
            parts.append(mixed[l * CH : (l + 1) * CH, :] * total)
        scalars = jnp.concatenate(parts, axis=0).astype(bf16)
        z = _mm(update_t_ref[...], hidden.astype(bf16)) + _mm(tensor_t_ref[...], scalars)
        gate = _sigmoid(z)
        update = z * gate
        readout = jnp.sum((hidden + update) * energy_w_ref[...], axis=0, keepdims=True)
        energy = energy + envelope * readout
        dz = (envelope * energy_w_ref[...]) * (gate * (1.0 + z * (1.0 - gate)))
        dz_low = dz.astype(bf16)
        dscalars = _mm(tensor_ref[...], dz_low).astype(bf16).astype(f32)
        dlow_s[:, at] = _mm(update_ref[...], dz_low)
        dgeo = jnp.where(sub == 8, readout, 0.0)
        for l in range(3):
            ds = dscalars[l * CH : (l + 1) * CH, :]
            damp_s[l * CH : (l + 1) * CH, at] = ds * totals[l]
            dtotal = ds * mixed[l * CH : (l + 1) * CH, :]
            for m in GROUPS[l]:
                dgeo = dgeo + jnp.where(
                    sub == 9 + m, jnp.sum(dtotal * twice(env_s[m]), axis=0, keepdims=True), 0.0
                )
                denv_s[m] = denv_s[m] + fold(dtotal * geo[9 + m : 10 + m, :])
        dgeo_s[:, at] = dgeo
        return energy

    energy = lax.fori_loop(0, K // SLOTS, second, jnp.zeros((1, span), f32))
    energy_ref[...] = jnp.broadcast_to(fold(energy), energy_ref.shape)

    def third(k, centre_grad):
        at = block(k)
        geo = geo_ref[:, at]
        envelope = geo[8:9, :]
        mixed = mixed_s[:, at]
        dgeo = dgeo_s[:, at]
        dweights = []
        for l in range(3):
            weight = mixed[3 * CH + l * CH : 3 * CH + (l + 1) * CH, :]
            dweight = 0.0
            for m in GROUPS[l]:
                denv = twice(denv_s[m])
                dweight = dweight + denv * (geo[9 + m : 10 + m, :] * inv_root)
                dgeo = dgeo + jnp.where(
                    sub == 9 + m,
                    jnp.sum(denv * weight, axis=0, keepdims=True) * inv_root,
                    0.0,
                )
            dweights.append(dweight)
        dmixed = jnp.concatenate([damp_s[:, at]] + dweights, axis=0).astype(bf16)
        dlow = dlow_s[:, at] + _mm(split_ref[...], dmixed)
        dhidden = envelope * energy_w_ref[...] + dlow
        pre = pre_s[:, at]
        sig = _sigmoid(pre)
        act = pre * sig
        dgeo = dgeo + jnp.where(sub == 8, jnp.sum(dhidden * act, axis=0, keepdims=True), 0.0)
        dpre = dhidden * envelope * (sig * (1.0 + pre * (1.0 - sig)))
        grad_rows_ref[:, at] = dpre
        dgeo = dgeo + split_mm(basis_ref[...], dpre)
        grad_geo_ref[:, at] = dgeo
        return centre_grad + fold(dpre)

    grad_centre_ref[...] = lax.fori_loop(
        0, K // SLOTS, third, jnp.zeros(grad_centre_ref.shape, f32)
    )


def pair_terms(rows_t, centre_t, geo, basis_proj, split_proj, update_proj, tensor_proj, energy_proj):
    width, pairs = rows_t.shape
    atoms = centre_t.shape[1]
    f32 = jnp.float32
    bf16 = jnp.bfloat16
    basis_pad = jnp.concatenate([basis_proj, jnp.zeros((128 - NB, width), bf16)], axis=0)
    vmem = pl.BlockSpec(memory_space=pltpu.VMEM)
    outs = pl.pallas_call(
        _pair_kernel,
        out_shape=(
            jax.ShapeDtypeStruct((width, pairs), f32),
            jax.ShapeDtypeStruct((width, atoms), f32),
            jax.ShapeDtypeStruct((128, pairs), f32),
            jax.ShapeDtypeStruct((8, atoms), f32),
        ),
        in_specs=[vmem] * 12,
        out_specs=(vmem, vmem, vmem, vmem),
        scratch_shapes=[
            pltpu.VMEM((width, pairs), f32),
            pltpu.VMEM((width, pairs), f32),
            pltpu.VMEM((6 * CH, pairs), f32),
            pltpu.VMEM((3 * CH, pairs), f32),
            pltpu.VMEM((width, pairs), f32),
            pltpu.VMEM((128, pairs), f32),
            pltpu.VMEM((9, CH, atoms), f32),
            pltpu.VMEM((9, CH, atoms), f32),
        ],
        compiler_params=pltpu.CompilerParams(vmem_limit_bytes=60 * 1024 * 1024),
        cost_estimate=pl.CostEstimate(
            flops=int(24 * pairs * width * 128),
            transcendentals=int(3 * pairs * width),
            bytes_accessed=int(16 * pairs * width),
        ),
    )(
        rows_t,
        centre_t,
        geo,
        basis_pad.T,
        split_proj.T,
        split_proj,
        update_proj.T,
        update_proj,
        tensor_proj.T,
        tensor_proj,
        basis_pad,
        jnp.broadcast_to(energy_proj.astype(f32)[:, None], (width, SLOTS * atoms)),
    )
    grad_rows_t, grad_centre_t, grad_geo, energy = outs
    return grad_rows_t, grad_centre_t, grad_geo, energy[0]


def shards(
    latent,
    positions,
    species,
    send_list,
    neighbour,
    atom_count,
    centre_proj,
    neigh_proj,
    centre_table,
    neigh_table,
    basis_proj,
    split_proj,
    update_proj,
    tensor_proj,
    energy_proj,
    species_shift,
):
    atoms, width = latent.shape
    extra = 128
    face_x = atoms // 8
    face_y = atoms // 2
    face_z = atoms // 8
    lengths = [face_x, face_x, face_y, face_y, face_z, face_z]
    starts = [
        0,
        face_x,
        2 * face_x,
        2 * face_x + face_y,
        2 * face_x + 2 * face_y,
        2 * face_x + 2 * face_y + face_z,
    ]
    kinds = jnp.arange(NSPEC, dtype=jnp.int32)

    def lookup(codes, table):
        onehot = (codes[:, None] == kinds[None, :]).astype(jnp.float32)
        return jnp.dot(onehot, table, precision=lax.Precision.HIGHEST)

    def project(rows, codes, weight, table):
        return (
            jnp.dot(rows, weight, preferred_element_type=jnp.float32) + lookup(codes, table)
        ).astype(jnp.bfloat16)

    def spread_cols(onehot, values):
        high = values.astype(jnp.bfloat16)
        low = (values - high.astype(jnp.float32)).astype(jnp.bfloat16)
        return jnp.einsum(
            "wn,nr->wr", high, onehot, preferred_element_type=jnp.float32
        ) + jnp.einsum("wn,nr->wr", low, onehot, preferred_element_type=jnp.float32)

    def spread(onehot, values):
        high = values.astype(jnp.bfloat16)
        low = (values - high.astype(jnp.float32)).astype(jnp.bfloat16)
        return jnp.einsum(
            "nr,nw->rw", onehot, high, preferred_element_type=jnp.float32
        ) + jnp.einsum("nr,nw->rw", onehot, low, preferred_element_type=jnp.float32)

    proj_c = project(latent, species, centre_proj, centre_table)
    proj_n = project(latent, species, neigh_proj, neigh_table)
    send_rows = send_list[0]
    coarse = positions // 16
    fine = positions - coarse * 16
    coord_cols = jnp.concatenate([coarse, fine], axis=0).T.astype(jnp.bfloat16)
    table = jnp.concatenate(
        [proj_n, coord_cols, jnp.zeros((atoms, extra - 6), jnp.bfloat16)], axis=1
    )
    shifts = [(0, -LX_FIX), (0, LX_FIX), (1, -LY_FIX), (1, LY_FIX), (2, -LZ_FIX), (2, LZ_FIX)]
    sections = (("gx", (1, 0)), ("gy", (3, 2)), ("gz", (5, 4)))
    pickers = {}
    base_rows = []
    for section, (axis, segs) in enumerate(sections):
        rows_now = table.shape[0]
        base_rows.append(rows_now)
        parts = [table]
        for number, (segment, direction) in enumerate(((segs[0], 1), (segs[1], -1))):
            picked = send_rows[starts[segment] : starts[segment] + lengths[segment]]
            onehot = (
                picked[:, None] == jnp.arange(rows_now, dtype=jnp.int32)[None, :]
            ).astype(jnp.bfloat16)
            pickers[segment] = onehot
            if section == 0:
                chosen = jnp.dot(onehot, latent, preferred_element_type=jnp.float32)
                kinds_of = jnp.take(species, picked, axis=0)
                out = jnp.concatenate(
                    [
                        project(chosen.astype(jnp.bfloat16), kinds_of, neigh_proj, neigh_table),
                        jnp.dot(
                            onehot, table[:, width:], preferred_element_type=jnp.float32
                        ).astype(jnp.bfloat16),
                    ],
                    axis=1,
                )
            else:
                out = jnp.dot(onehot, table, preferred_element_type=jnp.float32).astype(
                    jnp.bfloat16
                )
            got = passed_along(out, axis, direction)
            coord_axis, offset = shifts[2 * section + number]
            columns = jnp.arange(width + extra, dtype=jnp.int32)[None, :]
            shift = jnp.where(columns == width + coord_axis, offset // 16, 0).astype(jnp.bfloat16)
            parts.append(got + shift)
        table = jnp.concatenate(parts, axis=0)
    total_rows = table.shape[0]
    neighbour = neighbour.reshape(atoms, K).T.reshape(-1)
    select = (neighbour[:, None] == jnp.arange(total_rows, dtype=jnp.int32)[None, :]).astype(
        jnp.bfloat16
    )
    gathered = jnp.einsum("tw,pt->wp", table, select, preferred_element_type=jnp.float32)
    neigh_cols = gathered[:width].astype(jnp.bfloat16)
    coords_n = gathered[width : width + 3] * 16.0 + gathered[width + 3 : width + 6]
    delta = (coords_n.reshape(3, K, atoms) - positions.astype(jnp.float32)[:, None, :]) * (
        1.0 / 64.0
    )
    live = (jnp.arange(atoms) < atom_count[0]).astype(jnp.float32)
    valid_pair = live[None, :]

    geo, geo_pull = jax.vjp(lambda d: geometry(d, valid_pair), delta)
    grad_neigh, grad_centre, grad_geo, atom_energy = pair_terms(
        neigh_cols,
        proj_c.astype(jnp.float32).T,
        geo,
        basis_proj,
        split_proj,
        update_proj,
        tensor_proj,
        energy_proj,
    )
    (grad_delta,) = geo_pull(grad_geo)
    pairs = grad_neigh.shape[1]
    grads = jnp.concatenate(
        [
            grad_neigh,
            grad_delta.reshape(3, pairs),
            jnp.zeros((extra - 3, pairs), jnp.float32),
        ],
        axis=0,
    )
    sums = spread_cols(select, grads).T
    own_pos = grad_delta.sum(axis=1)
    sums = sums - jnp.pad(own_pos.T, ((0, total_rows - atoms), (width, extra - 3)))
    for section in (2, 1, 0):
        axis, segs = sections[section]
        rows_now = base_rows[section]
        first = atoms + starts[2 * section]
        second = atoms + starts[2 * section + 1]
        back_first = passed_along(sums[first : first + lengths[2 * section]], axis, -1)
        back_second = passed_along(sums[second : second + lengths[2 * section + 1]], axis, 1)
        sums = (
            sums[:rows_now]
            + spread(pickers[segs[0]], back_first)
            + spread(pickers[segs[1]], back_second)
        )
    back_neigh = neigh_proj.astype(jnp.float32).T
    back_centre = centre_proj.astype(jnp.float32).T
    latent_grad = jnp.dot(grad_centre.T, back_centre, precision=lax.Precision.HIGHEST)
    latent_grad = latent_grad + jnp.dot(
        sums[:, :width], back_neigh, precision=lax.Precision.HIGHEST
    )
    forces = -sums[:, width : width + 3].T
    energies = live * (lookup(species, species_shift[:, None])[:, 0] + atom_energy)
    return (energies, forces, latent_grad)


def solution(mesh):
    in_specs = (
        P(("gx", "gy", "gz"), None),
        P(None, ("gx", "gy", "gz")),
        P(("gx", "gy", "gz")),
        P(("gx", "gy", "gz"), None),
        P(("gx", "gy", "gz")),
        P(("gx", "gy", "gz")),
        P(),
        P(),
        P(),
        P(),
        P(),
        P(),
        P(),
        P(),
        P(),
        P(),
    )
    out_specs = (P(("gx", "gy", "gz")), P(None, ("gx", "gy", "gz")), P(("gx", "gy", "gz"), None))
    return jax.shard_map(shards, mesh=mesh, in_specs=in_specs, out_specs=out_specs, check_vma=False)
```

```python
import math

import jax
import jax.numpy as jnp
from jax import lax
from jax.experimental import pallas as pl
from jax.experimental.pallas import tpu as pltpu
from jax.sharding import PartitionSpec as P

K = 8
CH = 64
NB = 8
NSPEC = 5
LX_FIX = 1024
LY_FIX = 512
LZ_FIX = 1280


CUTOFF = 6.0
SOFTEN = 0.25


def shortened(shard):
    return jax.tree.map(lambda a: a.astype(jnp.bfloat16) if a.dtype == jnp.float32 else a, shard)


def passed_along(block, axis, distance):
    devices = range(lax.axis_size(axis))
    route = [((i - distance) % len(devices), i) for i in devices]
    return lax.ppermute(block, axis, route)


def by_order(values):
    rest = values.shape[1:]
    return jnp.concatenate(
        [
            values[0:1],
            jnp.broadcast_to(values[1:2], (3,) + rest),
            jnp.broadcast_to(values[2:3], (5,) + rest),
        ],
        axis=0,
    )


SLOTS = 8
ORDER_OF = (0, 1, 1, 1, 2, 2, 2, 2, 2)
GROUPS = ((0,), (1, 2, 3), (4, 5, 6, 7, 8))


def geometry(delta, valid_pair):
    atoms = delta.shape[2]
    radius = jnp.sqrt(jnp.sum(delta * delta, axis=0) + SOFTEN)
    unit = delta / radius
    ratio = radius / CUTOFF
    envelope = jnp.where(ratio < 1.0, (1.0 - ratio * ratio) ** 2, 0.0) * valid_pair
    orders = jnp.arange(1, NB + 1).astype(jnp.float32)
    basis = (
        jnp.sin(orders[:, None, None] * (math.pi / CUTOFF) * radius[None])
        * (envelope / radius)[None]
    )
    ux, uy, uz = unit[0], unit[1], unit[2]
    r3 = math.sqrt(3.0)
    r15 = math.sqrt(15.0)
    r5 = math.sqrt(5.0)
    harmonics = jnp.stack(
        [
            jnp.ones_like(ux),
            r3 * ux,
            r3 * uy,
            r3 * uz,
            r15 * ux * uy,
            r15 * uy * uz,
            0.5 * r5 * (2.0 * uz * uz - ux * ux - uy * uy),
            r15 * ux * uz,
            0.5 * r15 * (ux * ux - uy * uy),
        ],
        axis=0,
    )
    rows = jnp.concatenate([basis, envelope[None], harmonics], axis=0).reshape(18, K * atoms)
    return jnp.concatenate([rows, jnp.zeros((128 - 18, K * atoms), jnp.float32)], axis=0)


def _mm(a, b):
    return jnp.dot(a, b, preferred_element_type=jnp.float32)


def _sigmoid(v):
    return 0.5 + 0.5 * jnp.tanh(0.5 * v)


def _pair_kernel(
    rows_ref, centre_ref, geo_ref, basis_t_ref, split_t_ref, split_ref, update_t_ref,
    update_ref, tensor_t_ref, tensor_ref, basis_ref, energy_w_ref,
    grad_rows_ref, grad_centre_ref, grad_geo_ref, energy_ref,
    pre_s, hidden_s, mixed_s, damp_s, dlow_s, dgeo_s, env_s, denv_s,
):
    atoms = centre_ref.shape[1]
    f32 = jnp.float32
    bf16 = jnp.bfloat16
    span = SLOTS * atoms
    sub = lax.broadcasted_iota(jnp.int32, (128, span), 0)
    inv_root = 1.0 / math.sqrt(K)
    env_s[...] = jnp.zeros_like(env_s)
    denv_s[...] = jnp.zeros_like(denv_s)

    def block(k):
        return pl.ds(pl.multiple_of(k * span, span), span)

    def twice(v):
        return jnp.concatenate([v] * SLOTS, axis=1)

    def fold(v):
        total = v[:, :atoms]
        for slot in range(1, SLOTS):
            total = total + v[:, slot * atoms : (slot + 1) * atoms]
        return total

    def split_mm(weight, values):
        high = values.astype(bf16)
        low = (values - high.astype(f32)).astype(bf16)
        return _mm(weight, high) + _mm(weight, low)

    def first(k, carry):
        at = block(k)
        geo = geo_ref[:, at]
        radial = split_mm(basis_t_ref[...], geo)
        pre = twice(centre_ref[...]) + rows_ref[:, at].astype(f32) + radial
        envelope = geo[8:9, :]
        hidden = pre * _sigmoid(pre) * envelope
        pre_s[:, at] = pre
        hidden_s[:, at] = hidden
        mixed = _mm(split_t_ref[...], hidden.astype(bf16))
        mixed_s[:, at] = mixed
        for m in range(9):
            l = ORDER_OF[m]
            weight = mixed[3 * CH + l * CH : 3 * CH + (l + 1) * CH, :]
            env_s[m] = env_s[m] + fold(weight * (geo[9 + m : 10 + m, :] * inv_root))
        return carry

    lax.fori_loop(0, K // SLOTS, first, 0)

    def second(k, energy):
        at = block(k)
        geo = geo_ref[:, at]
        envelope = geo[8:9, :]
        hidden = hidden_s[:, at]
        mixed = mixed_s[:, at]
        parts = []
        totals = []
        for l in range(3):
            total = 0.0
            for m in GROUPS[l]:
                total = total + geo[9 + m : 10 + m, :] * twice(env_s[m])
            totals.append(total)
            parts.append(mixed[l * CH : (l + 1) * CH, :] * total)
        scalars = jnp.concatenate(parts, axis=0).astype(bf16)
        z = _mm(update_t_ref[...], hidden.astype(bf16)) + _mm(tensor_t_ref[...], scalars)
        gate = _sigmoid(z)
        update = z * gate
        readout = jnp.sum((hidden + update) * energy_w_ref[...], axis=0, keepdims=True)
        energy = energy + envelope * readout
        dz = (envelope * energy_w_ref[...]) * (gate * (1.0 + z * (1.0 - gate)))
        dz_low = dz.astype(bf16)
        dscalars = _mm(tensor_ref[...], dz_low).astype(bf16).astype(f32)
        dlow_s[:, at] = _mm(update_ref[...], dz_low)
        dgeo = jnp.where(sub == 8, readout, 0.0)
        for l in range(3):
            ds = dscalars[l * CH : (l + 1) * CH, :]
            damp_s[l * CH : (l + 1) * CH, at] = ds * totals[l]
            dtotal = ds * mixed[l * CH : (l + 1) * CH, :]
            for m in GROUPS[l]:
                dgeo = dgeo + jnp.where(
                    sub == 9 + m, jnp.sum(dtotal * twice(env_s[m]), axis=0, keepdims=True), 0.0
                )
                denv_s[m] = denv_s[m] + fold(dtotal * geo[9 + m : 10 + m, :])
        dgeo_s[:, at] = dgeo
        return energy

    energy = lax.fori_loop(0, K // SLOTS, second, jnp.zeros((1, span), f32))
    energy_ref[...] = jnp.broadcast_to(fold(energy), energy_ref.shape)

    def third(k, centre_grad):
        at = block(k)
        geo = geo_ref[:, at]
        envelope = geo[8:9, :]
        mixed = mixed_s[:, at]
        dgeo = dgeo_s[:, at]
        dweights = []
        for l in range(3):
            weight = mixed[3 * CH + l * CH : 3 * CH + (l + 1) * CH, :]
            dweight = 0.0
            for m in GROUPS[l]:
                denv = twice(denv_s[m])
                dweight = dweight + denv * (geo[9 + m : 10 + m, :] * inv_root)
                dgeo = dgeo + jnp.where(
                    sub == 9 + m,
                    jnp.sum(denv * weight, axis=0, keepdims=True) * inv_root,
                    0.0,
                )
            dweights.append(dweight)
        dmixed = jnp.concatenate([damp_s[:, at]] + dweights, axis=0).astype(bf16)
        dlow = dlow_s[:, at] + _mm(split_ref[...], dmixed)
        dhidden = envelope * energy_w_ref[...] + dlow
        pre = pre_s[:, at]
        sig = _sigmoid(pre)
        act = pre * sig
        dgeo = dgeo + jnp.where(sub == 8, jnp.sum(dhidden * act, axis=0, keepdims=True), 0.0)
        dpre = dhidden * envelope * (sig * (1.0 + pre * (1.0 - sig)))
        grad_rows_ref[:, at] = dpre
        dgeo = dgeo + split_mm(basis_ref[...], dpre)
        grad_geo_ref[:, at] = dgeo
        return centre_grad + fold(dpre)

    grad_centre_ref[...] = lax.fori_loop(
        0, K // SLOTS, third, jnp.zeros(grad_centre_ref.shape, f32)
    )


def pair_terms(rows_t, centre_t, geo, basis_proj, split_proj, update_proj, tensor_proj, energy_proj):
    width, pairs = rows_t.shape
    atoms = centre_t.shape[1]
    f32 = jnp.float32
    bf16 = jnp.bfloat16
    basis_pad = jnp.concatenate([basis_proj, jnp.zeros((128 - NB, width), bf16)], axis=0)
    vmem = pl.BlockSpec(memory_space=pltpu.VMEM)
    outs = pl.pallas_call(
        _pair_kernel,
        out_shape=(
            jax.ShapeDtypeStruct((width, pairs), f32),
            jax.ShapeDtypeStruct((width, atoms), f32),
            jax.ShapeDtypeStruct((128, pairs), f32),
            jax.ShapeDtypeStruct((8, atoms), f32),
        ),
        in_specs=[vmem] * 12,
        out_specs=(vmem, vmem, vmem, vmem),
        scratch_shapes=[
            pltpu.VMEM((width, pairs), f32),
            pltpu.VMEM((width, pairs), f32),
            pltpu.VMEM((6 * CH, pairs), f32),
            pltpu.VMEM((3 * CH, pairs), f32),
            pltpu.VMEM((width, pairs), f32),
            pltpu.VMEM((128, pairs), f32),
            pltpu.VMEM((9, CH, atoms), f32),
            pltpu.VMEM((9, CH, atoms), f32),
        ],
        compiler_params=pltpu.CompilerParams(vmem_limit_bytes=60 * 1024 * 1024),
        cost_estimate=pl.CostEstimate(
            flops=int(24 * pairs * width * 128),
            transcendentals=int(3 * pairs * width),
            bytes_accessed=int(16 * pairs * width),
        ),
    )(
        rows_t,
        centre_t,
        geo,
        basis_pad.T,
        split_proj.T,
        split_proj,
        update_proj.T,
        update_proj,
        tensor_proj.T,
        tensor_proj,
        basis_pad,
        jnp.broadcast_to(energy_proj.astype(f32)[:, None], (width, SLOTS * atoms)),
    )
    grad_rows_t, grad_centre_t, grad_geo, energy = outs
    return grad_rows_t, grad_centre_t, grad_geo, energy[0]


def shards(
    latent,
    positions,
    species,
    send_list,
    neighbour,
    atom_count,
    centre_proj,
    neigh_proj,
    centre_table,
    neigh_table,
    basis_proj,
    split_proj,
    update_proj,
    tensor_proj,
    energy_proj,
    species_shift,
):
    atoms, width = latent.shape
    extra = 128
    face_x = atoms // 8
    face_y = atoms // 2
    face_z = atoms // 8
    lengths = [face_x, face_x, face_y, face_y, face_z, face_z]
    starts = [
        0,
        face_x,
        2 * face_x,
        2 * face_x + face_y,
        2 * face_x + 2 * face_y,
        2 * face_x + 2 * face_y + face_z,
    ]
    kinds = jnp.arange(NSPEC, dtype=jnp.int32)

    def lookup(codes, table):
        onehot = (codes[:, None] == kinds[None, :]).astype(jnp.float32)
        return jnp.dot(onehot, table, precision=lax.Precision.HIGHEST)

    def project(rows, codes, weight, table):
        return (
            jnp.dot(rows, weight, preferred_element_type=jnp.float32) + lookup(codes, table)
        ).astype(jnp.bfloat16)

    def spread_cols(onehot, values):
        high = values.astype(jnp.bfloat16)
        low = (values - high.astype(jnp.float32)).astype(jnp.bfloat16)
        return jnp.einsum(
            "wn,nr->wr", high, onehot, preferred_element_type=jnp.float32
        ) + jnp.einsum("wn,nr->wr", low, onehot, preferred_element_type=jnp.float32)

    def spread(onehot, values):
        high = values.astype(jnp.bfloat16)
        low = (values - high.astype(jnp.float32)).astype(jnp.bfloat16)
        return jnp.einsum(
            "nr,nw->rw", onehot, high, preferred_element_type=jnp.float32
        ) + jnp.einsum("nr,nw->rw", onehot, low, preferred_element_type=jnp.float32)

    proj_c = project(latent, species, centre_proj, centre_table)
    proj_n = project(latent, species, neigh_proj, neigh_table)
    send_rows = send_list[0]
    coarse = positions // 16
    fine = positions - coarse * 16
    coord_cols = jnp.concatenate([coarse, fine], axis=0).T.astype(jnp.bfloat16)
    table = jnp.concatenate(
        [proj_n, coord_cols, jnp.zeros((atoms, extra - 6), jnp.bfloat16)], axis=1
    )
    shifts = [(0, -LX_FIX), (0, LX_FIX), (1, -LY_FIX), (1, LY_FIX), (2, -LZ_FIX), (2, LZ_FIX)]
    sections = (("gx", (1, 0)), ("gy", (3, 2)), ("gz", (5, 4)))
    pickers = {}
    base_rows = []
    for section, (axis, segs) in enumerate(sections):
        rows_now = table.shape[0]
        base_rows.append(rows_now)
        parts = [table]
        for number, (segment, direction) in enumerate(((segs[0], 1), (segs[1], -1))):
            picked = send_rows[starts[segment] : starts[segment] + lengths[segment]]
            onehot = (
                picked[:, None] == jnp.arange(rows_now, dtype=jnp.int32)[None, :]
            ).astype(jnp.bfloat16)
            pickers[segment] = onehot
            if section == 0:
                chosen = jnp.dot(onehot, latent, preferred_element_type=jnp.float32)
                kinds_of = jnp.dot(
                    onehot, species.astype(jnp.bfloat16)[:, None], preferred_element_type=jnp.float32
                )[:, 0].astype(jnp.int32)
                out = jnp.concatenate(
                    [
                        project(chosen.astype(jnp.bfloat16), kinds_of, neigh_proj, neigh_table),
                        jnp.dot(
                            onehot, table[:, width:], preferred_element_type=jnp.float32
                        ).astype(jnp.bfloat16),
                    ],
                    axis=1,
                )
            else:
                out = jnp.dot(onehot, table, preferred_element_type=jnp.float32).astype(
                    jnp.bfloat16
                )
            got = passed_along(out, axis, direction)
            coord_axis, offset = shifts[2 * section + number]
            columns = jnp.arange(width + extra, dtype=jnp.int32)[None, :]
            shift = jnp.where(columns == width + coord_axis, offset // 16, 0).astype(jnp.bfloat16)
            parts.append(got + shift)
        table = jnp.concatenate(parts, axis=0)
    total_rows = table.shape[0]
    neighbour = neighbour.reshape(atoms, K).T.reshape(-1)
    select = (neighbour[:, None] == jnp.arange(total_rows, dtype=jnp.int32)[None, :]).astype(
        jnp.bfloat16
    )
    gathered = jnp.einsum("tw,pt->wp", table, select, preferred_element_type=jnp.float32)
    neigh_cols = gathered[:width].astype(jnp.bfloat16)
    coords_n = gathered[width : width + 3] * 16.0 + gathered[width + 3 : width + 6]
    delta = (coords_n.reshape(3, K, atoms) - positions.astype(jnp.float32)[:, None, :]) * (
        1.0 / 64.0
    )
    live = (jnp.arange(atoms) < atom_count[0]).astype(jnp.float32)
    valid_pair = live[None, :]

    geo, geo_pull = jax.vjp(lambda d: geometry(d, valid_pair), delta)
    grad_neigh, grad_centre, grad_geo, atom_energy = pair_terms(
        neigh_cols,
        proj_c.astype(jnp.float32).T,
        geo,
        basis_proj,
        split_proj,
        update_proj,
        tensor_proj,
        energy_proj,
    )
    (grad_delta,) = geo_pull(grad_geo)
    pairs = grad_neigh.shape[1]
    grads = jnp.concatenate(
        [
            grad_neigh,
            grad_delta.reshape(3, pairs),
            jnp.zeros((extra - 3, pairs), jnp.float32),
        ],
        axis=0,
    )
    sums = spread_cols(select, grads).T
    own_pos = grad_delta.sum(axis=1)
    sums = sums - jnp.pad(own_pos.T, ((0, total_rows - atoms), (width, extra - 3)))
    for section in (2, 1, 0):
        axis, segs = sections[section]
        rows_now = base_rows[section]
        first = atoms + starts[2 * section]
        second = atoms + starts[2 * section + 1]
        back_first = passed_along(sums[first : first + lengths[2 * section]], axis, -1)
        back_second = passed_along(sums[second : second + lengths[2 * section + 1]], axis, 1)
        sums = (
            sums[:rows_now]
            + spread(pickers[segs[0]], back_first)
            + spread(pickers[segs[1]], back_second)
        )
    back_neigh = neigh_proj.astype(jnp.float32).T
    back_centre = centre_proj.astype(jnp.float32).T
    latent_grad = jnp.dot(grad_centre.T, back_centre, precision=lax.Precision.HIGHEST)
    latent_grad = latent_grad + jnp.dot(
        sums[:, :width], back_neigh, precision=lax.Precision.HIGHEST
    )
    forces = -sums[:, width : width + 3].T
    energies = live * (lookup(species, species_shift[:, None])[:, 0] + atom_energy)
    return (energies, forces, latent_grad)


def solution(mesh):
    in_specs = (
        P(("gx", "gy", "gz"), None),
        P(None, ("gx", "gy", "gz")),
        P(("gx", "gy", "gz")),
        P(("gx", "gy", "gz"), None),
        P(("gx", "gy", "gz")),
        P(("gx", "gy", "gz")),
        P(),
        P(),
        P(),
        P(),
        P(),
        P(),
        P(),
        P(),
        P(),
        P(),
    )
    out_specs = (P(("gx", "gy", "gz")), P(None, ("gx", "gy", "gz")), P(("gx", "gy", "gz"), None))
    return jax.shard_map(shards, mesh=mesh, in_specs=in_specs, out_specs=out_specs, check_vma=False)
```

```python
import math

import jax
import jax.numpy as jnp
from jax import lax
from jax.experimental import pallas as pl
from jax.experimental.pallas import tpu as pltpu
from jax.sharding import PartitionSpec as P

K = 8
CH = 64
NB = 8
NSPEC = 5
LX_FIX = 1024
LY_FIX = 512
LZ_FIX = 1280


CUTOFF = 6.0
SOFTEN = 0.25


def shortened(shard):
    return jax.tree.map(lambda a: a.astype(jnp.bfloat16) if a.dtype == jnp.float32 else a, shard)


def passed_along(block, axis, distance):
    devices = range(lax.axis_size(axis))
    route = [((i - distance) % len(devices), i) for i in devices]
    return lax.ppermute(block, axis, route)


def by_order(values):
    rest = values.shape[1:]
    return jnp.concatenate(
        [
            values[0:1],
            jnp.broadcast_to(values[1:2], (3,) + rest),
            jnp.broadcast_to(values[2:3], (5,) + rest),
        ],
        axis=0,
    )


SLOTS = 8
ORDER_OF = (0, 1, 1, 1, 2, 2, 2, 2, 2)
GROUPS = ((0,), (1, 2, 3), (4, 5, 6, 7, 8))


def geometry(delta, valid_pair):
    atoms = delta.shape[2]
    radius = jnp.sqrt(jnp.sum(delta * delta, axis=0) + SOFTEN)
    unit = delta / radius
    ratio = radius / CUTOFF
    envelope = jnp.where(ratio < 1.0, (1.0 - ratio * ratio) ** 2, 0.0) * valid_pair
    orders = jnp.arange(1, NB + 1).astype(jnp.float32)
    basis = (
        jnp.sin(orders[:, None, None] * (math.pi / CUTOFF) * radius[None])
        * (envelope / radius)[None]
    )
    ux, uy, uz = unit[0], unit[1], unit[2]
    r3 = math.sqrt(3.0)
    r15 = math.sqrt(15.0)
    r5 = math.sqrt(5.0)
    harmonics = jnp.stack(
        [
            jnp.ones_like(ux),
            r3 * ux,
            r3 * uy,
            r3 * uz,
            r15 * ux * uy,
            r15 * uy * uz,
            0.5 * r5 * (2.0 * uz * uz - ux * ux - uy * uy),
            r15 * ux * uz,
            0.5 * r15 * (ux * ux - uy * uy),
        ],
        axis=0,
    )
    rows = jnp.concatenate([basis, envelope[None], harmonics], axis=0).reshape(18, K * atoms)
    return jnp.concatenate([rows, jnp.zeros((128 - 18, K * atoms), jnp.float32)], axis=0)


def _mm(a, b):
    return jnp.dot(a, b, preferred_element_type=jnp.float32)


def _sigmoid(v):
    return 0.5 + 0.5 * jnp.tanh(0.5 * v)


def _pair_kernel(
    rows_ref, centre_ref, geo_ref, basis_t_ref, split_t_ref, split_ref, update_t_ref,
    update_ref, tensor_t_ref, tensor_ref, basis_ref, energy_w_ref,
    grad_rows_ref, grad_centre_ref, grad_geo_ref, energy_ref,
    pre_s, hidden_s, mixed_s, damp_s, dlow_s, dgeo_s, env_s, denv_s,
):
    atoms = centre_ref.shape[1]
    f32 = jnp.float32
    bf16 = jnp.bfloat16
    span = SLOTS * atoms
    sub = lax.broadcasted_iota(jnp.int32, (128, span), 0)
    inv_root = 1.0 / math.sqrt(K)
    env_s[...] = jnp.zeros_like(env_s)
    denv_s[...] = jnp.zeros_like(denv_s)

    def block(k):
        return pl.ds(pl.multiple_of(k * span, span), span)

    def twice(v):
        return jnp.concatenate([v] * SLOTS, axis=1)

    def fold(v):
        total = v[:, :atoms]
        for slot in range(1, SLOTS):
            total = total + v[:, slot * atoms : (slot + 1) * atoms]
        return total

    def split_mm(weight, values):
        high = values.astype(bf16)
        low = (values - high.astype(f32)).astype(bf16)
        return _mm(weight, high) + _mm(weight, low)

    def first(k, carry):
        at = block(k)
        geo = geo_ref[:, at]
        radial = split_mm(basis_t_ref[...], geo)
        pre = twice(centre_ref[...]) + rows_ref[:, at].astype(f32) + radial
        envelope = geo[8:9, :]
        hidden = pre * _sigmoid(pre) * envelope
        pre_s[:, at] = pre
        hidden_s[:, at] = hidden
        mixed = _mm(split_t_ref[...], hidden.astype(bf16))
        mixed_s[:, at] = mixed
        for m in range(9):
            l = ORDER_OF[m]
            weight = mixed[3 * CH + l * CH : 3 * CH + (l + 1) * CH, :]
            env_s[m] = env_s[m] + fold(weight * (geo[9 + m : 10 + m, :] * inv_root))
        return carry

    lax.fori_loop(0, K // SLOTS, first, 0)

    def second(k, energy):
        at = block(k)
        geo = geo_ref[:, at]
        envelope = geo[8:9, :]
        hidden = hidden_s[:, at]
        mixed = mixed_s[:, at]
        parts = []
        totals = []
        for l in range(3):
            total = 0.0
            for m in GROUPS[l]:
                total = total + geo[9 + m : 10 + m, :] * twice(env_s[m])
            totals.append(total)
            parts.append(mixed[l * CH : (l + 1) * CH, :] * total)
        scalars = jnp.concatenate(parts, axis=0).astype(bf16)
        z = _mm(update_t_ref[...], hidden.astype(bf16)) + _mm(tensor_t_ref[...], scalars)
        gate = _sigmoid(z)
        update = z * gate
        readout = jnp.sum((hidden + update) * energy_w_ref[...], axis=0, keepdims=True)
        energy = energy + envelope * readout
        dz = (envelope * energy_w_ref[...]) * (gate * (1.0 + z * (1.0 - gate)))
        dz_low = dz.astype(bf16)
        dscalars = _mm(tensor_ref[...], dz_low).astype(bf16).astype(f32)
        dlow_s[:, at] = _mm(update_ref[...], dz_low)
        dgeo = jnp.where(sub == 8, readout, 0.0)
        for l in range(3):
            ds = dscalars[l * CH : (l + 1) * CH, :]
            damp_s[l * CH : (l + 1) * CH, at] = ds * totals[l]
            dtotal = ds * mixed[l * CH : (l + 1) * CH, :]
            for m in GROUPS[l]:
                dgeo = dgeo + jnp.where(
                    sub == 9 + m, jnp.sum(dtotal * twice(env_s[m]), axis=0, keepdims=True), 0.0
                )
                denv_s[m] = denv_s[m] + fold(dtotal * geo[9 + m : 10 + m, :])
        dgeo_s[:, at] = dgeo
        return energy

    energy = lax.fori_loop(0, K // SLOTS, second, jnp.zeros((1, span), f32))
    energy_ref[...] = jnp.broadcast_to(fold(energy), energy_ref.shape)

    def third(k, centre_grad):
        at = block(k)
        geo = geo_ref[:, at]
        envelope = geo[8:9, :]
        mixed = mixed_s[:, at]
        dgeo = dgeo_s[:, at]
        dweights = []
        for l in range(3):
            weight = mixed[3 * CH + l * CH : 3 * CH + (l + 1) * CH, :]
            dweight = 0.0
            for m in GROUPS[l]:
                denv = twice(denv_s[m])
                dweight = dweight + denv * (geo[9 + m : 10 + m, :] * inv_root)
                dgeo = dgeo + jnp.where(
                    sub == 9 + m,
                    jnp.sum(denv * weight, axis=0, keepdims=True) * inv_root,
                    0.0,
                )
            dweights.append(dweight)
        dmixed = jnp.concatenate([damp_s[:, at]] + dweights, axis=0).astype(bf16)
        dlow = dlow_s[:, at] + _mm(split_ref[...], dmixed)
        dhidden = envelope * energy_w_ref[...] + dlow
        pre = pre_s[:, at]
        sig = _sigmoid(pre)
        act = pre * sig
        dgeo = dgeo + jnp.where(sub == 8, jnp.sum(dhidden * act, axis=0, keepdims=True), 0.0)
        dpre = dhidden * envelope * (sig * (1.0 + pre * (1.0 - sig)))
        grad_rows_ref[:, at] = dpre
        dgeo = dgeo + split_mm(basis_ref[...], dpre)
        grad_geo_ref[:, at] = dgeo
        return centre_grad + fold(dpre)

    grad_centre_ref[...] = lax.fori_loop(
        0, K // SLOTS, third, jnp.zeros(grad_centre_ref.shape, f32)
    )


def pair_terms(rows_t, centre_t, geo, basis_proj, split_proj, update_proj, tensor_proj, energy_proj):
    width, pairs = rows_t.shape
    atoms = centre_t.shape[1]
    f32 = jnp.float32
    bf16 = jnp.bfloat16
    basis_pad = jnp.concatenate([basis_proj, jnp.zeros((128 - NB, width), bf16)], axis=0)
    vmem = pl.BlockSpec(memory_space=pltpu.VMEM)
    outs = pl.pallas_call(
        _pair_kernel,
        out_shape=(
            jax.ShapeDtypeStruct((width, pairs), f32),
            jax.ShapeDtypeStruct((width, atoms), f32),
            jax.ShapeDtypeStruct((128, pairs), f32),
            jax.ShapeDtypeStruct((8, atoms), f32),
        ),
        in_specs=[vmem] * 12,
        out_specs=(vmem, vmem, vmem, vmem),
        scratch_shapes=[
            pltpu.VMEM((width, pairs), f32),
            pltpu.VMEM((width, pairs), f32),
            pltpu.VMEM((6 * CH, pairs), f32),
            pltpu.VMEM((3 * CH, pairs), f32),
            pltpu.VMEM((width, pairs), f32),
            pltpu.VMEM((128, pairs), f32),
            pltpu.VMEM((9, CH, atoms), f32),
            pltpu.VMEM((9, CH, atoms), f32),
        ],
        compiler_params=pltpu.CompilerParams(vmem_limit_bytes=60 * 1024 * 1024),
        cost_estimate=pl.CostEstimate(
            flops=int(24 * pairs * width * 128),
            transcendentals=int(3 * pairs * width),
            bytes_accessed=int(16 * pairs * width),
        ),
    )(
        rows_t,
        centre_t,
        geo,
        basis_pad.T,
        split_proj.T,
        split_proj,
        update_proj.T,
        update_proj,
        tensor_proj.T,
        tensor_proj,
        basis_pad,
        jnp.broadcast_to(energy_proj.astype(f32)[:, None], (width, SLOTS * atoms)),
    )
    grad_rows_t, grad_centre_t, grad_geo, energy = outs
    return grad_rows_t, grad_centre_t, grad_geo, energy[0]


def shards(
    latent,
    positions,
    species,
    send_list,
    neighbour,
    atom_count,
    centre_proj,
    neigh_proj,
    centre_table,
    neigh_table,
    basis_proj,
    split_proj,
    update_proj,
    tensor_proj,
    energy_proj,
    species_shift,
):
    atoms, width = latent.shape
    extra = 128
    face_x = atoms // 8
    face_y = atoms // 2
    face_z = atoms // 8
    lengths = [face_x, face_x, face_y, face_y, face_z, face_z]
    starts = [
        0,
        face_x,
        2 * face_x,
        2 * face_x + face_y,
        2 * face_x + 2 * face_y,
        2 * face_x + 2 * face_y + face_z,
    ]
    kinds = jnp.arange(NSPEC, dtype=jnp.int32)

    def lookup(codes, table):
        onehot = (codes[:, None] == kinds[None, :]).astype(jnp.float32)
        return jnp.dot(onehot, table, precision=lax.Precision.HIGHEST)

    def project(rows, codes, weight, table):
        return (
            jnp.dot(rows, weight, preferred_element_type=jnp.float32) + lookup(codes, table)
        ).astype(jnp.bfloat16)

    def spread_cols(onehot, values):
        return jnp.einsum(
            "wn,nr->wr", values.astype(jnp.bfloat16), onehot, preferred_element_type=jnp.float32
        )

    def spread(onehot, values):
        return jnp.einsum(
            "nr,nw->rw", onehot, values.astype(jnp.bfloat16), preferred_element_type=jnp.float32
        )

    proj_c = project(latent, species, centre_proj, centre_table)
    proj_n = project(latent, species, neigh_proj, neigh_table)
    send_rows = send_list[0]
    coarse = positions // 16
    fine = positions - coarse * 16
    coord_cols = jnp.concatenate([coarse, fine], axis=0).T.astype(jnp.bfloat16)
    table = jnp.concatenate(
        [proj_n, coord_cols, jnp.zeros((atoms, extra - 6), jnp.bfloat16)], axis=1
    )
    shifts = [(0, -LX_FIX), (0, LX_FIX), (1, -LY_FIX), (1, LY_FIX), (2, -LZ_FIX), (2, LZ_FIX)]
    sections = (("gx", (1, 0)), ("gy", (3, 2)), ("gz", (5, 4)))
    pickers = {}
    base_rows = []
    for section, (axis, segs) in enumerate(sections):
        rows_now = table.shape[0]
        base_rows.append(rows_now)
        parts = [table]
        for number, (segment, direction) in enumerate(((segs[0], 1), (segs[1], -1))):
            picked = send_rows[starts[segment] : starts[segment] + lengths[segment]]
            onehot = (
                picked[:, None] == jnp.arange(rows_now, dtype=jnp.int32)[None, :]
            ).astype(jnp.bfloat16)
            pickers[segment] = onehot
            out = jnp.dot(onehot, table, preferred_element_type=jnp.float32).astype(jnp.bfloat16)
            got = passed_along(out, axis, direction)
            coord_axis, offset = shifts[2 * section + number]
            columns = jnp.arange(width + extra, dtype=jnp.int32)[None, :]
            shift = jnp.where(columns == width + coord_axis, offset // 16, 0).astype(jnp.bfloat16)
            parts.append(got + shift)
        table = jnp.concatenate(parts, axis=0)
    total_rows = table.shape[0]
    neighbour = neighbour.reshape(atoms, K).T.reshape(-1)
    select = (neighbour[:, None] == jnp.arange(total_rows, dtype=jnp.int32)[None, :]).astype(
        jnp.bfloat16
    )
    gathered = jnp.einsum("tw,pt->wp", table, select, preferred_element_type=jnp.float32)
    neigh_cols = gathered[:width].astype(jnp.bfloat16)
    coords_n = gathered[width : width + 3] * 16.0 + gathered[width + 3 : width + 6]
    delta = (coords_n.reshape(3, K, atoms) - positions.astype(jnp.float32)[:, None, :]) * (
        1.0 / 64.0
    )
    live = (jnp.arange(atoms) < atom_count[0]).astype(jnp.float32)
    valid_pair = live[None, :]

    geo, geo_pull = jax.vjp(lambda d: geometry(d, valid_pair), delta)
    grad_neigh, grad_centre, grad_geo, atom_energy = pair_terms(
        neigh_cols,
        proj_c.astype(jnp.float32).T,
        geo,
        basis_proj,
        split_proj,
        update_proj,
        tensor_proj,
        energy_proj,
    )
    (grad_delta,) = geo_pull(grad_geo)
    pairs = grad_neigh.shape[1]
    grads = jnp.concatenate(
        [
            grad_neigh,
            grad_delta.reshape(3, pairs),
            jnp.zeros((extra - 3, pairs), jnp.float32),
        ],
        axis=0,
    )
    sums = spread_cols(select, grads).T
    own_pos = grad_delta.sum(axis=1)
    sums = sums - jnp.pad(own_pos.T, ((0, total_rows - atoms), (width, extra - 3)))
    for section in (2, 1, 0):
        axis, segs = sections[section]
        rows_now = base_rows[section]
        first = atoms + starts[2 * section]
        second = atoms + starts[2 * section + 1]
        back_first = passed_along(sums[first : first + lengths[2 * section]], axis, -1)
        back_second = passed_along(sums[second : second + lengths[2 * section + 1]], axis, 1)
        sums = (
            sums[:rows_now]
            + spread(pickers[segs[0]], back_first)
            + spread(pickers[segs[1]], back_second)
        )
    back_neigh = neigh_proj.astype(jnp.float32).T
    back_centre = centre_proj.astype(jnp.float32).T
    latent_grad = jnp.dot(grad_centre.T, back_centre, precision=lax.Precision.HIGHEST)
    latent_grad = latent_grad + jnp.dot(
        sums[:, :width], back_neigh, precision=lax.Precision.HIGHEST
    )
    forces = -sums[:, width : width + 3].T
    energies = live * (lookup(species, species_shift[:, None])[:, 0] + atom_energy)
    return (energies, forces, latent_grad)


def solution(mesh):
    in_specs = (
        P(("gx", "gy", "gz"), None),
        P(None, ("gx", "gy", "gz")),
        P(("gx", "gy", "gz")),
        P(("gx", "gy", "gz"), None),
        P(("gx", "gy", "gz")),
        P(("gx", "gy", "gz")),
        P(),
        P(),
        P(),
        P(),
        P(),
        P(),
        P(),
        P(),
        P(),
        P(),
    )
    out_specs = (P(("gx", "gy", "gz")), P(None, ("gx", "gy", "gz")), P(("gx", "gy", "gz"), None))
    return jax.shard_map(shards, mesh=mesh, in_specs=in_specs, out_specs=out_specs, check_vma=False)
```

```python
import math

import jax
import jax.numpy as jnp
from jax import lax
from jax.experimental import pallas as pl
from jax.experimental.pallas import tpu as pltpu
from jax.sharding import PartitionSpec as P

K = 8
CH = 64
NB = 8
NSPEC = 5
LX_FIX = 1024
LY_FIX = 512
LZ_FIX = 1280


CUTOFF = 6.0
SOFTEN = 0.25


def shortened(shard):
    return jax.tree.map(lambda a: a.astype(jnp.bfloat16) if a.dtype == jnp.float32 else a, shard)


def passed_along(block, axis, distance):
    devices = range(lax.axis_size(axis))
    route = [((i - distance) % len(devices), i) for i in devices]
    return lax.ppermute(block, axis, route)


def by_order(values):
    rest = values.shape[1:]
    return jnp.concatenate(
        [
            values[0:1],
            jnp.broadcast_to(values[1:2], (3,) + rest),
            jnp.broadcast_to(values[2:3], (5,) + rest),
        ],
        axis=0,
    )


SLOTS = 8
ORDER_OF = (0, 1, 1, 1, 2, 2, 2, 2, 2)
GROUPS = ((0,), (1, 2, 3), (4, 5, 6, 7, 8))


def geometry(delta, valid_pair):
    atoms = delta.shape[2]
    radius = jnp.sqrt(jnp.sum(delta * delta, axis=0) + SOFTEN)
    unit = delta / radius
    ratio = radius / CUTOFF
    envelope = jnp.where(ratio < 1.0, (1.0 - ratio * ratio) ** 2, 0.0) * valid_pair
    orders = jnp.arange(1, NB + 1).astype(jnp.float32)
    basis = (
        jnp.sin(orders[:, None, None] * (math.pi / CUTOFF) * radius[None])
        * (envelope / radius)[None]
    )
    ux, uy, uz = unit[0], unit[1], unit[2]
    r3 = math.sqrt(3.0)
    r15 = math.sqrt(15.0)
    r5 = math.sqrt(5.0)
    harmonics = jnp.stack(
        [
            jnp.ones_like(ux),
            r3 * ux,
            r3 * uy,
            r3 * uz,
            r15 * ux * uy,
            r15 * uy * uz,
            0.5 * r5 * (2.0 * uz * uz - ux * ux - uy * uy),
            r15 * ux * uz,
            0.5 * r15 * (ux * ux - uy * uy),
        ],
        axis=0,
    )
    rows = jnp.concatenate([basis, envelope[None], harmonics], axis=0).reshape(18, K * atoms)
    return jnp.concatenate([rows, jnp.zeros((128 - 18, K * atoms), jnp.float32)], axis=0)


def _mm(a, b):
    return jnp.dot(a, b, preferred_element_type=jnp.float32)


def _sigmoid(v):
    return 0.5 + 0.5 * jnp.tanh(0.5 * v)


def _pair_kernel(
    rows_ref, centre_ref, geo_ref, basis_t_ref, split_t_ref, split_ref, update_t_ref,
    update_ref, tensor_t_ref, tensor_ref, basis_ref, energy_w_ref,
    grad_rows_ref, grad_centre_ref, grad_geo_ref, energy_ref,
    pre_s, hidden_s, mixed_s, damp_s, dlow_s, dgeo_s, env_s, denv_s,
):
    atoms = centre_ref.shape[1]
    f32 = jnp.float32
    bf16 = jnp.bfloat16
    span = SLOTS * atoms
    sub = lax.broadcasted_iota(jnp.int32, (128, span), 0)
    inv_root = 1.0 / math.sqrt(K)
    env_s[...] = jnp.zeros_like(env_s)
    denv_s[...] = jnp.zeros_like(denv_s)

    def block(k):
        return pl.ds(pl.multiple_of(k * span, span), span)

    def twice(v):
        return jnp.concatenate([v] * SLOTS, axis=1)

    def fold(v):
        total = v[:, :atoms]
        for slot in range(1, SLOTS):
            total = total + v[:, slot * atoms : (slot + 1) * atoms]
        return total

    def split_mm(weight, values):
        high = values.astype(bf16)
        low = (values - high.astype(f32)).astype(bf16)
        return _mm(weight, high) + _mm(weight, low)

    def first(k, carry):
        at = block(k)
        geo = geo_ref[:, at]
        radial = split_mm(basis_t_ref[...], geo)
        pre = twice(centre_ref[...]) + rows_ref[:, at].astype(f32) + radial
        envelope = geo[8:9, :]
        hidden = pre * _sigmoid(pre) * envelope
        pre_s[:, at] = pre
        hidden_s[:, at] = hidden
        mixed = _mm(split_t_ref[...], hidden.astype(bf16))
        mixed_s[:, at] = mixed
        for m in range(9):
            l = ORDER_OF[m]
            weight = mixed[3 * CH + l * CH : 3 * CH + (l + 1) * CH, :]
            env_s[m] = env_s[m] + fold(weight * (geo[9 + m : 10 + m, :] * inv_root))
        return carry

    lax.fori_loop(0, K // SLOTS, first, 0)

    def second(k, energy):
        at = block(k)
        geo = geo_ref[:, at]
        envelope = geo[8:9, :]
        hidden = hidden_s[:, at]
        mixed = mixed_s[:, at]
        parts = []
        totals = []
        for l in range(3):
            total = 0.0
            for m in GROUPS[l]:
                total = total + geo[9 + m : 10 + m, :] * twice(env_s[m])
            totals.append(total)
            parts.append(mixed[l * CH : (l + 1) * CH, :] * total)
        scalars = jnp.concatenate(parts, axis=0).astype(bf16)
        z = _mm(update_t_ref[...], hidden.astype(bf16)) + _mm(tensor_t_ref[...], scalars)
        gate = _sigmoid(z)
        update = z * gate
        readout = jnp.sum((hidden + update) * energy_w_ref[...], axis=0, keepdims=True)
        energy = energy + envelope * readout
        dz = (envelope * energy_w_ref[...]) * (gate * (1.0 + z * (1.0 - gate)))
        dz_low = dz.astype(bf16)
        dscalars = _mm(tensor_ref[...], dz_low).astype(bf16).astype(f32)
        dlow_s[:, at] = _mm(update_ref[...], dz_low)
        dgeo = jnp.where(sub == 8, readout, 0.0)
        for l in range(3):
            ds = dscalars[l * CH : (l + 1) * CH, :]
            damp_s[l * CH : (l + 1) * CH, at] = ds * totals[l]
            dtotal = ds * mixed[l * CH : (l + 1) * CH, :]
            for m in GROUPS[l]:
                dgeo = dgeo + jnp.where(
                    sub == 9 + m, jnp.sum(dtotal * twice(env_s[m]), axis=0, keepdims=True), 0.0
                )
                denv_s[m] = denv_s[m] + fold(dtotal * geo[9 + m : 10 + m, :])
        dgeo_s[:, at] = dgeo
        return energy

    energy = lax.fori_loop(0, K // SLOTS, second, jnp.zeros((1, span), f32))
    energy_ref[...] = jnp.broadcast_to(fold(energy), energy_ref.shape)

    def third(k, centre_grad):
        at = block(k)
        geo = geo_ref[:, at]
        envelope = geo[8:9, :]
        mixed = mixed_s[:, at]
        dgeo = dgeo_s[:, at]
        dweights = []
        for l in range(3):
            weight = mixed[3 * CH + l * CH : 3 * CH + (l + 1) * CH, :]
            dweight = 0.0
            for m in GROUPS[l]:
                denv = twice(denv_s[m])
                dweight = dweight + denv * (geo[9 + m : 10 + m, :] * inv_root)
                dgeo = dgeo + jnp.where(
                    sub == 9 + m,
                    jnp.sum(denv * weight, axis=0, keepdims=True) * inv_root,
                    0.0,
                )
            dweights.append(dweight)
        dmixed = jnp.concatenate([damp_s[:, at]] + dweights, axis=0).astype(bf16)
        dlow = dlow_s[:, at] + _mm(split_ref[...], dmixed)
        dhidden = envelope * energy_w_ref[...] + dlow
        pre = pre_s[:, at]
        sig = _sigmoid(pre)
        act = pre * sig
        dgeo = dgeo + jnp.where(sub == 8, jnp.sum(dhidden * act, axis=0, keepdims=True), 0.0)
        dpre = dhidden * envelope * (sig * (1.0 + pre * (1.0 - sig)))
        grad_rows_ref[:, at] = dpre
        dgeo = dgeo + split_mm(basis_ref[...], dpre)
        grad_geo_ref[:, at] = dgeo
        return centre_grad + fold(dpre)

    grad_centre_ref[...] = lax.fori_loop(
        0, K // SLOTS, third, jnp.zeros(grad_centre_ref.shape, f32)
    )


def pair_terms(rows_t, centre_t, geo, basis_proj, split_proj, update_proj, tensor_proj, energy_proj):
    width, pairs = rows_t.shape
    atoms = centre_t.shape[1]
    f32 = jnp.float32
    bf16 = jnp.bfloat16
    basis_pad = jnp.concatenate([basis_proj, jnp.zeros((128 - NB, width), bf16)], axis=0)
    vmem = pl.BlockSpec(memory_space=pltpu.VMEM)
    outs = pl.pallas_call(
        _pair_kernel,
        out_shape=(
            jax.ShapeDtypeStruct((width, pairs), f32),
            jax.ShapeDtypeStruct((width, atoms), f32),
            jax.ShapeDtypeStruct((128, pairs), f32),
            jax.ShapeDtypeStruct((8, atoms), f32),
        ),
        in_specs=[vmem] * 12,
        out_specs=(vmem, vmem, vmem, vmem),
        scratch_shapes=[
            pltpu.VMEM((width, pairs), f32),
            pltpu.VMEM((width, pairs), f32),
            pltpu.VMEM((6 * CH, pairs), f32),
            pltpu.VMEM((3 * CH, pairs), f32),
            pltpu.VMEM((width, pairs), f32),
            pltpu.VMEM((128, pairs), f32),
            pltpu.VMEM((9, CH, atoms), f32),
            pltpu.VMEM((9, CH, atoms), f32),
        ],
        compiler_params=pltpu.CompilerParams(vmem_limit_bytes=60 * 1024 * 1024),
        cost_estimate=pl.CostEstimate(
            flops=int(24 * pairs * width * 128),
            transcendentals=int(3 * pairs * width),
            bytes_accessed=int(16 * pairs * width),
        ),
    )(
        rows_t,
        centre_t,
        geo,
        basis_pad.T,
        split_proj.T,
        split_proj,
        update_proj.T,
        update_proj,
        tensor_proj.T,
        tensor_proj,
        basis_pad,
        jnp.broadcast_to(energy_proj.astype(f32)[:, None], (width, SLOTS * atoms)),
    )
    grad_rows_t, grad_centre_t, grad_geo, energy = outs
    return grad_rows_t, grad_centre_t, grad_geo, energy[0]


def shards(
    latent,
    positions,
    species,
    send_list,
    neighbour,
    atom_count,
    centre_proj,
    neigh_proj,
    centre_table,
    neigh_table,
    basis_proj,
    split_proj,
    update_proj,
    tensor_proj,
    energy_proj,
    species_shift,
):
    atoms, width = latent.shape
    extra = 128
    face_x = atoms // 8
    face_y = atoms // 2
    face_z = atoms // 8
    lengths = [face_x, face_x, face_y, face_y, face_z, face_z]
    starts = [
        0,
        face_x,
        2 * face_x,
        2 * face_x + face_y,
        2 * face_x + 2 * face_y,
        2 * face_x + 2 * face_y + face_z,
    ]
    kinds = jnp.arange(NSPEC, dtype=jnp.int32)

    def lookup(codes, table):
        onehot = (codes[:, None] == kinds[None, :]).astype(jnp.float32)
        return jnp.dot(onehot, table, precision=lax.Precision.HIGHEST)

    def project(rows, codes, weight, table):
        return (
            jnp.dot(rows, weight, preferred_element_type=jnp.float32) + lookup(codes, table)
        ).astype(jnp.bfloat16)

    def spread_cols(onehot, values):
        return jnp.einsum(
            "wn,nr->wr", values.astype(jnp.bfloat16), onehot, preferred_element_type=jnp.float32
        )

    def spread(onehot, values):
        return jnp.einsum(
            "nr,nw->rw", onehot, values.astype(jnp.bfloat16), preferred_element_type=jnp.float32
        )

    proj_c = project(latent, species, centre_proj, centre_table)
    proj_n = project(latent, species, neigh_proj, neigh_table)
    send_rows = send_list[0]
    coarse = positions // 16
    fine = positions - coarse * 16
    coord_cols = jnp.concatenate([coarse, fine], axis=0).T.astype(jnp.bfloat16)
    table = jnp.concatenate(
        [proj_n, coord_cols, jnp.zeros((atoms, extra - 6), jnp.bfloat16)], axis=1
    )
    shifts = [(0, -LX_FIX), (0, LX_FIX), (1, -LY_FIX), (1, LY_FIX), (2, -LZ_FIX), (2, LZ_FIX)]
    sections = (("gx", (1, 0)), ("gy", (3, 2)), ("gz", (5, 4)))
    pickers = {}
    base_rows = []
    for section, (axis, segs) in enumerate(sections):
        rows_now = table.shape[0]
        base_rows.append(rows_now)
        parts = [table]
        for number, (segment, direction) in enumerate(((segs[0], 1), (segs[1], -1))):
            picked = send_rows[starts[segment] : starts[segment] + lengths[segment]]
            onehot = (
                picked[:, None] == jnp.arange(rows_now, dtype=jnp.int32)[None, :]
            ).astype(jnp.bfloat16)
            pickers[segment] = onehot
            out = jnp.dot(onehot, table, preferred_element_type=jnp.float32).astype(jnp.bfloat16)
            got = passed_along(out, axis, direction)
            coord_axis, offset = shifts[2 * section + number]
            columns = jnp.arange(width + extra, dtype=jnp.int32)[None, :]
            shift = jnp.where(columns == width + coord_axis, offset // 16, 0).astype(jnp.bfloat16)
            parts.append(got + shift)
        table = jnp.concatenate(parts, axis=0)
    total_rows = table.shape[0]
    neighbour = neighbour.reshape(atoms, K).T.reshape(-1)
    select = (neighbour[:, None] == jnp.arange(total_rows, dtype=jnp.int32)[None, :]).astype(
        jnp.bfloat16
    )
    gathered = jnp.einsum("tw,pt->wp", table, select, preferred_element_type=jnp.float32)
    neigh_cols = gathered[:width].astype(jnp.bfloat16)
    coords_n = gathered[width : width + 3] * 16.0 + gathered[width + 3 : width + 6]
    delta = (coords_n.reshape(3, K, atoms) - positions.astype(jnp.float32)[:, None, :]) * (
        1.0 / 64.0
    )
    live = (jnp.arange(atoms) < atom_count[0]).astype(jnp.float32)
    valid_pair = live[None, :]

    geo, geo_pull = jax.vjp(lambda d: geometry(d, valid_pair), delta)
    grad_neigh, grad_centre, grad_geo, atom_energy = pair_terms(
        neigh_cols,
        proj_c.astype(jnp.float32).T,
        geo,
        basis_proj,
        split_proj,
        update_proj,
        tensor_proj,
        energy_proj,
    )
    (grad_delta,) = geo_pull(grad_geo)
    pairs = grad_neigh.shape[1]
    grads = jnp.concatenate(
        [
            grad_neigh,
            grad_delta.reshape(3, pairs),
            jnp.zeros((extra - 3, pairs), jnp.float32),
        ],
        axis=0,
    )
    sums = spread_cols(select, grads).T
    own_pos = grad_delta.sum(axis=1)
    sums = sums - jnp.pad(own_pos.T, ((0, total_rows - atoms), (width, extra - 3)))
    for section in (2, 1, 0):
        axis, segs = sections[section]
        rows_now = base_rows[section]
        first = atoms + starts[2 * section]
        second = atoms + starts[2 * section + 1]
        back_first = passed_along(sums[first : first + lengths[2 * section]], axis, -1)
        back_second = passed_along(sums[second : second + lengths[2 * section + 1]], axis, 1)
        sums = (
            sums[:rows_now]
            + spread(pickers[segs[0]], back_first)
            + spread(pickers[segs[1]], back_second)
        )
    def times_transposed(values, weight):
        high = values.astype(jnp.bfloat16)
        low = (values - high.astype(jnp.float32)).astype(jnp.bfloat16)
        return jnp.einsum(
            "ah,ih->ai", high, weight, preferred_element_type=jnp.float32
        ) + jnp.einsum("ah,ih->ai", low, weight, preferred_element_type=jnp.float32)

    latent_grad = times_transposed(grad_centre.T, centre_proj)
    latent_grad = latent_grad + times_transposed(sums[:, :width], neigh_proj)
    forces = -sums[:, width : width + 3].T
    energies = live * (lookup(species, species_shift[:, None])[:, 0] + atom_energy)
    return (energies, forces, latent_grad)


def solution(mesh):
    in_specs = (
        P(("gx", "gy", "gz"), None),
        P(None, ("gx", "gy", "gz")),
        P(("gx", "gy", "gz")),
        P(("gx", "gy", "gz"), None),
        P(("gx", "gy", "gz")),
        P(("gx", "gy", "gz")),
        P(),
        P(),
        P(),
        P(),
        P(),
        P(),
        P(),
        P(),
        P(),
        P(),
    )
    out_specs = (P(("gx", "gy", "gz")), P(None, ("gx", "gy", "gz")), P(("gx", "gy", "gz"), None))
    return jax.shard_map(shards, mesh=mesh, in_specs=in_specs, out_specs=out_specs, check_vma=False)
```

```python
import math

import jax
import jax.numpy as jnp
from jax import lax
from jax.experimental import pallas as pl
from jax.experimental.pallas import tpu as pltpu
from jax.sharding import PartitionSpec as P

K = 8
CH = 64
NB = 8
NSPEC = 5
LX_FIX = 1024
LY_FIX = 512
LZ_FIX = 1280


CUTOFF = 6.0
SOFTEN = 0.25


def shortened(shard):
    return jax.tree.map(lambda a: a.astype(jnp.bfloat16) if a.dtype == jnp.float32 else a, shard)


def passed_along(block, axis, distance):
    devices = range(lax.axis_size(axis))
    route = [((i - distance) % len(devices), i) for i in devices]
    return lax.ppermute(block, axis, route)


def by_order(values):
    rest = values.shape[1:]
    return jnp.concatenate(
        [
            values[0:1],
            jnp.broadcast_to(values[1:2], (3,) + rest),
            jnp.broadcast_to(values[2:3], (5,) + rest),
        ],
        axis=0,
    )


SLOTS = 8
ORDER_OF = (0, 1, 1, 1, 2, 2, 2, 2, 2)
GROUPS = ((0,), (1, 2, 3), (4, 5, 6, 7, 8))


def geometry(delta, valid_pair):
    atoms = delta.shape[2]
    radius = jnp.sqrt(jnp.sum(delta * delta, axis=0) + SOFTEN)
    unit = delta / radius
    ratio = radius / CUTOFF
    envelope = jnp.where(ratio < 1.0, (1.0 - ratio * ratio) ** 2, 0.0) * valid_pair
    orders = jnp.arange(1, NB + 1).astype(jnp.float32)
    basis = (
        jnp.sin(orders[:, None, None] * (math.pi / CUTOFF) * radius[None])
        * (envelope / radius)[None]
    )
    ux, uy, uz = unit[0], unit[1], unit[2]
    r3 = math.sqrt(3.0)
    r15 = math.sqrt(15.0)
    r5 = math.sqrt(5.0)
    harmonics = jnp.stack(
        [
            jnp.ones_like(ux),
            r3 * ux,
            r3 * uy,
            r3 * uz,
            r15 * ux * uy,
            r15 * uy * uz,
            0.5 * r5 * (2.0 * uz * uz - ux * ux - uy * uy),
            r15 * ux * uz,
            0.5 * r15 * (ux * ux - uy * uy),
        ],
        axis=0,
    )
    rows = jnp.concatenate([basis, envelope[None], harmonics], axis=0).reshape(18, K * atoms)
    return jnp.concatenate([rows, jnp.zeros((128 - 18, K * atoms), jnp.float32)], axis=0)


def _mm(a, b):
    return jnp.dot(a, b, preferred_element_type=jnp.float32)


def _sigmoid(v):
    return 0.5 + 0.5 * jnp.tanh(0.5 * v)


def _pair_kernel(
    rows_ref, centre_ref, geo_ref, basis_t_ref, split_t_ref, split_ref, update_t_ref,
    update_ref, tensor_t_ref, tensor_ref, basis_ref, energy_w_ref,
    grad_rows_ref, grad_centre_ref, grad_geo_ref, energy_ref,
    pre_s, hidden_s, mixed_s, damp_s, dlow_s, dgeo_s, env_s, denv_s,
):
    atoms = centre_ref.shape[1]
    f32 = jnp.float32
    bf16 = jnp.bfloat16
    span = SLOTS * atoms
    sub = lax.broadcasted_iota(jnp.int32, (128, span), 0)
    inv_root = 1.0 / math.sqrt(K)
    env_s[...] = jnp.zeros_like(env_s)
    denv_s[...] = jnp.zeros_like(denv_s)

    def block(k):
        return pl.ds(pl.multiple_of(k * span, span), span)

    def twice(v):
        return jnp.concatenate([v] * SLOTS, axis=1)

    def fold(v):
        total = v[:, :atoms]
        for slot in range(1, SLOTS):
            total = total + v[:, slot * atoms : (slot + 1) * atoms]
        return total

    def split_mm(weight, values):
        high = values.astype(bf16)
        low = (values - high.astype(f32)).astype(bf16)
        return _mm(weight, high) + _mm(weight, low)

    def first(k, carry):
        at = block(k)
        geo = geo_ref[:, at]
        radial = split_mm(basis_t_ref[...], geo)
        pre = twice(centre_ref[...]) + rows_ref[:, at].astype(f32) + radial
        envelope = geo[8:9, :]
        hidden = pre * _sigmoid(pre) * envelope
        pre_s[:, at] = pre
        hidden_s[:, at] = hidden
        mixed = _mm(split_t_ref[...], hidden.astype(bf16))
        mixed_s[:, at] = mixed
        for m in range(9):
            l = ORDER_OF[m]
            weight = mixed[3 * CH + l * CH : 3 * CH + (l + 1) * CH, :]
            env_s[m] = env_s[m] + fold(weight * (geo[9 + m : 10 + m, :] * inv_root))
        return carry

    lax.fori_loop(0, K // SLOTS, first, 0)

    def second(k, energy):
        at = block(k)
        geo = geo_ref[:, at]
        envelope = geo[8:9, :]
        hidden = hidden_s[:, at]
        mixed = mixed_s[:, at]
        parts = []
        totals = []
        for l in range(3):
            total = 0.0
            for m in GROUPS[l]:
                total = total + geo[9 + m : 10 + m, :] * twice(env_s[m])
            totals.append(total)
            parts.append(mixed[l * CH : (l + 1) * CH, :] * total)
        scalars = jnp.concatenate(parts, axis=0).astype(bf16)
        z = _mm(update_t_ref[...], hidden.astype(bf16)) + _mm(tensor_t_ref[...], scalars)
        gate = _sigmoid(z)
        update = z * gate
        readout = jnp.sum((hidden + update) * energy_w_ref[...], axis=0, keepdims=True)
        energy = energy + envelope * readout
        dz = (envelope * energy_w_ref[...]) * (gate * (1.0 + z * (1.0 - gate)))
        dz_low = dz.astype(bf16)
        dscalars = _mm(tensor_ref[...], dz_low).astype(bf16).astype(f32)
        dlow_s[:, at] = _mm(update_ref[...], dz_low)
        dgeo = jnp.where(sub == 8, readout, 0.0)
        for l in range(3):
            ds = dscalars[l * CH : (l + 1) * CH, :]
            damp_s[l * CH : (l + 1) * CH, at] = ds * totals[l]
            dtotal = ds * mixed[l * CH : (l + 1) * CH, :]
            for m in GROUPS[l]:
                dgeo = dgeo + jnp.where(
                    sub == 9 + m, jnp.sum(dtotal * twice(env_s[m]), axis=0, keepdims=True), 0.0
                )
                denv_s[m] = denv_s[m] + fold(dtotal * geo[9 + m : 10 + m, :])
        dgeo_s[:, at] = dgeo
        return energy

    energy = lax.fori_loop(0, K // SLOTS, second, jnp.zeros((1, span), f32))
    energy_ref[...] = jnp.broadcast_to(fold(energy), energy_ref.shape)

    def third(k, centre_grad):
        at = block(k)
        geo = geo_ref[:, at]
        envelope = geo[8:9, :]
        mixed = mixed_s[:, at]
        dgeo = dgeo_s[:, at]
        dweights = []
        for l in range(3):
            weight = mixed[3 * CH + l * CH : 3 * CH + (l + 1) * CH, :]
            dweight = 0.0
            for m in GROUPS[l]:
                denv = twice(denv_s[m])
                dweight = dweight + denv * (geo[9 + m : 10 + m, :] * inv_root)
                dgeo = dgeo + jnp.where(
                    sub == 9 + m,
                    jnp.sum(denv * weight, axis=0, keepdims=True) * inv_root,
                    0.0,
                )
            dweights.append(dweight)
        dmixed = jnp.concatenate([damp_s[:, at]] + dweights, axis=0).astype(bf16)
        dlow = dlow_s[:, at] + _mm(split_ref[...], dmixed)
        dhidden = envelope * energy_w_ref[...] + dlow
        pre = pre_s[:, at]
        sig = _sigmoid(pre)
        act = pre * sig
        dgeo = dgeo + jnp.where(sub == 8, jnp.sum(dhidden * act, axis=0, keepdims=True), 0.0)
        dpre = dhidden * envelope * (sig * (1.0 + pre * (1.0 - sig)))
        grad_rows_ref[:, at] = dpre
        dgeo = dgeo + split_mm(basis_ref[...], dpre)
        grad_geo_ref[:, at] = dgeo
        return centre_grad + fold(dpre)

    grad_centre_ref[...] = lax.fori_loop(
        0, K // SLOTS, third, jnp.zeros(grad_centre_ref.shape, f32)
    )


def pair_terms(rows_t, centre_t, geo, basis_proj, split_proj, update_proj, tensor_proj, energy_proj):
    width, pairs = rows_t.shape
    atoms = centre_t.shape[1]
    f32 = jnp.float32
    bf16 = jnp.bfloat16
    basis_pad = jnp.concatenate([basis_proj, jnp.zeros((128 - NB, width), bf16)], axis=0)
    vmem = pl.BlockSpec(memory_space=pltpu.VMEM)
    outs = pl.pallas_call(
        _pair_kernel,
        out_shape=(
            jax.ShapeDtypeStruct((width, pairs), f32),
            jax.ShapeDtypeStruct((width, atoms), f32),
            jax.ShapeDtypeStruct((128, pairs), f32),
            jax.ShapeDtypeStruct((8, atoms), f32),
        ),
        in_specs=[vmem] * 12,
        out_specs=(vmem, vmem, vmem, vmem),
        scratch_shapes=[
            pltpu.VMEM((width, pairs), f32),
            pltpu.VMEM((width, pairs), f32),
            pltpu.VMEM((6 * CH, pairs), f32),
            pltpu.VMEM((3 * CH, pairs), f32),
            pltpu.VMEM((width, pairs), f32),
            pltpu.VMEM((128, pairs), f32),
            pltpu.VMEM((9, CH, atoms), f32),
            pltpu.VMEM((9, CH, atoms), f32),
        ],
        compiler_params=pltpu.CompilerParams(vmem_limit_bytes=60 * 1024 * 1024),
        cost_estimate=pl.CostEstimate(
            flops=int(24 * pairs * width * 128),
            transcendentals=int(3 * pairs * width),
            bytes_accessed=int(16 * pairs * width),
        ),
    )(
        rows_t,
        centre_t,
        geo,
        basis_pad.T,
        split_proj.T,
        split_proj,
        update_proj.T,
        update_proj,
        tensor_proj.T,
        tensor_proj,
        basis_pad,
        jnp.broadcast_to(energy_proj.astype(f32)[:, None], (width, SLOTS * atoms)),
    )
    grad_rows_t, grad_centre_t, grad_geo, energy = outs
    return grad_rows_t, grad_centre_t, grad_geo, energy[0]


def shards(
    latent,
    positions,
    species,
    send_list,
    neighbour,
    atom_count,
    centre_proj,
    neigh_proj,
    centre_table,
    neigh_table,
    basis_proj,
    split_proj,
    update_proj,
    tensor_proj,
    energy_proj,
    species_shift,
):
    atoms, width = latent.shape
    extra = 128
    face_x = atoms // 8
    face_y = atoms // 2
    face_z = atoms // 8
    lengths = [face_x, face_x, face_y, face_y, face_z, face_z]
    starts = [
        0,
        face_x,
        2 * face_x,
        2 * face_x + face_y,
        2 * face_x + 2 * face_y,
        2 * face_x + 2 * face_y + face_z,
    ]
    kinds = jnp.arange(NSPEC, dtype=jnp.int32)

    def lookup(codes, table):
        onehot = (codes[:, None] == kinds[None, :]).astype(jnp.float32)
        return jnp.dot(onehot, table, precision=lax.Precision.HIGHEST)

    def project(rows, codes, weight, table):
        return (
            jnp.dot(rows, weight, preferred_element_type=jnp.float32) + lookup(codes, table)
        ).astype(jnp.bfloat16)

    def spread_cols(onehot, values):
        return jnp.einsum(
            "wn,nr->wr", values.astype(jnp.bfloat16), onehot, preferred_element_type=jnp.float32
        )

    def spread(onehot, values):
        return jnp.einsum(
            "nr,nw->rw", onehot, values.astype(jnp.bfloat16), preferred_element_type=jnp.float32
        )

    proj_c = project(latent, species, centre_proj, centre_table)
    proj_n = project(latent, species, neigh_proj, neigh_table)
    send_rows = send_list[0]
    coarse = positions // 16
    fine = positions - coarse * 16
    coord_cols = jnp.concatenate([coarse, fine], axis=0).T.astype(jnp.bfloat16)
    table = jnp.concatenate(
        [proj_n, coord_cols, jnp.zeros((atoms, extra - 6), jnp.bfloat16)], axis=1
    )
    shifts = [(0, -LX_FIX), (0, LX_FIX), (1, -LY_FIX), (1, LY_FIX), (2, -LZ_FIX), (2, LZ_FIX)]
    sections = (("gx", (1, 0)), ("gy", (3, 2)), ("gz", (5, 4)))
    pickers = {}
    base_rows = []
    for section, (axis, segs) in enumerate(sections):
        rows_now = table.shape[0]
        base_rows.append(rows_now)
        parts = [table]
        for number, (segment, direction) in enumerate(((segs[0], 1), (segs[1], -1))):
            picked = send_rows[starts[segment] : starts[segment] + lengths[segment]]
            onehot = (
                picked[:, None] == jnp.arange(rows_now, dtype=jnp.int32)[None, :]
            ).astype(jnp.bfloat16)
            pickers[segment] = onehot
            out = jnp.dot(onehot, table, preferred_element_type=jnp.float32).astype(jnp.bfloat16)
            got = passed_along(out, axis, direction)
            coord_axis, offset = shifts[2 * section + number]
            columns = jnp.arange(width + extra, dtype=jnp.int32)[None, :]
            shift = jnp.where(columns == width + coord_axis, offset // 16, 0).astype(jnp.bfloat16)
            parts.append(got + shift)
        table = jnp.concatenate(parts, axis=0)
    total_rows = table.shape[0]
    neighbour = neighbour.reshape(atoms, K).T.reshape(-1)
    select = (neighbour[:, None] == jnp.arange(total_rows, dtype=jnp.int32)[None, :]).astype(
        jnp.bfloat16
    )
    gathered = jnp.einsum("tw,pt->wp", table, select, preferred_element_type=jnp.float32)
    neigh_cols = gathered[:width].astype(jnp.bfloat16)
    coords_n = gathered[width : width + 3] * 16.0 + gathered[width + 3 : width + 6]
    delta = (coords_n.reshape(3, K, atoms) - positions.astype(jnp.float32)[:, None, :]) * (
        1.0 / 64.0
    )
    live = (jnp.arange(atoms) < atom_count[0]).astype(jnp.float32)
    valid_pair = live[None, :]

    geo, geo_pull = jax.vjp(lambda d: geometry(d, valid_pair), delta)
    grad_neigh, grad_centre, grad_geo, atom_energy = pair_terms(
        neigh_cols,
        proj_c.astype(jnp.float32).T,
        geo,
        basis_proj,
        split_proj,
        update_proj,
        tensor_proj,
        energy_proj,
    )
    (grad_delta,) = geo_pull(grad_geo)
    pairs = grad_neigh.shape[1]
    pos_grads = jnp.concatenate(
        [grad_delta.reshape(3, pairs), jnp.zeros((extra - 3, pairs), jnp.float32)], axis=0
    )
    sums = jnp.concatenate(
        [spread_cols(select, grad_neigh), spread_cols(select, pos_grads)], axis=0
    ).T
    own_pos = grad_delta.sum(axis=1)
    sums = sums - jnp.pad(own_pos.T, ((0, total_rows - atoms), (width, extra - 3)))
    for section in (2, 1, 0):
        axis, segs = sections[section]
        rows_now = base_rows[section]
        first = atoms + starts[2 * section]
        second = atoms + starts[2 * section + 1]
        back_first = passed_along(sums[first : first + lengths[2 * section]], axis, -1)
        back_second = passed_along(sums[second : second + lengths[2 * section + 1]], axis, 1)
        sums = (
            sums[:rows_now]
            + spread(pickers[segs[0]], back_first)
            + spread(pickers[segs[1]], back_second)
        )
    back_neigh = neigh_proj.astype(jnp.float32).T
    back_centre = centre_proj.astype(jnp.float32).T
    latent_grad = jnp.dot(grad_centre.T, back_centre, precision=lax.Precision.HIGHEST)
    latent_grad = latent_grad + jnp.dot(
        sums[:, :width], back_neigh, precision=lax.Precision.HIGHEST
    )
    forces = -sums[:, width : width + 3].T
    energies = live * (lookup(species, species_shift[:, None])[:, 0] + atom_energy)
    return (energies, forces, latent_grad)


def solution(mesh):
    in_specs = (
        P(("gx", "gy", "gz"), None),
        P(None, ("gx", "gy", "gz")),
        P(("gx", "gy", "gz")),
        P(("gx", "gy", "gz"), None),
        P(("gx", "gy", "gz")),
        P(("gx", "gy", "gz")),
        P(),
        P(),
        P(),
        P(),
        P(),
        P(),
        P(),
        P(),
        P(),
        P(),
    )
    out_specs = (P(("gx", "gy", "gz")), P(None, ("gx", "gy", "gz")), P(("gx", "gy", "gz"), None))
    return jax.shard_map(shards, mesh=mesh, in_specs=in_specs, out_specs=out_specs, check_vma=False)
```

```python
import math

import jax
import jax.numpy as jnp
from jax import lax
from jax.experimental import pallas as pl
from jax.experimental.pallas import tpu as pltpu
from jax.sharding import PartitionSpec as P

K = 8
CH = 64
NB = 8
NSPEC = 5
LX_FIX = 1024
LY_FIX = 512
LZ_FIX = 1280


CUTOFF = 6.0
SOFTEN = 0.25


def shortened(shard):
    return jax.tree.map(lambda a: a.astype(jnp.bfloat16) if a.dtype == jnp.float32 else a, shard)


def passed_along(block, axis, distance):
    devices = range(lax.axis_size(axis))
    route = [((i - distance) % len(devices), i) for i in devices]
    return lax.ppermute(block, axis, route)


def by_order(values):
    rest = values.shape[1:]
    return jnp.concatenate(
        [
            values[0:1],
            jnp.broadcast_to(values[1:2], (3,) + rest),
            jnp.broadcast_to(values[2:3], (5,) + rest),
        ],
        axis=0,
    )


SLOTS = 8
ORDER_OF = (0, 1, 1, 1, 2, 2, 2, 2, 2)
GROUPS = ((0,), (1, 2, 3), (4, 5, 6, 7, 8))


def geometry(delta, valid_pair):
    atoms = delta.shape[2]
    radius = jnp.sqrt(jnp.sum(delta * delta, axis=0) + SOFTEN)
    unit = delta / radius
    ratio = radius / CUTOFF
    envelope = jnp.where(ratio < 1.0, (1.0 - ratio * ratio) ** 2, 0.0) * valid_pair
    orders = jnp.arange(1, NB + 1).astype(jnp.float32)
    basis = (
        jnp.sin(orders[:, None, None] * (math.pi / CUTOFF) * radius[None])
        * (envelope / radius)[None]
    )
    ux, uy, uz = unit[0], unit[1], unit[2]
    r3 = math.sqrt(3.0)
    r15 = math.sqrt(15.0)
    r5 = math.sqrt(5.0)
    harmonics = jnp.stack(
        [
            jnp.ones_like(ux),
            r3 * ux,
            r3 * uy,
            r3 * uz,
            r15 * ux * uy,
            r15 * uy * uz,
            0.5 * r5 * (2.0 * uz * uz - ux * ux - uy * uy),
            r15 * ux * uz,
            0.5 * r15 * (ux * ux - uy * uy),
        ],
        axis=0,
    )
    rows = jnp.concatenate([basis, envelope[None], harmonics], axis=0).reshape(18, K * atoms)
    return jnp.concatenate([rows, jnp.zeros((128 - 18, K * atoms), jnp.float32)], axis=0)


def _mm(a, b):
    return jnp.dot(a, b, preferred_element_type=jnp.float32)


def _sigmoid(v):
    return 0.5 + 0.5 * jnp.tanh(0.5 * v)


def _pair_kernel(
    rows_ref, centre_ref, geo_ref, basis_t_ref, split_t_ref, split_ref, update_t_ref,
    update_ref, tensor_t_ref, tensor_ref, basis_ref, energy_w_ref,
    grad_rows_ref, grad_centre_ref, grad_geo_ref, energy_ref,
    pre_s, hidden_s, mixed_s, damp_s, dlow_s, dgeo_s, env_s, denv_s,
):
    atoms = centre_ref.shape[1]
    f32 = jnp.float32
    bf16 = jnp.bfloat16
    span = SLOTS * atoms
    sub = lax.broadcasted_iota(jnp.int32, (128, span), 0)
    inv_root = 1.0 / math.sqrt(K)
    env_s[...] = jnp.zeros_like(env_s)
    denv_s[...] = jnp.zeros_like(denv_s)

    def block(k):
        return pl.ds(pl.multiple_of(k * span, span), span)

    def twice(v):
        return jnp.concatenate([v] * SLOTS, axis=1)

    def fold(v):
        total = v[:, :atoms]
        for slot in range(1, SLOTS):
            total = total + v[:, slot * atoms : (slot + 1) * atoms]
        return total

    def split_mm(weight, values):
        high = values.astype(bf16)
        low = (values - high.astype(f32)).astype(bf16)
        return _mm(weight, high) + _mm(weight, low)

    def first(k, carry):
        at = block(k)
        geo = geo_ref[:, at]
        radial = split_mm(basis_t_ref[...], geo)
        pre = twice(centre_ref[...]) + rows_ref[:, at].astype(f32) + radial
        envelope = geo[8:9, :]
        hidden = pre * _sigmoid(pre) * envelope
        pre_s[:, at] = pre
        hidden_s[:, at] = hidden
        mixed = _mm(split_t_ref[...], hidden.astype(bf16))
        mixed_s[:, at] = mixed
        for m in range(9):
            l = ORDER_OF[m]
            weight = mixed[3 * CH + l * CH : 3 * CH + (l + 1) * CH, :]
            env_s[m] = env_s[m] + fold(weight * (geo[9 + m : 10 + m, :] * inv_root))
        return carry

    lax.fori_loop(0, K // SLOTS, first, 0)

    def second(k, energy):
        at = block(k)
        geo = geo_ref[:, at]
        envelope = geo[8:9, :]
        hidden = hidden_s[:, at]
        mixed = mixed_s[:, at]
        parts = []
        totals = []
        for l in range(3):
            total = 0.0
            for m in GROUPS[l]:
                total = total + geo[9 + m : 10 + m, :] * twice(env_s[m])
            totals.append(total)
            parts.append(mixed[l * CH : (l + 1) * CH, :] * total)
        scalars = jnp.concatenate(parts, axis=0).astype(bf16)
        z = _mm(update_t_ref[...], hidden.astype(bf16)) + _mm(tensor_t_ref[...], scalars)
        gate = _sigmoid(z)
        update = z * gate
        readout = jnp.sum((hidden + update) * twice(energy_w_ref[...]), axis=0, keepdims=True)
        energy = energy + envelope * readout
        dz = (envelope * twice(energy_w_ref[...])) * (gate * (1.0 + z * (1.0 - gate)))
        dz_low = dz.astype(bf16)
        dscalars = _mm(tensor_ref[...], dz_low).astype(bf16).astype(f32)
        dlow_s[:, at] = _mm(update_ref[...], dz_low)
        dgeo = jnp.where(sub == 8, readout, 0.0)
        for l in range(3):
            ds = dscalars[l * CH : (l + 1) * CH, :]
            damp_s[l * CH : (l + 1) * CH, at] = ds * totals[l]
            dtotal = ds * mixed[l * CH : (l + 1) * CH, :]
            for m in GROUPS[l]:
                dgeo = dgeo + jnp.where(
                    sub == 9 + m, jnp.sum(dtotal * twice(env_s[m]), axis=0, keepdims=True), 0.0
                )
                denv_s[m] = denv_s[m] + fold(dtotal * geo[9 + m : 10 + m, :])
        dgeo_s[:, at] = dgeo
        return energy

    energy = lax.fori_loop(0, K // SLOTS, second, jnp.zeros((1, span), f32))
    energy_ref[...] = jnp.broadcast_to(fold(energy), energy_ref.shape)

    def third(k, centre_grad):
        at = block(k)
        geo = geo_ref[:, at]
        envelope = geo[8:9, :]
        mixed = mixed_s[:, at]
        dgeo = dgeo_s[:, at]
        dweights = []
        for l in range(3):
            weight = mixed[3 * CH + l * CH : 3 * CH + (l + 1) * CH, :]
            dweight = 0.0
            for m in GROUPS[l]:
                denv = twice(denv_s[m])
                dweight = dweight + denv * (geo[9 + m : 10 + m, :] * inv_root)
                dgeo = dgeo + jnp.where(
                    sub == 9 + m,
                    jnp.sum(denv * weight, axis=0, keepdims=True) * inv_root,
                    0.0,
                )
            dweights.append(dweight)
        dmixed = jnp.concatenate([damp_s[:, at]] + dweights, axis=0).astype(bf16)
        dlow = dlow_s[:, at] + _mm(split_ref[...], dmixed)
        dhidden = envelope * twice(energy_w_ref[...]) + dlow
        pre = pre_s[:, at]
        sig = _sigmoid(pre)
        act = pre * sig
        dgeo = dgeo + jnp.where(sub == 8, jnp.sum(dhidden * act, axis=0, keepdims=True), 0.0)
        dpre = dhidden * envelope * (sig * (1.0 + pre * (1.0 - sig)))
        grad_rows_ref[:, at] = dpre
        dgeo = dgeo + split_mm(basis_ref[...], dpre)
        grad_geo_ref[:, at] = dgeo
        return centre_grad + fold(dpre)

    grad_centre_ref[...] = lax.fori_loop(
        0, K // SLOTS, third, jnp.zeros(grad_centre_ref.shape, f32)
    )


def pair_terms(rows_t, centre_t, geo, basis_proj, split_proj, update_proj, tensor_proj, energy_proj):
    width, pairs = rows_t.shape
    atoms = centre_t.shape[1]
    f32 = jnp.float32
    bf16 = jnp.bfloat16
    basis_pad = jnp.concatenate([basis_proj, jnp.zeros((128 - NB, width), bf16)], axis=0)
    vmem = pl.BlockSpec(memory_space=pltpu.VMEM)
    outs = pl.pallas_call(
        _pair_kernel,
        out_shape=(
            jax.ShapeDtypeStruct((width, pairs), f32),
            jax.ShapeDtypeStruct((width, atoms), f32),
            jax.ShapeDtypeStruct((128, pairs), f32),
            jax.ShapeDtypeStruct((8, atoms), f32),
        ),
        in_specs=[vmem] * 12,
        out_specs=(vmem, vmem, vmem, vmem),
        scratch_shapes=[
            pltpu.VMEM((width, pairs), f32),
            pltpu.VMEM((width, pairs), f32),
            pltpu.VMEM((6 * CH, pairs), f32),
            pltpu.VMEM((3 * CH, pairs), f32),
            pltpu.VMEM((width, pairs), f32),
            pltpu.VMEM((128, pairs), f32),
            pltpu.VMEM((9, CH, atoms), f32),
            pltpu.VMEM((9, CH, atoms), f32),
        ],
        compiler_params=pltpu.CompilerParams(vmem_limit_bytes=60 * 1024 * 1024),
        cost_estimate=pl.CostEstimate(
            flops=int(24 * pairs * width * 128),
            transcendentals=int(3 * pairs * width),
            bytes_accessed=int(16 * pairs * width),
        ),
    )(
        rows_t,
        centre_t,
        geo,
        basis_pad.T,
        split_proj.T,
        split_proj,
        update_proj.T,
        update_proj,
        tensor_proj.T,
        tensor_proj,
        basis_pad,
        jnp.broadcast_to(energy_proj.astype(f32)[:, None], (width, atoms)),
    )
    grad_rows_t, grad_centre_t, grad_geo, energy = outs
    return grad_rows_t, grad_centre_t, grad_geo, energy[0]


def shards(
    latent,
    positions,
    species,
    send_list,
    neighbour,
    atom_count,
    centre_proj,
    neigh_proj,
    centre_table,
    neigh_table,
    basis_proj,
    split_proj,
    update_proj,
    tensor_proj,
    energy_proj,
    species_shift,
):
    atoms, width = latent.shape
    extra = 128
    face_x = atoms // 8
    face_y = atoms // 2
    face_z = atoms // 8
    lengths = [face_x, face_x, face_y, face_y, face_z, face_z]
    starts = [
        0,
        face_x,
        2 * face_x,
        2 * face_x + face_y,
        2 * face_x + 2 * face_y,
        2 * face_x + 2 * face_y + face_z,
    ]
    kinds = jnp.arange(NSPEC, dtype=jnp.int32)

    def lookup(codes, table):
        onehot = (codes[:, None] == kinds[None, :]).astype(jnp.float32)
        return jnp.dot(onehot, table, precision=lax.Precision.HIGHEST)

    def project(rows, codes, weight, table):
        return (
            jnp.dot(rows, weight, preferred_element_type=jnp.float32) + lookup(codes, table)
        ).astype(jnp.bfloat16)

    def spread_cols(onehot, values):
        return jnp.einsum(
            "wn,nr->wr", values.astype(jnp.bfloat16), onehot, preferred_element_type=jnp.float32
        )

    def spread(onehot, values):
        return jnp.einsum(
            "nr,nw->rw", onehot, values.astype(jnp.bfloat16), preferred_element_type=jnp.float32
        )

    proj_c = project(latent, species, centre_proj, centre_table)
    proj_n = project(latent, species, neigh_proj, neigh_table)
    send_rows = send_list[0]
    coarse = positions // 16
    fine = positions - coarse * 16
    coord_cols = jnp.concatenate([coarse, fine], axis=0).T.astype(jnp.bfloat16)
    table = jnp.concatenate(
        [proj_n, coord_cols, jnp.zeros((atoms, extra - 6), jnp.bfloat16)], axis=1
    )
    shifts = [(0, -LX_FIX), (0, LX_FIX), (1, -LY_FIX), (1, LY_FIX), (2, -LZ_FIX), (2, LZ_FIX)]
    sections = (("gx", (1, 0)), ("gy", (3, 2)), ("gz", (5, 4)))
    pickers = {}
    base_rows = []
    for section, (axis, segs) in enumerate(sections):
        rows_now = table.shape[0]
        base_rows.append(rows_now)
        parts = [table]
        for number, (segment, direction) in enumerate(((segs[0], 1), (segs[1], -1))):
            picked = send_rows[starts[segment] : starts[segment] + lengths[segment]]
            onehot = (
                picked[:, None] == jnp.arange(rows_now, dtype=jnp.int32)[None, :]
            ).astype(jnp.bfloat16)
            pickers[segment] = onehot
            out = jnp.dot(onehot, table, preferred_element_type=jnp.float32).astype(jnp.bfloat16)
            got = passed_along(out, axis, direction)
            coord_axis, offset = shifts[2 * section + number]
            columns = jnp.arange(width + extra, dtype=jnp.int32)[None, :]
            shift = jnp.where(columns == width + coord_axis, offset // 16, 0).astype(jnp.bfloat16)
            parts.append(got + shift)
        table = jnp.concatenate(parts, axis=0)
    total_rows = table.shape[0]
    neighbour = neighbour.reshape(atoms, K).T.reshape(-1)
    select = (neighbour[:, None] == jnp.arange(total_rows, dtype=jnp.int32)[None, :]).astype(
        jnp.bfloat16
    )
    gathered = jnp.einsum("tw,pt->wp", table, select, preferred_element_type=jnp.float32)
    neigh_cols = gathered[:width].astype(jnp.bfloat16)
    coords_n = gathered[width : width + 3] * 16.0 + gathered[width + 3 : width + 6]
    delta = (coords_n.reshape(3, K, atoms) - positions.astype(jnp.float32)[:, None, :]) * (
        1.0 / 64.0
    )
    live = (jnp.arange(atoms) < atom_count[0]).astype(jnp.float32)
    valid_pair = live[None, :]

    geo, geo_pull = jax.vjp(lambda d: geometry(d, valid_pair), delta)
    grad_neigh, grad_centre, grad_geo, atom_energy = pair_terms(
        neigh_cols,
        proj_c.astype(jnp.float32).T,
        geo,
        basis_proj,
        split_proj,
        update_proj,
        tensor_proj,
        energy_proj,
    )
    (grad_delta,) = geo_pull(grad_geo)
    pairs = grad_neigh.shape[1]
    grads = jnp.concatenate(
        [
            grad_neigh,
            grad_delta.reshape(3, pairs),
            jnp.zeros((extra - 3, pairs), jnp.float32),
        ],
        axis=0,
    )
    sums = spread_cols(select, grads).T
    own_pos = grad_delta.sum(axis=1)
    sums = sums - jnp.pad(own_pos.T, ((0, total_rows - atoms), (width, extra - 3)))
    for section in (2, 1, 0):
        axis, segs = sections[section]
        rows_now = base_rows[section]
        first = atoms + starts[2 * section]
        second = atoms + starts[2 * section + 1]
        back_first = passed_along(sums[first : first + lengths[2 * section]], axis, -1)
        back_second = passed_along(sums[second : second + lengths[2 * section + 1]], axis, 1)
        sums = (
            sums[:rows_now]
            + spread(pickers[segs[0]], back_first)
            + spread(pickers[segs[1]], back_second)
        )
    back_neigh = neigh_proj.astype(jnp.float32).T
    back_centre = centre_proj.astype(jnp.float32).T
    latent_grad = jnp.dot(grad_centre.T, back_centre, precision=lax.Precision.HIGHEST)
    latent_grad = latent_grad + jnp.dot(
        sums[:, :width], back_neigh, precision=lax.Precision.HIGHEST
    )
    forces = -sums[:, width : width + 3].T
    energies = live * (lookup(species, species_shift[:, None])[:, 0] + atom_energy)
    return (energies, forces, latent_grad)


def solution(mesh):
    in_specs = (
        P(("gx", "gy", "gz"), None),
        P(None, ("gx", "gy", "gz")),
        P(("gx", "gy", "gz")),
        P(("gx", "gy", "gz"), None),
        P(("gx", "gy", "gz")),
        P(("gx", "gy", "gz")),
        P(),
        P(),
        P(),
        P(),
        P(),
        P(),
        P(),
        P(),
        P(),
        P(),
    )
    out_specs = (P(("gx", "gy", "gz")), P(None, ("gx", "gy", "gz")), P(("gx", "gy", "gz"), None))
    return jax.shard_map(shards, mesh=mesh, in_specs=in_specs, out_specs=out_specs, check_vma=False)
```

```python
import math

import jax
import jax.numpy as jnp
from jax import lax
from jax.experimental import pallas as pl
from jax.experimental.pallas import tpu as pltpu
from jax.sharding import PartitionSpec as P

K = 8
CH = 64
NB = 8
NSPEC = 5
LX_FIX = 1024
LY_FIX = 512
LZ_FIX = 1280


CUTOFF = 6.0
SOFTEN = 0.25


def shortened(shard):
    return jax.tree.map(lambda a: a.astype(jnp.bfloat16) if a.dtype == jnp.float32 else a, shard)


def passed_along(block, axis, distance):
    devices = range(lax.axis_size(axis))
    route = [((i - distance) % len(devices), i) for i in devices]
    return lax.ppermute(block, axis, route)


def by_order(values):
    rest = values.shape[1:]
    return jnp.concatenate(
        [
            values[0:1],
            jnp.broadcast_to(values[1:2], (3,) + rest),
            jnp.broadcast_to(values[2:3], (5,) + rest),
        ],
        axis=0,
    )


SLOTS = 8
ORDER_OF = (0, 1, 1, 1, 2, 2, 2, 2, 2)
GROUPS = ((0,), (1, 2, 3), (4, 5, 6, 7, 8))


def geometry(delta, valid_pair):
    atoms = delta.shape[2]
    radius = jnp.sqrt(jnp.sum(delta * delta, axis=0) + SOFTEN)
    unit = delta / radius
    ratio = radius / CUTOFF
    envelope = jnp.where(ratio < 1.0, (1.0 - ratio * ratio) ** 2, 0.0) * valid_pair
    orders = jnp.arange(1, NB + 1).astype(jnp.float32)
    basis = (
        jnp.sin(orders[:, None, None] * (math.pi / CUTOFF) * radius[None])
        * (envelope / radius)[None]
    )
    ux, uy, uz = unit[0], unit[1], unit[2]
    r3 = math.sqrt(3.0)
    r15 = math.sqrt(15.0)
    r5 = math.sqrt(5.0)
    harmonics = jnp.stack(
        [
            jnp.ones_like(ux),
            r3 * ux,
            r3 * uy,
            r3 * uz,
            r15 * ux * uy,
            r15 * uy * uz,
            0.5 * r5 * (2.0 * uz * uz - ux * ux - uy * uy),
            r15 * ux * uz,
            0.5 * r15 * (ux * ux - uy * uy),
        ],
        axis=0,
    )
    rows = jnp.concatenate([basis, envelope[None], harmonics], axis=0).reshape(18, K * atoms)
    return jnp.concatenate([rows, jnp.zeros((128 - 18, K * atoms), jnp.float32)], axis=0)


def _mm(a, b):
    return jnp.dot(a, b, preferred_element_type=jnp.float32)


def _sigmoid(v):
    return 0.5 + 0.5 * jnp.tanh(0.5 * v)


def _pair_kernel(
    rows_ref, centre_ref, geo_ref, basis_t_ref, split_t_ref, split_ref, update_t_ref,
    update_ref, tensor_t_ref, tensor_ref, basis_ref, energy_w_ref,
    grad_rows_ref, grad_centre_ref, grad_geo_ref, energy_ref,
    pre_s, hidden_s, mixed_s, damp_s, dlow_s, dgeo_s, env_s, denv_s,
):
    atoms = centre_ref.shape[1]
    f32 = jnp.float32
    bf16 = jnp.bfloat16
    span = SLOTS * atoms
    sub = lax.broadcasted_iota(jnp.int32, (128, span), 0)
    inv_root = 1.0 / math.sqrt(K)
    env_s[...] = jnp.zeros_like(env_s)
    denv_s[...] = jnp.zeros_like(denv_s)

    def block(k):
        return pl.ds(pl.multiple_of(k * span, span), span)

    def twice(v):
        return jnp.concatenate([v] * SLOTS, axis=1)

    def fold(v):
        total = v[:, :atoms]
        for slot in range(1, SLOTS):
            total = total + v[:, slot * atoms : (slot + 1) * atoms]
        return total

    def split_mm(weight, values):
        high = values.astype(bf16)
        low = (values - high.astype(f32)).astype(bf16)
        return _mm(weight, high) + _mm(weight, low)

    def first(k, carry):
        at = block(k)
        geo = geo_ref[:, at]
        radial = split_mm(basis_t_ref[...], geo)
        pre = twice(centre_ref[...]) + rows_ref[:, at].astype(f32) + radial
        envelope = geo[8:9, :]
        hidden = pre * _sigmoid(pre) * envelope
        pre_s[:, at] = pre
        hidden_s[:, at] = hidden
        mixed = _mm(split_t_ref[...], hidden.astype(bf16))
        mixed_s[:, at] = mixed
        for m in range(9):
            l = ORDER_OF[m]
            weight = mixed[3 * CH + l * CH : 3 * CH + (l + 1) * CH, :]
            env_s[m] = env_s[m] + fold(weight * (geo[9 + m : 10 + m, :] * inv_root))
        return carry

    lax.fori_loop(0, K // SLOTS, first, 0)

    def second(k, energy):
        at = block(k)
        geo = geo_ref[:, at]
        envelope = geo[8:9, :]
        hidden = hidden_s[:, at]
        mixed = mixed_s[:, at]
        parts = []
        totals = []
        for l in range(3):
            total = 0.0
            for m in GROUPS[l]:
                total = total + geo[9 + m : 10 + m, :] * twice(env_s[m])
            totals.append(total)
            parts.append(mixed[l * CH : (l + 1) * CH, :] * total)
        scalars = jnp.concatenate(parts, axis=0).astype(bf16)
        z = _mm(update_t_ref[...], hidden.astype(bf16)) + _mm(tensor_t_ref[...], scalars)
        gate = _sigmoid(z)
        update = z * gate
        readout = jnp.sum((hidden + update) * twice(energy_w_ref[...]), axis=0, keepdims=True)
        energy = energy + envelope * readout
        dz = (envelope * twice(energy_w_ref[...])) * (gate * (1.0 + z * (1.0 - gate)))
        dz_low = dz.astype(bf16)
        dscalars = _mm(tensor_ref[...], dz_low).astype(bf16).astype(f32)
        dlow_s[:, at] = _mm(update_ref[...], dz_low)
        dgeo = jnp.where(sub == 8, readout, 0.0)
        for l in range(3):
            ds = dscalars[l * CH : (l + 1) * CH, :]
            damp_s[l * CH : (l + 1) * CH, at] = ds * totals[l]
            dtotal = ds * mixed[l * CH : (l + 1) * CH, :]
            for m in GROUPS[l]:
                dgeo = dgeo + jnp.where(
                    sub == 9 + m, jnp.sum(dtotal * twice(env_s[m]), axis=0, keepdims=True), 0.0
                )
                denv_s[m] = denv_s[m] + fold(dtotal * geo[9 + m : 10 + m, :])
        dgeo_s[:, at] = dgeo
        return energy

    energy = lax.fori_loop(0, K // SLOTS, second, jnp.zeros((1, span), f32))
    energy_ref[...] = jnp.broadcast_to(fold(energy), energy_ref.shape)

    def third(k, centre_grad):
        at = block(k)
        geo = geo_ref[:, at]
        envelope = geo[8:9, :]
        mixed = mixed_s[:, at]
        dgeo = dgeo_s[:, at]
        dweights = []
        for l in range(3):
            weight = mixed[3 * CH + l * CH : 3 * CH + (l + 1) * CH, :]
            dweight = 0.0
            for m in GROUPS[l]:
                denv = twice(denv_s[m])
                dweight = dweight + denv * (geo[9 + m : 10 + m, :] * inv_root)
                dgeo = dgeo + jnp.where(
                    sub == 9 + m,
                    jnp.sum(denv * weight, axis=0, keepdims=True) * inv_root,
                    0.0,
                )
            dweights.append(dweight)
        dmixed = jnp.concatenate([damp_s[:, at]] + dweights, axis=0).astype(bf16)
        dlow = dlow_s[:, at] + _mm(split_ref[...], dmixed)
        dhidden = envelope * twice(energy_w_ref[...]) + dlow
        pre = pre_s[:, at]
        sig = _sigmoid(pre)
        act = pre * sig
        dgeo = dgeo + jnp.where(sub == 8, jnp.sum(dhidden * act, axis=0, keepdims=True), 0.0)
        dpre = dhidden * envelope * (sig * (1.0 + pre * (1.0 - sig)))
        grad_rows_ref[:, at] = dpre
        dgeo = dgeo + split_mm(basis_ref[...], dpre)
        grad_geo_ref[:, at] = dgeo
        return centre_grad + fold(dpre)

    grad_centre_ref[...] = lax.fori_loop(
        0, K // SLOTS, third, jnp.zeros(grad_centre_ref.shape, f32)
    )


def pair_terms(rows_t, centre_t, geo, basis_proj, split_proj, update_proj, tensor_proj, energy_proj):
    width, pairs = rows_t.shape
    atoms = centre_t.shape[1]
    f32 = jnp.float32
    bf16 = jnp.bfloat16
    basis_pad = jnp.concatenate([basis_proj, jnp.zeros((128 - NB, width), bf16)], axis=0)
    vmem = pl.BlockSpec(memory_space=pltpu.VMEM)
    outs = pl.pallas_call(
        _pair_kernel,
        out_shape=(
            jax.ShapeDtypeStruct((width, pairs), f32),
            jax.ShapeDtypeStruct((width, atoms), f32),
            jax.ShapeDtypeStruct((128, pairs), f32),
            jax.ShapeDtypeStruct((8, atoms), f32),
        ),
        in_specs=[vmem] * 12,
        out_specs=(vmem, vmem, vmem, vmem),
        scratch_shapes=[
            pltpu.VMEM((width, pairs), f32),
            pltpu.VMEM((width, pairs), f32),
            pltpu.VMEM((6 * CH, pairs), f32),
            pltpu.VMEM((3 * CH, pairs), f32),
            pltpu.VMEM((width, pairs), f32),
            pltpu.VMEM((128, pairs), f32),
            pltpu.VMEM((9, CH, atoms), f32),
            pltpu.VMEM((9, CH, atoms), f32),
        ],
        compiler_params=pltpu.CompilerParams(vmem_limit_bytes=60 * 1024 * 1024),
        cost_estimate=pl.CostEstimate(
            flops=int(24 * pairs * width * 128),
            transcendentals=int(3 * pairs * width),
            bytes_accessed=int(16 * pairs * width),
        ),
    )(
        rows_t,
        centre_t,
        geo,
        basis_pad.T,
        split_proj.T,
        split_proj,
        update_proj.T,
        update_proj,
        tensor_proj.T,
        tensor_proj,
        basis_pad,
        jnp.broadcast_to(energy_proj.astype(f32)[:, None], (width, atoms)),
    )
    grad_rows_t, grad_centre_t, grad_geo, energy = outs
    return grad_rows_t, grad_centre_t, grad_geo, energy[0]


def shards(
    latent,
    positions,
    species,
    send_list,
    neighbour,
    atom_count,
    centre_proj,
    neigh_proj,
    centre_table,
    neigh_table,
    basis_proj,
    split_proj,
    update_proj,
    tensor_proj,
    energy_proj,
    species_shift,
):
    atoms, width = latent.shape
    extra = 128
    face_x = atoms // 8
    face_y = atoms // 2
    face_z = atoms // 8
    lengths = [face_x, face_x, face_y, face_y, face_z, face_z]
    starts = [
        0,
        face_x,
        2 * face_x,
        2 * face_x + face_y,
        2 * face_x + 2 * face_y,
        2 * face_x + 2 * face_y + face_z,
    ]
    kinds = jnp.arange(NSPEC, dtype=jnp.int32)

    def lookup(codes, table):
        onehot = (codes[:, None] == kinds[None, :]).astype(jnp.float32)
        return jnp.dot(onehot, table, precision=lax.Precision.HIGHEST)

    def project(rows, codes, weight, table):
        return (
            jnp.dot(rows, weight, preferred_element_type=jnp.float32) + lookup(codes, table)
        ).astype(jnp.bfloat16)

    def spread_cols(onehot, values):
        return jnp.einsum(
            "wn,nr->wr", values.astype(jnp.bfloat16), onehot, preferred_element_type=jnp.float32
        )

    def spread(onehot, values):
        return jnp.einsum(
            "nr,nw->rw", onehot, values.astype(jnp.bfloat16), preferred_element_type=jnp.float32
        )

    proj_c = project(latent, species, centre_proj, centre_table)
    proj_n = project(latent, species, neigh_proj, neigh_table)
    send_rows = send_list[0]
    coarse = positions // 16
    fine = positions - coarse * 16
    coord_cols = jnp.concatenate([coarse, fine], axis=0).T.astype(jnp.bfloat16)
    table = jnp.concatenate(
        [proj_n, coord_cols, jnp.zeros((atoms, extra - 6), jnp.bfloat16)], axis=1
    )
    shifts = [(0, -LX_FIX), (0, LX_FIX), (1, -LY_FIX), (1, LY_FIX), (2, -LZ_FIX), (2, LZ_FIX)]
    sections = (("gx", (1, 0)), ("gy", (3, 2)), ("gz", (5, 4)))
    pickers = {}
    base_rows = []
    for section, (axis, segs) in enumerate(sections):
        rows_now = table.shape[0]
        base_rows.append(rows_now)
        parts = [table]
        for number, (segment, direction) in enumerate(((segs[0], 1), (segs[1], -1))):
            picked = send_rows[starts[segment] : starts[segment] + lengths[segment]]
            onehot = (
                picked[:, None] == jnp.arange(rows_now, dtype=jnp.int32)[None, :]
            ).astype(jnp.bfloat16)
            pickers[segment] = onehot
            out = jnp.dot(onehot, table, preferred_element_type=jnp.float32).astype(jnp.bfloat16)
            got = passed_along(out, axis, direction)
            coord_axis, offset = shifts[2 * section + number]
            columns = jnp.arange(width + extra, dtype=jnp.int32)[None, :]
            shift = jnp.where(columns == width + coord_axis, offset // 16, 0).astype(jnp.bfloat16)
            parts.append(got + shift)
        table = jnp.concatenate(parts, axis=0)
    total_rows = table.shape[0]
    neighbour = neighbour.reshape(atoms, K).T.reshape(-1)
    select = (neighbour[:, None] == jnp.arange(total_rows, dtype=jnp.int32)[None, :]).astype(
        jnp.bfloat16
    )
    neigh_cols = jnp.einsum(
        "tw,pt->wp", table[:, :width], select, preferred_element_type=jnp.float32
    ).astype(jnp.bfloat16)
    gathered = jnp.einsum(
        "tw,pt->wp", table[:, width:], select, preferred_element_type=jnp.float32
    )
    coords_n = gathered[0:3] * 16.0 + gathered[3:6]
    delta = (coords_n.reshape(3, K, atoms) - positions.astype(jnp.float32)[:, None, :]) * (
        1.0 / 64.0
    )
    live = (jnp.arange(atoms) < atom_count[0]).astype(jnp.float32)
    valid_pair = live[None, :]

    geo, geo_pull = jax.vjp(lambda d: geometry(d, valid_pair), delta)
    grad_neigh, grad_centre, grad_geo, atom_energy = pair_terms(
        neigh_cols,
        proj_c.astype(jnp.float32).T,
        geo,
        basis_proj,
        split_proj,
        update_proj,
        tensor_proj,
        energy_proj,
    )
    (grad_delta,) = geo_pull(grad_geo)
    pairs = grad_neigh.shape[1]
    grads = jnp.concatenate(
        [
            grad_neigh,
            grad_delta.reshape(3, pairs),
            jnp.zeros((extra - 3, pairs), jnp.float32),
        ],
        axis=0,
    )
    sums = spread_cols(select, grads).T
    own_pos = grad_delta.sum(axis=1)
    sums = sums - jnp.pad(own_pos.T, ((0, total_rows - atoms), (width, extra - 3)))
    for section in (2, 1, 0):
        axis, segs = sections[section]
        rows_now = base_rows[section]
        first = atoms + starts[2 * section]
        second = atoms + starts[2 * section + 1]
        back_first = passed_along(sums[first : first + lengths[2 * section]], axis, -1)
        back_second = passed_along(sums[second : second + lengths[2 * section + 1]], axis, 1)
        sums = (
            sums[:rows_now]
            + spread(pickers[segs[0]], back_first)
            + spread(pickers[segs[1]], back_second)
        )
    back_neigh = neigh_proj.astype(jnp.float32).T
    back_centre = centre_proj.astype(jnp.float32).T
    latent_grad = jnp.dot(grad_centre.T, back_centre, precision=lax.Precision.HIGHEST)
    latent_grad = latent_grad + jnp.dot(
        sums[:, :width], back_neigh, precision=lax.Precision.HIGHEST
    )
    forces = -sums[:, width : width + 3].T
    energies = live * (lookup(species, species_shift[:, None])[:, 0] + atom_energy)
    return (energies, forces, latent_grad)


def solution(mesh):
    in_specs = (
        P(("gx", "gy", "gz"), None),
        P(None, ("gx", "gy", "gz")),
        P(("gx", "gy", "gz")),
        P(("gx", "gy", "gz"), None),
        P(("gx", "gy", "gz")),
        P(("gx", "gy", "gz")),
        P(),
        P(),
        P(),
        P(),
        P(),
        P(),
        P(),
        P(),
        P(),
        P(),
    )
    out_specs = (P(("gx", "gy", "gz")), P(None, ("gx", "gy", "gz")), P(("gx", "gy", "gz"), None))
    return jax.shard_map(shards, mesh=mesh, in_specs=in_specs, out_specs=out_specs, check_vma=False)
```

```python
import math

import jax
import jax.numpy as jnp
from jax import lax
from jax.experimental import pallas as pl
from jax.experimental.pallas import tpu as pltpu
from jax.sharding import PartitionSpec as P

K = 8
CH = 64
NB = 8
NSPEC = 5
LX_FIX = 1024
LY_FIX = 512
LZ_FIX = 1280


CUTOFF = 6.0
SOFTEN = 0.25


def shortened(shard):
    return jax.tree.map(lambda a: a.astype(jnp.bfloat16) if a.dtype == jnp.float32 else a, shard)


def passed_along(block, axis, distance):
    devices = range(lax.axis_size(axis))
    route = [((i - distance) % len(devices), i) for i in devices]
    return lax.ppermute(block, axis, route)


def by_order(values):
    rest = values.shape[1:]
    return jnp.concatenate(
        [
            values[0:1],
            jnp.broadcast_to(values[1:2], (3,) + rest),
            jnp.broadcast_to(values[2:3], (5,) + rest),
        ],
        axis=0,
    )


SLOTS = 8
ORDER_OF = (0, 1, 1, 1, 2, 2, 2, 2, 2)
GROUPS = ((0,), (1, 2, 3), (4, 5, 6, 7, 8))


def geometry(delta, valid_pair):
    atoms = delta.shape[2]
    radius = jnp.sqrt(jnp.sum(delta * delta, axis=0) + SOFTEN)
    unit = delta / radius
    ratio = radius / CUTOFF
    envelope = jnp.where(ratio < 1.0, (1.0 - ratio * ratio) ** 2, 0.0) * valid_pair
    orders = jnp.arange(1, NB + 1).astype(jnp.float32)
    basis = (
        jnp.sin(orders[:, None, None] * (math.pi / CUTOFF) * radius[None])
        * (envelope / radius)[None]
    )
    ux, uy, uz = unit[0], unit[1], unit[2]
    r3 = math.sqrt(3.0)
    r15 = math.sqrt(15.0)
    r5 = math.sqrt(5.0)
    harmonics = jnp.stack(
        [
            jnp.ones_like(ux),
            r3 * ux,
            r3 * uy,
            r3 * uz,
            r15 * ux * uy,
            r15 * uy * uz,
            0.5 * r5 * (2.0 * uz * uz - ux * ux - uy * uy),
            r15 * ux * uz,
            0.5 * r15 * (ux * ux - uy * uy),
        ],
        axis=0,
    )
    rows = jnp.concatenate([basis, envelope[None], harmonics], axis=0).reshape(18, K * atoms)
    return jnp.concatenate([rows, jnp.zeros((128 - 18, K * atoms), jnp.float32)], axis=0)


def _mm(a, b):
    return jnp.dot(a, b, preferred_element_type=jnp.float32)


def _sigmoid(v):
    return 0.5 + 0.5 * jnp.tanh(0.5 * v)


def _pair_kernel(
    rows_ref, centre_ref, geo_ref, basis_t_ref, split_t_ref, split_ref, update_t_ref,
    update_ref, tensor_t_ref, tensor_ref, basis_ref, energy_w_ref,
    grad_rows_ref, grad_centre_ref, grad_geo_ref, energy_ref,
    pre_s, hidden_s, mixed_s, damp_s, dlow_s, dgeo_s, env_s, denv_s,
):
    atoms = centre_ref.shape[1]
    f32 = jnp.float32
    bf16 = jnp.bfloat16
    span = SLOTS * atoms
    sub = lax.broadcasted_iota(jnp.int32, (128, span), 0)
    inv_root = 1.0 / math.sqrt(K)
    env_s[...] = jnp.zeros_like(env_s)
    denv_s[...] = jnp.zeros_like(denv_s)

    def block(k):
        return pl.ds(pl.multiple_of(k * span, span), span)

    def twice(v):
        return jnp.concatenate([v] * SLOTS, axis=1)

    def fold(v):
        total = v[:, :atoms]
        for slot in range(1, SLOTS):
            total = total + v[:, slot * atoms : (slot + 1) * atoms]
        return total

    def split_mm(weight, values):
        high = values.astype(bf16)
        low = (values - high.astype(f32)).astype(bf16)
        return _mm(weight, high) + _mm(weight, low)

    def first(k, carry):
        at = block(k)
        geo = geo_ref[:, at]
        radial = split_mm(basis_t_ref[...], geo)
        pre = twice(centre_ref[...]) + rows_ref[:, at].astype(f32) + radial
        envelope = geo[8:9, :]
        hidden = pre * _sigmoid(pre) * envelope
        pre_s[:, at] = pre
        hidden_s[:, at] = hidden
        mixed = _mm(split_t_ref[...], hidden.astype(bf16))
        mixed_s[:, at] = mixed
        for m in range(9):
            l = ORDER_OF[m]
            weight = mixed[3 * CH + l * CH : 3 * CH + (l + 1) * CH, :]
            env_s[m] = env_s[m] + fold(weight * (geo[9 + m : 10 + m, :] * inv_root))
        return carry

    lax.fori_loop(0, K // SLOTS, first, 0)

    def second(k, energy):
        at = block(k)
        geo = geo_ref[:, at]
        envelope = geo[8:9, :]
        hidden = hidden_s[:, at]
        mixed = mixed_s[:, at]
        parts = []
        totals = []
        for l in range(3):
            total = 0.0
            for m in GROUPS[l]:
                total = total + geo[9 + m : 10 + m, :] * twice(env_s[m])
            totals.append(total)
            parts.append(mixed[l * CH : (l + 1) * CH, :] * total)
        scalars = jnp.concatenate(parts, axis=0).astype(bf16)
        z = _mm(update_t_ref[...], hidden.astype(bf16)) + _mm(tensor_t_ref[...], scalars)
        gate = _sigmoid(z)
        update = z * gate
        readout = jnp.sum((hidden + update) * twice(energy_w_ref[...]), axis=0, keepdims=True)
        energy = energy + envelope * readout
        dz = (envelope * twice(energy_w_ref[...])) * (gate * (1.0 + z * (1.0 - gate)))
        dz_low = dz.astype(bf16)
        dscalars = _mm(tensor_ref[...], dz_low).astype(bf16).astype(f32)
        dlow_s[:, at] = _mm(update_ref[...], dz_low)
        dgeo = jnp.where(sub == 8, readout, 0.0)
        for l in range(3):
            ds = dscalars[l * CH : (l + 1) * CH, :]
            damp_s[l * CH : (l + 1) * CH, at] = ds * totals[l]
            dtotal = ds * mixed[l * CH : (l + 1) * CH, :]
            for m in GROUPS[l]:
                dgeo = dgeo + jnp.where(
                    sub == 9 + m, jnp.sum(dtotal * twice(env_s[m]), axis=0, keepdims=True), 0.0
                )
                denv_s[m] = denv_s[m] + fold(dtotal * geo[9 + m : 10 + m, :])
        dgeo_s[:, at] = dgeo
        return energy

    energy = lax.fori_loop(0, K // SLOTS, second, jnp.zeros((1, span), f32))
    energy_ref[...] = jnp.broadcast_to(fold(energy), energy_ref.shape)

    def third(k, centre_grad):
        at = block(k)
        geo = geo_ref[:, at]
        envelope = geo[8:9, :]
        mixed = mixed_s[:, at]
        dgeo = dgeo_s[:, at]
        dweights = []
        for l in range(3):
            weight = mixed[3 * CH + l * CH : 3 * CH + (l + 1) * CH, :]
            dweight = 0.0
            for m in GROUPS[l]:
                denv = twice(denv_s[m])
                dweight = dweight + denv * (geo[9 + m : 10 + m, :] * inv_root)
                dgeo = dgeo + jnp.where(
                    sub == 9 + m,
                    jnp.sum(denv * weight, axis=0, keepdims=True) * inv_root,
                    0.0,
                )
            dweights.append(dweight)
        dmixed = jnp.concatenate([damp_s[:, at]] + dweights, axis=0).astype(bf16)
        dlow = dlow_s[:, at] + _mm(split_ref[...], dmixed)
        dhidden = envelope * twice(energy_w_ref[...]) + dlow
        pre = pre_s[:, at]
        sig = _sigmoid(pre)
        act = pre * sig
        dgeo = dgeo + jnp.where(sub == 8, jnp.sum(dhidden * act, axis=0, keepdims=True), 0.0)
        dpre = dhidden * envelope * (sig * (1.0 + pre * (1.0 - sig)))
        grad_rows_ref[:, at] = dpre
        dgeo = dgeo + _mm(basis_ref[...], dpre.astype(bf16))
        grad_geo_ref[:, at] = dgeo
        return centre_grad + fold(dpre)

    grad_centre_ref[...] = lax.fori_loop(
        0, K // SLOTS, third, jnp.zeros(grad_centre_ref.shape, f32)
    )


def pair_terms(rows_t, centre_t, geo, basis_proj, split_proj, update_proj, tensor_proj, energy_proj):
    width, pairs = rows_t.shape
    atoms = centre_t.shape[1]
    f32 = jnp.float32
    bf16 = jnp.bfloat16
    basis_pad = jnp.concatenate([basis_proj, jnp.zeros((128 - NB, width), bf16)], axis=0)
    vmem = pl.BlockSpec(memory_space=pltpu.VMEM)
    outs = pl.pallas_call(
        _pair_kernel,
        out_shape=(
            jax.ShapeDtypeStruct((width, pairs), f32),
            jax.ShapeDtypeStruct((width, atoms), f32),
            jax.ShapeDtypeStruct((128, pairs), f32),
            jax.ShapeDtypeStruct((8, atoms), f32),
        ),
        in_specs=[vmem] * 12,
        out_specs=(vmem, vmem, vmem, vmem),
        scratch_shapes=[
            pltpu.VMEM((width, pairs), f32),
            pltpu.VMEM((width, pairs), f32),
            pltpu.VMEM((6 * CH, pairs), f32),
            pltpu.VMEM((3 * CH, pairs), f32),
            pltpu.VMEM((width, pairs), f32),
            pltpu.VMEM((128, pairs), f32),
            pltpu.VMEM((9, CH, atoms), f32),
            pltpu.VMEM((9, CH, atoms), f32),
        ],
        compiler_params=pltpu.CompilerParams(vmem_limit_bytes=60 * 1024 * 1024),
        cost_estimate=pl.CostEstimate(
            flops=int(24 * pairs * width * 128),
            transcendentals=int(3 * pairs * width),
            bytes_accessed=int(16 * pairs * width),
        ),
    )(
        rows_t,
        centre_t,
        geo,
        basis_pad.T,
        split_proj.T,
        split_proj,
        update_proj.T,
        update_proj,
        tensor_proj.T,
        tensor_proj,
        basis_pad,
        jnp.broadcast_to(energy_proj.astype(f32)[:, None], (width, atoms)),
    )
    grad_rows_t, grad_centre_t, grad_geo, energy = outs
    return grad_rows_t, grad_centre_t, grad_geo, energy[0]


def shards(
    latent,
    positions,
    species,
    send_list,
    neighbour,
    atom_count,
    centre_proj,
    neigh_proj,
    centre_table,
    neigh_table,
    basis_proj,
    split_proj,
    update_proj,
    tensor_proj,
    energy_proj,
    species_shift,
):
    atoms, width = latent.shape
    extra = 128
    face_x = atoms // 8
    face_y = atoms // 2
    face_z = atoms // 8
    lengths = [face_x, face_x, face_y, face_y, face_z, face_z]
    starts = [
        0,
        face_x,
        2 * face_x,
        2 * face_x + face_y,
        2 * face_x + 2 * face_y,
        2 * face_x + 2 * face_y + face_z,
    ]
    kinds = jnp.arange(NSPEC, dtype=jnp.int32)

    def lookup(codes, table):
        onehot = (codes[:, None] == kinds[None, :]).astype(jnp.float32)
        return jnp.dot(onehot, table, precision=lax.Precision.HIGHEST)

    def project(rows, codes, weight, table):
        return (
            jnp.dot(rows, weight, preferred_element_type=jnp.float32) + lookup(codes, table)
        ).astype(jnp.bfloat16)

    def spread_cols(onehot, values):
        return jnp.einsum(
            "wn,nr->wr", values.astype(jnp.bfloat16), onehot, preferred_element_type=jnp.float32
        )

    def spread(onehot, values):
        return jnp.einsum(
            "nr,nw->rw", onehot, values.astype(jnp.bfloat16), preferred_element_type=jnp.float32
        )

    proj_c = project(latent, species, centre_proj, centre_table)
    proj_n = project(latent, species, neigh_proj, neigh_table)
    send_rows = send_list[0]
    coarse = positions // 16
    fine = positions - coarse * 16
    coord_cols = jnp.concatenate([coarse, fine], axis=0).T.astype(jnp.bfloat16)
    table = jnp.concatenate(
        [proj_n, coord_cols, jnp.zeros((atoms, extra - 6), jnp.bfloat16)], axis=1
    )
    shifts = [(0, -LX_FIX), (0, LX_FIX), (1, -LY_FIX), (1, LY_FIX), (2, -LZ_FIX), (2, LZ_FIX)]
    sections = (("gx", (1, 0)), ("gy", (3, 2)), ("gz", (5, 4)))
    pickers = {}
    base_rows = []
    for section, (axis, segs) in enumerate(sections):
        rows_now = table.shape[0]
        base_rows.append(rows_now)
        parts = [table]
        for number, (segment, direction) in enumerate(((segs[0], 1), (segs[1], -1))):
            picked = send_rows[starts[segment] : starts[segment] + lengths[segment]]
            onehot = (
                picked[:, None] == jnp.arange(rows_now, dtype=jnp.int32)[None, :]
            ).astype(jnp.bfloat16)
            pickers[segment] = onehot
            out = jnp.dot(onehot, table, preferred_element_type=jnp.float32).astype(jnp.bfloat16)
            got = passed_along(out, axis, direction)
            coord_axis, offset = shifts[2 * section + number]
            columns = jnp.arange(width + extra, dtype=jnp.int32)[None, :]
            shift = jnp.where(columns == width + coord_axis, offset // 16, 0).astype(jnp.bfloat16)
            parts.append(got + shift)
        table = jnp.concatenate(parts, axis=0)
    total_rows = table.shape[0]
    neighbour = neighbour.reshape(atoms, K).T.reshape(-1)
    select = (neighbour[:, None] == jnp.arange(total_rows, dtype=jnp.int32)[None, :]).astype(
        jnp.bfloat16
    )
    gathered = jnp.einsum("tw,pt->wp", table, select, preferred_element_type=jnp.float32)
    neigh_cols = gathered[:width].astype(jnp.bfloat16)
    coords_n = gathered[width : width + 3] * 16.0 + gathered[width + 3 : width + 6]
    delta = (coords_n.reshape(3, K, atoms) - positions.astype(jnp.float32)[:, None, :]) * (
        1.0 / 64.0
    )
    live = (jnp.arange(atoms) < atom_count[0]).astype(jnp.float32)
    valid_pair = live[None, :]

    geo, geo_pull = jax.vjp(lambda d: geometry(d, valid_pair), delta)
    grad_neigh, grad_centre, grad_geo, atom_energy = pair_terms(
        neigh_cols,
        proj_c.astype(jnp.float32).T,
        geo,
        basis_proj,
        split_proj,
        update_proj,
        tensor_proj,
        energy_proj,
    )
    (grad_delta,) = geo_pull(grad_geo)
    pairs = grad_neigh.shape[1]
    grads = jnp.concatenate(
        [
            grad_neigh,
            grad_delta.reshape(3, pairs),
            jnp.zeros((extra - 3, pairs), jnp.float32),
        ],
        axis=0,
    )
    sums = spread_cols(select, grads).T
    own_pos = grad_delta.sum(axis=1)
    sums = sums - jnp.pad(own_pos.T, ((0, total_rows - atoms), (width, extra - 3)))
    for section in (2, 1, 0):
        axis, segs = sections[section]
        rows_now = base_rows[section]
        first = atoms + starts[2 * section]
        second = atoms + starts[2 * section + 1]
        back_first = passed_along(sums[first : first + lengths[2 * section]], axis, -1)
        back_second = passed_along(sums[second : second + lengths[2 * section + 1]], axis, 1)
        sums = (
            sums[:rows_now]
            + spread(pickers[segs[0]], back_first)
            + spread(pickers[segs[1]], back_second)
        )
    back_neigh = neigh_proj.astype(jnp.float32).T
    back_centre = centre_proj.astype(jnp.float32).T
    latent_grad = jnp.dot(grad_centre.T, back_centre, precision=lax.Precision.HIGHEST)
    latent_grad = latent_grad + jnp.dot(
        sums[:, :width], back_neigh, precision=lax.Precision.HIGHEST
    )
    forces = -sums[:, width : width + 3].T
    energies = live * (lookup(species, species_shift[:, None])[:, 0] + atom_energy)
    return (energies, forces, latent_grad)


def solution(mesh):
    in_specs = (
        P(("gx", "gy", "gz"), None),
        P(None, ("gx", "gy", "gz")),
        P(("gx", "gy", "gz")),
        P(("gx", "gy", "gz"), None),
        P(("gx", "gy", "gz")),
        P(("gx", "gy", "gz")),
        P(),
        P(),
        P(),
        P(),
        P(),
        P(),
        P(),
        P(),
        P(),
        P(),
    )
    out_specs = (P(("gx", "gy", "gz")), P(None, ("gx", "gy", "gz")), P(("gx", "gy", "gz"), None))
    return jax.shard_map(shards, mesh=mesh, in_specs=in_specs, out_specs=out_specs, check_vma=False)
```

```python
import math

import jax
import jax.numpy as jnp
from jax import lax
from jax.experimental import pallas as pl
from jax.experimental.pallas import tpu as pltpu
from jax.sharding import PartitionSpec as P

K = 8
CH = 64
NB = 8
NSPEC = 5
LX_FIX = 1024
LY_FIX = 512
LZ_FIX = 1280


CUTOFF = 6.0
SOFTEN = 0.25


def shortened(shard):
    return jax.tree.map(lambda a: a.astype(jnp.bfloat16) if a.dtype == jnp.float32 else a, shard)


def passed_along(block, axis, distance):
    devices = range(lax.axis_size(axis))
    route = [((i - distance) % len(devices), i) for i in devices]
    return lax.ppermute(block, axis, route)


def by_order(values):
    rest = values.shape[1:]
    return jnp.concatenate(
        [
            values[0:1],
            jnp.broadcast_to(values[1:2], (3,) + rest),
            jnp.broadcast_to(values[2:3], (5,) + rest),
        ],
        axis=0,
    )


SLOTS = 8
ORDER_OF = (0, 1, 1, 1, 2, 2, 2, 2, 2)
GROUPS = ((0,), (1, 2, 3), (4, 5, 6, 7, 8))


def geometry(delta, valid_pair):
    atoms = delta.shape[2]
    radius = jnp.sqrt(jnp.sum(delta * delta, axis=0) + SOFTEN)
    unit = delta / radius
    ratio = radius / CUTOFF
    envelope = jnp.where(ratio < 1.0, (1.0 - ratio * ratio) ** 2, 0.0) * valid_pair
    orders = jnp.arange(1, NB + 1).astype(jnp.float32)
    basis = (
        jnp.sin(orders[:, None, None] * (math.pi / CUTOFF) * radius[None])
        * (envelope / radius)[None]
    )
    ux, uy, uz = unit[0], unit[1], unit[2]
    r3 = math.sqrt(3.0)
    r15 = math.sqrt(15.0)
    r5 = math.sqrt(5.0)
    harmonics = jnp.stack(
        [
            jnp.ones_like(ux),
            r3 * ux,
            r3 * uy,
            r3 * uz,
            r15 * ux * uy,
            r15 * uy * uz,
            0.5 * r5 * (2.0 * uz * uz - ux * ux - uy * uy),
            r15 * ux * uz,
            0.5 * r15 * (ux * ux - uy * uy),
        ],
        axis=0,
    )
    rows = jnp.concatenate([basis, envelope[None], harmonics], axis=0).reshape(18, K * atoms)
    return jnp.concatenate([rows, jnp.zeros((128 - 18, K * atoms), jnp.float32)], axis=0)


def _mm(a, b):
    return jnp.dot(a, b, preferred_element_type=jnp.float32)


def _sigmoid(v):
    return 0.5 + 0.5 * jnp.tanh(0.5 * v)


def _pair_kernel(
    rows_ref, centre_ref, geo_ref, basis_t_ref, split_t_ref, split_ref, update_t_ref,
    update_ref, tensor_t_ref, tensor_ref, basis_ref, energy_w_ref,
    grad_rows_ref, grad_centre_ref, grad_geo_ref, energy_ref,
    pre_s, hidden_s, mixed_s, damp_s, dlow_s, dgeo_s, env_s, denv_s,
):
    atoms = centre_ref.shape[1]
    f32 = jnp.float32
    bf16 = jnp.bfloat16
    span = SLOTS * atoms
    sub = lax.broadcasted_iota(jnp.int32, (128, span), 0)
    inv_root = 1.0 / math.sqrt(K)
    env_s[...] = jnp.zeros_like(env_s)
    denv_s[...] = jnp.zeros_like(denv_s)

    def block(k):
        return pl.ds(pl.multiple_of(k * span, span), span)

    def twice(v):
        return jnp.concatenate([v] * SLOTS, axis=1)

    def fold(v):
        total = v[:, :atoms]
        for slot in range(1, SLOTS):
            total = total + v[:, slot * atoms : (slot + 1) * atoms]
        return total

    def split_mm(weight, values):
        high = values.astype(bf16)
        low = (values - high.astype(f32)).astype(bf16)
        return _mm(weight, high) + _mm(weight, low)

    def first(k, carry):
        at = block(k)
        geo = geo_ref[:, at]
        radial = split_mm(basis_t_ref[...], geo)
        pre = twice(centre_ref[...]) + rows_ref[:, at].astype(f32) + radial
        envelope = geo[8:9, :]
        hidden = pre * _sigmoid(pre) * envelope
        pre_s[:, at] = pre
        hidden_s[:, at] = hidden
        mixed = _mm(split_t_ref[...], hidden.astype(bf16))
        mixed_s[:, at] = mixed
        for m in range(9):
            l = ORDER_OF[m]
            weight = mixed[3 * CH + l * CH : 3 * CH + (l + 1) * CH, :]
            env_s[m] = env_s[m] + fold(weight * (geo[9 + m : 10 + m, :] * inv_root))
        return carry

    lax.fori_loop(0, K // SLOTS, first, 0)

    def second(k, energy):
        at = block(k)
        geo = geo_ref[:, at]
        envelope = geo[8:9, :]
        hidden = hidden_s[:, at]
        mixed = mixed_s[:, at]
        parts = []
        totals = []
        for l in range(3):
            total = 0.0
            for m in GROUPS[l]:
                total = total + geo[9 + m : 10 + m, :] * twice(env_s[m])
            totals.append(total)
            parts.append(mixed[l * CH : (l + 1) * CH, :] * total)
        scalars = jnp.concatenate(parts, axis=0).astype(bf16)
        z = _mm(update_t_ref[...], hidden.astype(bf16)) + _mm(tensor_t_ref[...], scalars)
        gate = _sigmoid(z)
        update = z * gate
        readout = jnp.sum((hidden + update) * twice(energy_w_ref[...]), axis=0, keepdims=True)
        energy = energy + envelope * readout
        dz = (envelope * twice(energy_w_ref[...])) * (gate * (1.0 + z * (1.0 - gate)))
        dz_low = dz.astype(bf16)
        dscalars = _mm(tensor_ref[...], dz_low).astype(bf16).astype(f32)
        dlow_s[:, at] = _mm(update_ref[...], dz_low)
        dgeo = jnp.where(sub == 8, readout, 0.0)
        for l in range(3):
            ds = dscalars[l * CH : (l + 1) * CH, :]
            damp_s[l * CH : (l + 1) * CH, at] = ds * totals[l]
            dtotal = ds * mixed[l * CH : (l + 1) * CH, :]
            for m in GROUPS[l]:
                dgeo = dgeo + jnp.where(
                    sub == 9 + m, jnp.sum(dtotal * twice(env_s[m]), axis=0, keepdims=True), 0.0
                )
                denv_s[m] = denv_s[m] + fold(dtotal * geo[9 + m : 10 + m, :])
        dgeo_s[:, at] = dgeo
        return energy

    energy = lax.fori_loop(0, K // SLOTS, second, jnp.zeros((1, span), f32))
    energy_ref[...] = jnp.broadcast_to(fold(energy), energy_ref.shape)

    def third(k, centre_grad):
        at = block(k)
        geo = geo_ref[:, at]
        envelope = geo[8:9, :]
        mixed = mixed_s[:, at]
        dgeo = dgeo_s[:, at]
        dweights = []
        for l in range(3):
            weight = mixed[3 * CH + l * CH : 3 * CH + (l + 1) * CH, :]
            dweight = 0.0
            for m in GROUPS[l]:
                denv = twice(denv_s[m])
                dweight = dweight + denv * (geo[9 + m : 10 + m, :] * inv_root)
                dgeo = dgeo + jnp.where(
                    sub == 9 + m,
                    jnp.sum(denv * weight, axis=0, keepdims=True) * inv_root,
                    0.0,
                )
            dweights.append(dweight)
        dmixed = jnp.concatenate([damp_s[:, at]] + dweights, axis=0).astype(bf16)
        dlow = dlow_s[:, at] + _mm(split_ref[...], dmixed)
        dhidden = envelope * twice(energy_w_ref[...]) + dlow
        pre = pre_s[:, at]
        sig = _sigmoid(pre)
        act = pre * sig
        dgeo = dgeo + jnp.where(sub == 8, jnp.sum(dhidden * act, axis=0, keepdims=True), 0.0)
        dpre = dhidden * envelope * (sig * (1.0 + pre * (1.0 - sig)))
        grad_rows_ref[:, at] = dpre
        dgeo = dgeo + split_mm(basis_ref[...], dpre)
        grad_geo_ref[:, at] = dgeo
        return centre_grad + fold(dpre)

    grad_centre_ref[...] = lax.fori_loop(
        0, K // SLOTS, third, jnp.zeros(grad_centre_ref.shape, f32)
    )


def pair_terms(rows_t, centre_t, geo, basis_proj, split_proj, update_proj, tensor_proj, energy_proj):
    width, pairs = rows_t.shape
    atoms = centre_t.shape[1]
    f32 = jnp.float32
    bf16 = jnp.bfloat16
    basis_pad = jnp.concatenate([basis_proj, jnp.zeros((128 - NB, width), bf16)], axis=0)
    vmem = pl.BlockSpec(memory_space=pltpu.VMEM)
    outs = pl.pallas_call(
        _pair_kernel,
        out_shape=(
            jax.ShapeDtypeStruct((width, pairs), f32),
            jax.ShapeDtypeStruct((width, atoms), f32),
            jax.ShapeDtypeStruct((128, pairs), f32),
            jax.ShapeDtypeStruct((8, atoms), f32),
        ),
        in_specs=[vmem] * 12,
        out_specs=(vmem, vmem, vmem, vmem),
        scratch_shapes=[
            pltpu.VMEM((width, pairs), f32),
            pltpu.VMEM((width, pairs), f32),
            pltpu.VMEM((6 * CH, pairs), f32),
            pltpu.VMEM((3 * CH, pairs), f32),
            pltpu.VMEM((width, pairs), f32),
            pltpu.VMEM((128, pairs), f32),
            pltpu.VMEM((9, CH, atoms), f32),
            pltpu.VMEM((9, CH, atoms), f32),
        ],
        compiler_params=pltpu.CompilerParams(vmem_limit_bytes=60 * 1024 * 1024),
        cost_estimate=pl.CostEstimate(
            flops=int(24 * pairs * width * 128),
            transcendentals=int(3 * pairs * width),
            bytes_accessed=int(16 * pairs * width),
        ),
    )(
        rows_t,
        centre_t,
        geo,
        basis_pad.T,
        split_proj.T,
        split_proj,
        update_proj.T,
        update_proj,
        tensor_proj.T,
        tensor_proj,
        basis_pad,
        jnp.broadcast_to(energy_proj.astype(f32)[:, None], (width, atoms)),
    )
    grad_rows_t, grad_centre_t, grad_geo, energy = outs
    return grad_rows_t, grad_centre_t, grad_geo, energy[0]


def shards(
    latent,
    positions,
    species,
    send_list,
    neighbour,
    atom_count,
    centre_proj,
    neigh_proj,
    centre_table,
    neigh_table,
    basis_proj,
    split_proj,
    update_proj,
    tensor_proj,
    energy_proj,
    species_shift,
):
    atoms, width = latent.shape
    extra = 128
    face_x = atoms // 8
    face_y = atoms // 2
    face_z = atoms // 8
    lengths = [face_x, face_x, face_y, face_y, face_z, face_z]
    starts = [
        0,
        face_x,
        2 * face_x,
        2 * face_x + face_y,
        2 * face_x + 2 * face_y,
        2 * face_x + 2 * face_y + face_z,
    ]
    kinds = jnp.arange(NSPEC, dtype=jnp.int32)

    def lookup(codes, table):
        onehot = (codes[:, None] == kinds[None, :]).astype(jnp.float32)
        return jnp.dot(onehot, table, precision=lax.Precision.HIGHEST)

    def project(rows, codes, weight, table):
        return (
            jnp.dot(rows, weight, preferred_element_type=jnp.float32) + lookup(codes, table)
        ).astype(jnp.bfloat16)

    def spread_cols(onehot, values):
        return jnp.einsum(
            "wn,nr->wr", values.astype(jnp.bfloat16), onehot, preferred_element_type=jnp.float32
        )

    def spread(onehot, values):
        return jnp.einsum(
            "nr,nw->rw", onehot, values.astype(jnp.bfloat16), preferred_element_type=jnp.float32
        )

    proj_c = project(latent, species, centre_proj, centre_table)
    proj_n = project(latent, species, neigh_proj, neigh_table)
    send_rows = send_list[0]
    coarse = positions // 16
    fine = positions - coarse * 16
    coord_cols = jnp.concatenate([coarse, fine], axis=0).T.astype(jnp.bfloat16)
    table = jnp.concatenate(
        [proj_n, coord_cols, jnp.zeros((atoms, extra - 6), jnp.bfloat16)], axis=1
    )
    shifts = [(0, -LX_FIX), (0, LX_FIX), (1, -LY_FIX), (1, LY_FIX), (2, -LZ_FIX), (2, LZ_FIX)]
    sections = (("gx", (1, 0)), ("gy", (3, 2)), ("gz", (5, 4)))
    pickers = {}
    base_rows = []
    for section, (axis, segs) in enumerate(sections):
        rows_now = table.shape[0]
        base_rows.append(rows_now)
        parts = [table]
        for number, (segment, direction) in enumerate(((segs[0], 1), (segs[1], -1))):
            picked = send_rows[starts[segment] : starts[segment] + lengths[segment]]
            onehot = (
                picked[:, None] == jnp.arange(rows_now, dtype=jnp.int32)[None, :]
            ).astype(jnp.bfloat16)
            pickers[segment] = onehot
            out = jnp.dot(onehot, table, preferred_element_type=jnp.float32).astype(jnp.bfloat16)
            got = passed_along(out, axis, direction)
            coord_axis, offset = shifts[2 * section + number]
            columns = jnp.arange(width + extra, dtype=jnp.int32)[None, :]
            shift = jnp.where(columns == width + coord_axis, offset // 16, 0).astype(jnp.bfloat16)
            parts.append(got + shift)
        table = jnp.concatenate(parts, axis=0)
    total_rows = table.shape[0]
    neighbour = neighbour.reshape(atoms, K).T.reshape(-1)
    select = (neighbour[:, None] == jnp.arange(total_rows, dtype=jnp.int32)[None, :]).astype(
        jnp.bfloat16
    )
    gathered = jnp.einsum("tw,pt->wp", table, select, preferred_element_type=jnp.float32)
    neigh_cols = gathered[:width].astype(jnp.bfloat16)
    coords_n = gathered[width : width + 3] * 16.0 + gathered[width + 3 : width + 6]
    delta = (coords_n.reshape(3, K, atoms) - positions.astype(jnp.float32)[:, None, :]) * (
        1.0 / 64.0
    )
    live = (jnp.arange(atoms) < atom_count[0]).astype(jnp.float32)
    valid_pair = live[None, :]

    geo, geo_pull = jax.vjp(lambda d: geometry(d, valid_pair), delta)
    grad_neigh, grad_centre, grad_geo, atom_energy = pair_terms(
        neigh_cols,
        proj_c.astype(jnp.float32).T,
        geo,
        basis_proj,
        split_proj,
        update_proj,
        tensor_proj,
        energy_proj,
    )
    (grad_delta,) = geo_pull(grad_geo)
    pairs = grad_neigh.shape[1]
    pos_grads = jnp.concatenate(
        [grad_delta.reshape(3, pairs), jnp.zeros((extra - 3, pairs), jnp.float32)], axis=0
    )
    sums = jnp.concatenate(
        [spread_cols(select, grad_neigh), spread_cols(select, pos_grads)], axis=0
    ).T
    own_pos = grad_delta.sum(axis=1)
    sums = sums - jnp.pad(own_pos.T, ((0, total_rows - atoms), (width, extra - 3)))
    for section in (2, 1, 0):
        axis, segs = sections[section]
        rows_now = base_rows[section]
        first = atoms + starts[2 * section]
        second = atoms + starts[2 * section + 1]
        back_first = passed_along(sums[first : first + lengths[2 * section]], axis, -1)
        back_second = passed_along(sums[second : second + lengths[2 * section + 1]], axis, 1)
        sums = (
            sums[:rows_now]
            + spread(pickers[segs[0]], back_first)
            + spread(pickers[segs[1]], back_second)
        )
    back_neigh = neigh_proj.astype(jnp.float32).T
    back_centre = centre_proj.astype(jnp.float32).T
    latent_grad = jnp.dot(grad_centre.T, back_centre, precision=lax.Precision.HIGHEST)
    latent_grad = latent_grad + jnp.dot(
        sums[:, :width], back_neigh, precision=lax.Precision.HIGHEST
    )
    forces = -sums[:, width : width + 3].T
    energies = live * (lookup(species, species_shift[:, None])[:, 0] + atom_energy)
    return (energies, forces, latent_grad)


def solution(mesh):
    in_specs = (
        P(("gx", "gy", "gz"), None),
        P(None, ("gx", "gy", "gz")),
        P(("gx", "gy", "gz")),
        P(("gx", "gy", "gz"), None),
        P(("gx", "gy", "gz")),
        P(("gx", "gy", "gz")),
        P(),
        P(),
        P(),
        P(),
        P(),
        P(),
        P(),
        P(),
        P(),
        P(),
    )
    out_specs = (P(("gx", "gy", "gz")), P(None, ("gx", "gy", "gz")), P(("gx", "gy", "gz"), None))
    return jax.shard_map(shards, mesh=mesh, in_specs=in_specs, out_specs=out_specs, check_vma=False)
```
